32 devices in a mesh: groups: 2 (over y), seq: 4 (over z), head: 4 (over x, core).
Axes of the slice: x: 2, y: 2, z: 4, core: 2. Of those that a mesh axis runs over, the one named last changes fastest.
Arguments:
- frames: bfloat16 [16384, 1024], P(('groups', 'seq')), parts along dimension 0, may hold values from -14 to 14
- latents: bfloat16 [1024, 1024], replicated, may hold values from -12 to 12
- lengths: int32 [2], P('groups'), parts along dimension 0, may hold values from 4096 to 8192
- w_query: bfloat16 [1024, 1024], P(None, 'head'), may hold values from -0.1875 to 0.1875
- w_key: bfloat16 [1024, 1024], P(None, 'head'), may hold values from -0.1875 to 0.1875
- w_value: bfloat16 [1024, 1024], P(None, 'head'), may hold values from -0.1875 to 0.1875
- w_out: bfloat16 [1024, 1024], P('head'), may hold values from -0.1875 to 0.1875
- w_latent_query: bfloat16 [1024, 1024], P(None, 'head'), may hold values from -0.1875 to 0.1875
- w_latent_out: bfloat16 [1024, 1024], P('head'), may hold values from -0.1875 to 0.1875
Outputs:
- frames_out: bfloat16 [16384, 1024], P(('groups', 'seq'), 'head'), parts along dimension 0
- latents_out: bfloat16 [2048, 1024], P(('groups', 'seq'), 'head'), parts along dimension 0
The draws below stay inside these ranges and needn't reach their ends.
There are 2 independent parts, one for each index of `groups`. The reference program is written for one: setup_inputs(seed, part) draws one part's arguments, and reference() takes and returns one part's arrays. A program takes and returns all parts, laid end to end along the dimension named above; an argument that names none is the same for every part. Nothing has to cross between parts.
All inputs are finite; a program needn't handle non-finite values.
Results may differ from the reference program's by a relative error of at most 0.04.
Values may be sent and summed in bfloat16 or wider, within the bound.
No kernel may reach another device: no remote copies, remote signals or barrier semaphores. Data moves between devices by JAX's collectives and lax.ppermute only.
A program may use at most 128 MiB of HBM per device.

```python
import jax
import jax.numpy as jnp
from jax import lax

D = 1024
HEADS = 16
HD = 64
NLAT = 1024
F_DEV = 2048
HALF = 256
FRAMES = 8192
HEAD_DEV = 4
N_HEAD = 4


def draw_frames(key, part):
    keys = jax.random.split(jax.random.fold_in(key, 11), 1)
    base = jnp.clip(jax.random.normal(keys[0], (FRAMES, D), jnp.float32), -6.0, 6.0)
    return base.astype(jnp.bfloat16)


def draw_latents(key, part):
    keys = jax.random.split(jax.random.fold_in(key, 23), 1)
    base = jnp.clip(jax.random.normal(keys[0], (NLAT, D), jnp.float32), -6.0, 6.0)
    return base.astype(jnp.bfloat16)


def block_scale(key, shape, pieces, low, high):
    def one(position, parts):
        steps = jax.random.uniform(jax.random.fold_in(jax.random.fold_in(key, 6), position), (parts,), jnp.float32, low / len(pieces), high / len(pieces))
        return jnp.repeat(jnp.exp(steps), shape[position] // parts).reshape((-1,) + (1,) * (len(shape) - position - 1))

    gain = one(*pieces[0])
    for cut in pieces[1:]:
        gain = gain * one(*cut)
    return gain


def noise(key, dims, scale, limit, pieces=(), kind=jnp.bfloat16):
    array = jax.random.normal(key, dims, jnp.float32) * scale
    if len(pieces) > 0:
        array = block_scale(key, dims, pieces, -0.22, 0.18) * array
    return jnp.clip(array, min=-limit, max=limit).astype(kind)


def setup_inputs(seed: int = 0, part: int = 0) -> dict:
    key_of = jax.random.split(jax.random.key(seed), 10)
    part_keys = jax.random.split(jax.random.fold_in(key_of[9], part), 10)
    return {
        "frames": draw_frames(jax.random.fold_in(jax.random.fold_in(key_of[9], part), 71), part),
        "latents": draw_latents(jax.random.fold_in(key_of[9], 71), part),
        "lengths": jax.random.randint(part_keys[2], (1,), FRAMES // 2, FRAMES + 1).astype(jnp.int32),
        "w_query": noise(key_of[3], (D, D), D ** -0.5, 0.1875, ((1, 4),)),
        "w_key": noise(key_of[4], (D, D), D ** -0.5, 0.1875, ((1, 4),)),
        "w_value": noise(key_of[5], (D, D), D ** -0.5, 0.1875, ((1, 4),)),
        "w_out": noise(key_of[6], (D, D), D ** -0.5, 0.1875, ((0, 4),)),
        "w_latent_query": noise(key_of[7], (D, D), D ** -0.5, 0.1875, ((1, 4),)),
        "w_latent_out": noise(key_of[8], (D, D), D ** -0.5, 0.1875, ((0, 4),)),
    }


def grouped_product(mixed, weight):
    group_width = HEAD_DEV * HD
    summed = jnp.zeros((mixed.shape[0], weight.shape[1]), jnp.float32)
    for group in range(N_HEAD):
        partial_term = jnp.dot(mixed[:, group * group_width:(group + 1) * group_width], weight[group * group_width:(group + 1) * group_width], preferred_element_type=jnp.float32)
        rounded = lax.optimization_barrier(partial_term.astype(jnp.bfloat16))
        summed = summed + rounded.astype(jnp.float32)
    return summed.astype(jnp.bfloat16)


def reference(frames, latents, lengths, w_query, w_key, w_value, w_out, w_latent_query, w_latent_out):
    length = lengths[0]
    query = jnp.dot(frames, w_query, preferred_element_type=jnp.float32).astype(jnp.bfloat16)
    keyed = jnp.dot(frames, w_key, preferred_element_type=jnp.float32).astype(jnp.bfloat16)
    valued = jnp.dot(frames, w_value, preferred_element_type=jnp.float32).astype(jnp.bfloat16)
    score_scale = HD ** -0.5
    block_size = min(512, F_DEV)
    span = block_size + 2 * HALF
    keys_padded = jnp.pad(keyed, ((HALF, HALF), (0, 0)))
    values_padded = jnp.pad(valued, ((HALF, HALF), (0, 0)))
    offsets = jnp.arange(span)[None, :] - jnp.arange(block_size)[:, None]
    in_window = (offsets >= 0) & (offsets <= 2 * HALF)

    def window_block(block_index):
        row_first = block_index * block_size
        query_block = lax.dynamic_slice_in_dim(query, row_first, block_size, 0).reshape(block_size, HEADS, HD)
        key_block = lax.dynamic_slice_in_dim(keys_padded, row_first, span, 0).reshape(span, HEADS, HD)
        value_block = lax.dynamic_slice_in_dim(values_padded, row_first, span, 0).reshape(span, HEADS, HD)
        scores = jnp.einsum("qhd,khd->hqk", query_block.astype(jnp.float32), key_block.astype(jnp.float32)) * score_scale
        key_pos = row_first - HALF + jnp.arange(span)
        key_valid = (key_pos >= 0) & (key_pos < length)
        allowed = in_window & key_valid[None, :]
        masked = jnp.where(allowed[None], scores, -1e30)
        row_peak = jnp.max(masked, axis=2, keepdims=True)
        weights = jnp.where(allowed[None], jnp.exp(masked - row_peak), 0.0)
        denom = jnp.sum(weights, axis=2)
        blended = jnp.einsum("hqk,khd->qhd", weights.astype(jnp.bfloat16).astype(jnp.float32), value_block.astype(jnp.float32))
        query_pos = row_first + jnp.arange(block_size)
        query_valid = query_pos < length
        divisor = jnp.where(query_valid[None, :], denom, 1.0)
        normed = blended / divisor.T[:, :, None]
        return jnp.where(query_valid[:, None, None], normed, 0.0).astype(jnp.bfloat16).reshape(block_size, D)

    attended = lax.map(window_block, jnp.arange(FRAMES // block_size)).reshape(FRAMES, D)
    frames_out = grouped_product(attended, w_out)

    latent_query = jnp.dot(latents, w_latent_query, preferred_element_type=jnp.float32).astype(jnp.bfloat16)
    frame_valid = jnp.arange(FRAMES) < length

    def latent_head(head_index):
        head_query = lax.dynamic_slice_in_dim(latent_query, head_index * HD, HD, 1)
        head_keys = lax.dynamic_slice_in_dim(keyed, head_index * HD, HD, 1)
        head_values = lax.dynamic_slice_in_dim(valued, head_index * HD, HD, 1)
        scores = jnp.dot(head_query, head_keys.T, preferred_element_type=jnp.float32) * score_scale
        masked = jnp.where(frame_valid[None, :], scores, -1e30)
        row_peak = jnp.max(masked, axis=1, keepdims=True)
        weights = jnp.where(frame_valid[None, :], jnp.exp(masked - row_peak), 0.0)
        totals = jnp.sum(weights, axis=1, keepdims=True)
        gathered = jnp.dot(weights.astype(jnp.bfloat16), head_values, preferred_element_type=jnp.float32)
        return gathered / totals

    per_head = lax.map(latent_head, jnp.arange(HEADS))
    summary = jnp.transpose(per_head, (1, 0, 2)).reshape(NLAT, D).astype(jnp.bfloat16)
    latents_out = grouped_product(summary, w_latent_out)
    return frames_out, latents_out
```

```python
import functools

import jax
import jax.numpy as jnp
from jax import lax
from jax.experimental import pallas as pl
from jax.experimental.pallas import tpu as pltpu
from jax.sharding import PartitionSpec as P

HD = 64
HALF = 256
NEG = -1e30


def extended(block, sides, width):
    for axis, dim in sides:
        count = lax.axis_size(axis)
        forward = [(i, i + 1) for i in range(count - 1)]
        backward = [(target, source) for source, target in forward]
        low = lax.ppermute(
            lax.slice_in_dim(block, block.shape[dim] - width, None, axis=dim), axis, forward
        )
        high = lax.ppermute(lax.slice_in_dim(block, 0, width, axis=dim), axis, backward)
        block = jnp.concatenate([low, block, high], axis=dim)
    return block


def combined_all(value, axis, combine):
    everything = jax.tree.map(
        lambda part, kind: lax.all_gather(part.astype(kind), axis),
        value,
        (jnp.bfloat16, jnp.bfloat16, jnp.bfloat16),
    )

    def take(k):
        return jax.tree.map(lambda part, own: part[k].astype(own.dtype), everything, value)

    return lax.fori_loop(
        1, lax.axis_size(axis), lambda k, so_far: combine(so_far, take(k)), take(0)
    )


def project(source, weight):
    return jnp.dot(source, weight, preferred_element_type=jnp.float32).astype(jnp.bfloat16)


def combine(earlier, latter):
    peak_first, total_first, accum_first = earlier
    peak_second, total_second, accum_second = latter
    joint = jnp.maximum(peak_first, peak_second)
    factor_first = jnp.exp(peak_first - joint)
    factor_second = jnp.exp(peak_second - joint)
    summed_total = total_first * factor_first + total_second * factor_second
    summed_accum = accum_first * jnp.repeat(factor_first, HD, axis=1) + accum_second * jnp.repeat(
        factor_second, HD, axis=1
    )
    return (joint, summed_total, summed_accum)


def window_kernel(scal_ref, q_ref, k_ref, v_ref, w_ref, o_ref, att_ref, *, heads, scale):
    tq = q_ref.shape[0]
    span = tq + 2 * HALF
    start = pl.multiple_of(pl.program_id(0) * tq, tq)
    first = scal_ref[0]
    length = scal_ref[1]
    row = lax.broadcasted_iota(jnp.int32, (tq, span), 0)
    col = lax.broadcasted_iota(jnp.int32, (tq, span), 1)
    offset = col - row
    key_pos = first + start - HALF + col
    allowed = (offset >= 0) & (offset <= 2 * HALF) & (key_pos >= 0) & (key_pos < length)
    query_pos = first + start + lax.broadcasted_iota(jnp.int32, (tq, 1), 0)
    query_valid = query_pos < length
    for h in range(heads):
        cols = slice(h * HD, (h + 1) * HD)
        q = q_ref[:, cols]
        k = k_ref[pl.ds(start, span), cols]
        v = v_ref[pl.ds(start, span), cols]
        s = lax.dot_general(
            q, k, (((1,), (1,)), ((), ())), preferred_element_type=jnp.float32
        ) * scale
        masked = jnp.where(allowed, s, NEG)
        peak = jnp.max(masked, axis=1, keepdims=True)
        weights = jnp.where(allowed, jnp.exp(masked - peak), 0.0)
        denom = jnp.sum(weights, axis=1, keepdims=True)
        blended = jnp.dot(weights.astype(jnp.bfloat16), v, preferred_element_type=jnp.float32)
        divisor = jnp.where(query_valid, denom, 1.0)
        att_ref[:, cols] = jnp.where(query_valid, blended / divisor, 0.0).astype(jnp.bfloat16)
    o_ref[...] = jnp.dot(
        att_ref[...], w_ref[...], preferred_element_type=jnp.float32
    ).astype(jnp.bfloat16)


def window_attention(query, keys_wide, values_wide, w_out, first_frame, length):
    frame_count, width = query.shape
    out_width = w_out.shape[1]
    tq = min(256, frame_count)
    scal = jnp.stack([first_frame, length]).astype(jnp.int32)
    kernel = functools.partial(window_kernel, heads=width // HD, scale=HD ** (-0.5))
    return pl.pallas_call(
        kernel,
        out_shape=jax.ShapeDtypeStruct((frame_count, out_width), jnp.bfloat16),
        grid_spec=pltpu.PrefetchScalarGridSpec(
            num_scalar_prefetch=1,
            grid=(frame_count // tq,),
            in_specs=[
                pl.BlockSpec((tq, width), lambda i, s: (i, 0)),
                pl.BlockSpec(keys_wide.shape, lambda i, s: (0, 0)),
                pl.BlockSpec(values_wide.shape, lambda i, s: (0, 0)),
                pl.BlockSpec(w_out.shape, lambda i, s: (0, 0)),
            ],
            out_specs=pl.BlockSpec((tq, out_width), lambda i, s: (i, 0)),
            scratch_shapes=[pltpu.VMEM((tq, width), jnp.bfloat16)],
        ),
    )(scal, query, keys_wide, values_wide, w_out)


def latent_kernel(scal_ref, q_ref, k_ref, v_ref, acc_ref, stat_ref, *, heads, scale):
    tl = q_ref.shape[0]
    frame_count = k_ref.shape[0]
    valid = lax.broadcasted_iota(jnp.int32, (tl, frame_count), 1) < scal_ref[0]
    stat_ref[...] = jnp.zeros_like(stat_ref)
    for h in range(heads):
        cols = slice(h * HD, (h + 1) * HD)
        s = lax.dot_general(
            q_ref[:, cols], k_ref[:, cols], (((1,), (1,)), ((), ())),
            preferred_element_type=jnp.float32,
        ) * scale
        masked = jnp.where(valid, s, NEG)
        peak = jnp.max(masked, axis=1, keepdims=True)
        weights = jnp.where(valid, jnp.exp(masked - peak), 0.0)
        total = jnp.sum(weights, axis=1, keepdims=True)
        acc_ref[:, cols] = jnp.dot(
            weights.astype(jnp.bfloat16), v_ref[:, cols], preferred_element_type=jnp.float32
        )
        stat_ref[:, h : h + 1] = peak
        stat_ref[:, heads + h : heads + h + 1] = total


def latent_attention(latent_query, keyed, valued, valid_count):
    latent_count, width = latent_query.shape
    heads = width // HD
    tl = min(256, latent_count)
    scal = jnp.reshape(valid_count, (1,)).astype(jnp.int32)
    kernel = functools.partial(latent_kernel, heads=heads, scale=HD ** (-0.5))
    acc, stat = pl.pallas_call(
        kernel,
        out_shape=(
            jax.ShapeDtypeStruct((latent_count, width), jnp.float32),
            jax.ShapeDtypeStruct((latent_count, 128), jnp.float32),
        ),
        grid_spec=pltpu.PrefetchScalarGridSpec(
            num_scalar_prefetch=1,
            grid=(latent_count // tl,),
            in_specs=[
                pl.BlockSpec((tl, width), lambda i, s: (i, 0)),
                pl.BlockSpec(keyed.shape, lambda i, s: (0, 0)),
                pl.BlockSpec(valued.shape, lambda i, s: (0, 0)),
            ],
            out_specs=[
                pl.BlockSpec((tl, width), lambda i, s: (i, 0)),
                pl.BlockSpec((tl, 128), lambda i, s: (i, 0)),
            ],
        ),
    )(scal, latent_query, keyed, valued)
    return stat[:, :heads], stat[:, heads : 2 * heads], acc


def per_device(
    frames, latents, lengths, w_query, w_key, w_value, w_out, w_latent_query, w_latent_out
):
    frame_count = frames.shape[0]
    head_width = w_query.shape[1]
    seq_devices = lax.axis_size("seq")
    seq_place = lax.axis_index("seq")
    first_frame = seq_place * frame_count
    length = lengths[0]
    query = project(frames, w_query)
    keyed = project(frames, w_key)
    valued = project(frames, w_value)
    stacked = jnp.concatenate([keyed, valued], axis=1)
    padded = extended(stacked, (("seq", 0),), HALF)
    keys_wide = padded[:, :head_width]
    values_wide = padded[:, head_width:]
    frame_terms = window_attention(query, keys_wide, values_wide, w_out, first_frame, length)
    frames_out = lax.psum_scatter(frame_terms, "head", scatter_dimension=1, tiled=True)
    latent_count = latents.shape[0]
    latent_query = project(latents, w_latent_query)
    valid_count = jnp.clip(length - first_frame, 0, frame_count)
    peaks, totals, local_accum = latent_attention(latent_query, keyed, valued, valid_count)
    rows_here = latent_count // seq_devices
    merged_peak, merged_total, merged_accum = combined_all(
        (peaks, totals, local_accum), "seq", combine
    )
    own_total = lax.dynamic_slice_in_dim(merged_total, seq_place * rows_here, rows_here, 0)
    own_accum = lax.dynamic_slice_in_dim(merged_accum, seq_place * rows_here, rows_here, 0)
    summary = (own_accum / jnp.repeat(own_total, HD, axis=1)).astype(jnp.bfloat16)
    latent_terms = jnp.dot(summary, w_latent_out, preferred_element_type=jnp.float32)
    latents_out = lax.psum_scatter(
        latent_terms.astype(jnp.bfloat16), "head", scatter_dimension=1, tiled=True
    )
    return (frames_out, latents_out)


def solution(mesh):
    return jax.shard_map(
        per_device,
        mesh=mesh,
        in_specs=(
            P(("groups", "seq"), None),
            P(),
            P("groups"),
            P(None, "head"),
            P(None, "head"),
            P(None, "head"),
            P("head", None),
            P(None, "head"),
            P("head", None),
        ),
        out_specs=(P(("groups", "seq"), "head"), P(("groups", "seq"), "head")),
        check_vma=False,
    )
```

```python
import functools

import jax
import jax.numpy as jnp
from jax import lax
from jax.experimental import pallas as pl
from jax.experimental.pallas import tpu as pltpu
from jax.sharding import PartitionSpec as P

HD = 64
HALF = 256
NEG = -1e30


def extended(block, sides, width):
    for axis, dim in sides:
        count = lax.axis_size(axis)
        forward = [(i, i + 1) for i in range(count - 1)]
        backward = [(target, source) for source, target in forward]
        low = lax.ppermute(
            lax.slice_in_dim(block, block.shape[dim] - width, None, axis=dim), axis, forward
        )
        high = lax.ppermute(lax.slice_in_dim(block, 0, width, axis=dim), axis, backward)
        block = jnp.concatenate([low, block, high], axis=dim)
    return block


def project(source, weight):
    return jnp.dot(source, weight, preferred_element_type=jnp.float32).astype(jnp.bfloat16)


def window_kernel(scal_ref, q_ref, k_ref, v_ref, w_ref, o_ref, att_ref, *, heads, scale):
    tq = q_ref.shape[0]
    span = tq + 2 * HALF
    start = pl.multiple_of(scal_ref[2] + pl.program_id(0) * tq, tq)
    first = scal_ref[0]
    length = scal_ref[1]
    row = lax.broadcasted_iota(jnp.int32, (tq, span), 0)
    col = lax.broadcasted_iota(jnp.int32, (tq, span), 1)
    offset = col - row
    key_pos = first + start - HALF + col
    allowed = (offset >= 0) & (offset <= 2 * HALF) & (key_pos >= 0) & (key_pos < length)
    query_pos = first + start + lax.broadcasted_iota(jnp.int32, (tq, 1), 0)
    query_valid = query_pos < length
    for h in range(heads):
        cols = slice(h * HD, (h + 1) * HD)
        q = q_ref[:, cols]
        k = k_ref[pl.ds(start, span), cols]
        v = v_ref[pl.ds(start, span), cols]
        s = lax.dot_general(
            q, k, (((1,), (1,)), ((), ())), preferred_element_type=jnp.float32
        ) * scale
        masked = jnp.where(allowed, s, NEG)
        peak = jnp.max(masked, axis=1, keepdims=True)
        weights = jnp.where(allowed, jnp.exp(masked - peak), 0.0)
        denom = jnp.sum(weights, axis=1, keepdims=True)
        blended = jnp.dot(weights.astype(jnp.bfloat16), v, preferred_element_type=jnp.float32)
        divisor = jnp.where(query_valid, denom, 1.0)
        att_ref[:, cols] = jnp.where(query_valid, blended / divisor, 0.0).astype(jnp.bfloat16)
    o_ref[...] = jnp.dot(
        att_ref[...], w_ref[...], preferred_element_type=jnp.float32
    ).astype(jnp.bfloat16)


def window_attention(query, keys_wide, values_wide, w_out, first_frame, length, row_base, rows):
    width = query.shape[1]
    out_width = w_out.shape[1]
    tq = min(256, rows)
    block_base = row_base // tq
    scal = jnp.array([0, 0, row_base], jnp.int32).at[0].set(first_frame).at[1].set(length)
    kernel = functools.partial(window_kernel, heads=width // HD, scale=HD ** (-0.5))
    return pl.pallas_call(
        kernel,
        out_shape=jax.ShapeDtypeStruct((rows, out_width), jnp.bfloat16),
        grid_spec=pltpu.PrefetchScalarGridSpec(
            num_scalar_prefetch=1,
            grid=(rows // tq,),
            in_specs=[
                pl.BlockSpec((tq, width), lambda i, s: (i + block_base, 0)),
                pl.BlockSpec(keys_wide.shape, lambda i, s: (0, 0)),
                pl.BlockSpec(values_wide.shape, lambda i, s: (0, 0)),
                pl.BlockSpec(w_out.shape, lambda i, s: (0, 0)),
            ],
            out_specs=pl.BlockSpec((tq, out_width), lambda i, s: (i, 0)),
            scratch_shapes=[pltpu.VMEM((tq, width), jnp.bfloat16)],
        ),
    )(scal, query, keys_wide, values_wide, w_out)


def latent_kernel(scal_ref, q_ref, k_ref, v_ref, acc_ref, stat_ref, *, heads, scale):
    tl = q_ref.shape[0]
    frame_count = k_ref.shape[0]
    valid = lax.broadcasted_iota(jnp.int32, (tl, frame_count), 1) < scal_ref[0]
    stat_ref[...] = jnp.zeros_like(stat_ref)
    for h in range(heads):
        cols = slice(h * HD, (h + 1) * HD)
        s = lax.dot_general(
            q_ref[:, cols], k_ref[:, cols], (((1,), (1,)), ((), ())),
            preferred_element_type=jnp.float32,
        ) * scale
        masked = jnp.where(valid, s, NEG)
        peak = jnp.max(masked, axis=1, keepdims=True)
        weights = jnp.where(valid, jnp.exp(masked - peak), 0.0)
        total = jnp.sum(weights, axis=1, keepdims=True)
        acc_ref[:, cols] = jnp.dot(
            weights.astype(jnp.bfloat16), v_ref[:, cols], preferred_element_type=jnp.float32
        )
        stat_ref[:, h : h + 1] = peak
        stat_ref[:, heads + h : heads + h + 1] = total


def latent_attention(latent_query, keyed, valued, valid_count):
    latent_count, width = latent_query.shape
    heads = width // HD
    tl = min(256, latent_count)
    scal = jnp.reshape(valid_count, (1,)).astype(jnp.int32)
    kernel = functools.partial(latent_kernel, heads=heads, scale=HD ** (-0.5))
    acc, stat = pl.pallas_call(
        kernel,
        out_shape=(
            jax.ShapeDtypeStruct((latent_count, width), jnp.float32),
            jax.ShapeDtypeStruct((latent_count, 128), jnp.float32),
        ),
        grid_spec=pltpu.PrefetchScalarGridSpec(
            num_scalar_prefetch=1,
            grid=(latent_count // tl,),
            in_specs=[
                pl.BlockSpec((tl, width), lambda i, s: (i, 0)),
                pl.BlockSpec(keyed.shape, lambda i, s: (0, 0)),
                pl.BlockSpec(valued.shape, lambda i, s: (0, 0)),
            ],
            out_specs=[
                pl.BlockSpec((tl, width), lambda i, s: (i, 0)),
                pl.BlockSpec((tl, 128), lambda i, s: (i, 0)),
            ],
        ),
    )(scal, latent_query, keyed, valued)
    return stat[:, :heads], stat[:, heads : 2 * heads], acc


def shifted_blocks(payload, axis, rows):
    count = lax.axis_size(axis)
    place = lax.axis_index(axis)
    own = lax.dynamic_slice_in_dim(payload, place * rows, rows, 0)
    parts = [own]
    for shift in range(1, count):
        target = (place + shift) % count
        block = lax.dynamic_slice_in_dim(payload, target * rows, rows, 0)
        pairs = [(i, (i + shift) % count) for i in range(count)]
        parts.append(lax.ppermute(block, axis, pairs))
    return jnp.stack(parts)


def column_sum(partial, axis):
    count = lax.axis_size(axis)
    place = lax.axis_index(axis)
    width = partial.shape[1] // count
    own = lax.dynamic_slice_in_dim(partial, place * width, width, 1)
    total = own.astype(jnp.float32)
    for shift in range(1, count):
        target = (place + shift) % count
        block = lax.dynamic_slice_in_dim(partial, target * width, width, 1)
        pairs = [(i, (i + shift) % count) for i in range(count)]
        total = total + lax.ppermute(block, axis, pairs).astype(jnp.float32)
    return total.astype(jnp.bfloat16)


def per_device(
    frames, latents, lengths, w_query, w_key, w_value, w_out, w_latent_query, w_latent_out
):
    frame_count = frames.shape[0]
    head_width = w_query.shape[1]
    heads_here = head_width // HD
    seq_devices = lax.axis_size("seq")
    seq_place = lax.axis_index("seq")
    first_frame = seq_place * frame_count
    length = lengths[0]
    query = project(frames, w_query)
    keyed = project(frames, w_key)
    valued = project(frames, w_value)
    stacked = jnp.concatenate([keyed, valued], axis=1)
    padded = extended(stacked, (("seq", 0),), HALF)
    keys_wide = padded[:, :head_width]
    values_wide = padded[:, head_width:]
    chunks = 2 if frame_count % 512 == 0 else 1
    chunk_rows = frame_count // chunks
    frame_parts = []
    for c in range(chunks):
        terms = window_attention(
            query, keys_wide, values_wide, w_out, first_frame, length, c * chunk_rows, chunk_rows
        )
        if c == 0:
            terms, keyed, valued = lax.optimization_barrier((terms, keyed, valued))
        frame_parts.append(lax.psum_scatter(terms, "head", scatter_dimension=1, tiled=True))
    frames_out = jnp.concatenate(frame_parts, axis=0)
    latent_count = latents.shape[0]
    latent_query = project(latents, w_latent_query)
    valid_count = jnp.clip(length - first_frame, 0, frame_count)
    peaks, totals, local_accum = latent_attention(latent_query, keyed, valued, valid_count)
    rows_here = latent_count // seq_devices
    payload = jnp.concatenate([local_accum, peaks, totals], axis=1)
    parts = shifted_blocks(payload, "seq", rows_here)
    part_accum = parts[:, :, :head_width]
    part_peak = parts[:, :, head_width : head_width + heads_here]
    part_total = parts[:, :, head_width + heads_here :]
    joint = jnp.max(part_peak, axis=0)
    factor = jnp.exp(part_peak - joint[None])
    own_total = jnp.sum(part_total * factor, axis=0)
    own_accum = jnp.sum(part_accum * jnp.repeat(factor, HD, axis=2), axis=0)
    summary = (own_accum / jnp.repeat(own_total, HD, axis=1)).astype(jnp.bfloat16)
    latent_terms = jnp.dot(summary, w_latent_out, preferred_element_type=jnp.float32)
    latents_out = column_sum(latent_terms.astype(jnp.bfloat16), "head")
    return (frames_out, latents_out)


def solution(mesh):
    return jax.shard_map(
        per_device,
        mesh=mesh,
        in_specs=(
            P(("groups", "seq"), None),
            P(),
            P("groups"),
            P(None, "head"),
            P(None, "head"),
            P(None, "head"),
            P("head", None),
            P(None, "head"),
            P("head", None),
        ),
        out_specs=(P(("groups", "seq"), "head"), P(("groups", "seq"), "head")),
        check_vma=False,
    )
```

```python
import functools

import jax
import jax.numpy as jnp
from jax import lax
from jax.experimental import pallas as pl
from jax.experimental.pallas import tpu as pltpu
from jax.sharding import PartitionSpec as P

HD = 64
HALF = 256
NEG = -1e30


def extended(block, sides, width):
    for axis, dim in sides:
        count = lax.axis_size(axis)
        forward = [(i, i + 1) for i in range(count - 1)]
        backward = [(target, source) for source, target in forward]
        low = lax.ppermute(
            lax.slice_in_dim(block, block.shape[dim] - width, None, axis=dim), axis, forward
        )
        high = lax.ppermute(lax.slice_in_dim(block, 0, width, axis=dim), axis, backward)
        block = jnp.concatenate([low, block, high], axis=dim)
    return block


def project(source, weight):
    return jnp.dot(source, weight, preferred_element_type=jnp.float32).astype(jnp.bfloat16)


def window_kernel(scal_ref, q_ref, k_ref, v_ref, w_ref, o_ref, att_ref, *, heads, scale):
    tq = q_ref.shape[0]
    span = tq + 2 * HALF
    start = pl.multiple_of(scal_ref[2] + pl.program_id(0) * tq, tq)
    first = scal_ref[0]
    length = scal_ref[1]
    row = lax.broadcasted_iota(jnp.int32, (tq, span), 0)
    col = lax.broadcasted_iota(jnp.int32, (tq, span), 1)
    offset = col - row
    key_pos = first + start - HALF + col
    allowed = (offset >= 0) & (offset <= 2 * HALF) & (key_pos >= 0) & (key_pos < length)
    query_pos = first + start + lax.broadcasted_iota(jnp.int32, (tq, 1), 0)
    query_valid = query_pos < length
    for h in range(heads):
        cols = slice(h * HD, (h + 1) * HD)
        q = q_ref[:, cols]
        k = k_ref[pl.ds(start, span), cols]
        v = v_ref[pl.ds(start, span), cols]
        s = lax.dot_general(
            q, k, (((1,), (1,)), ((), ())), preferred_element_type=jnp.float32
        ) * scale
        masked = jnp.where(allowed, s, NEG)
        peak = jnp.max(masked, axis=1, keepdims=True)
        weights = jnp.where(allowed, jnp.exp(masked - peak), 0.0)
        denom = jnp.sum(weights, axis=1, keepdims=True)
        blended = jnp.dot(weights.astype(jnp.bfloat16), v, preferred_element_type=jnp.float32)
        divisor = jnp.where(query_valid, denom, 1.0)
        att_ref[:, cols] = jnp.where(query_valid, blended / divisor, 0.0).astype(jnp.bfloat16)
    o_ref[...] = jnp.dot(
        att_ref[...], w_ref[...], preferred_element_type=jnp.float32
    ).astype(jnp.bfloat16)


def window_attention(query, keys_wide, values_wide, w_out, first_frame, length, row_base, rows):
    width = query.shape[1]
    out_width = w_out.shape[1]
    tq = min(256, rows)
    block_base = row_base // tq
    scal = jnp.array([0, 0, row_base], jnp.int32).at[0].set(first_frame).at[1].set(length)
    kernel = functools.partial(window_kernel, heads=width // HD, scale=HD ** (-0.5))
    span = tq + 2 * HALF
    cost = pl.CostEstimate(
        flops=4 * rows * span * width + 2 * rows * width * out_width,
        transcendentals=rows * span * (width // HD),
        bytes_accessed=2 * (rows * width + 2 * keys_wide.size + w_out.size + rows * out_width),
    )
    return pl.pallas_call(
        kernel,
        cost_estimate=cost,
        out_shape=jax.ShapeDtypeStruct((rows, out_width), jnp.bfloat16),
        grid_spec=pltpu.PrefetchScalarGridSpec(
            num_scalar_prefetch=1,
            grid=(rows // tq,),
            in_specs=[
                pl.BlockSpec((tq, width), lambda i, s: (i + block_base, 0)),
                pl.BlockSpec(keys_wide.shape, lambda i, s: (0, 0)),
                pl.BlockSpec(values_wide.shape, lambda i, s: (0, 0)),
                pl.BlockSpec(w_out.shape, lambda i, s: (0, 0)),
            ],
            out_specs=pl.BlockSpec((tq, out_width), lambda i, s: (i, 0)),
            scratch_shapes=[pltpu.VMEM((tq, width), jnp.bfloat16)],
        ),
    )(scal, query, keys_wide, values_wide, w_out)


def latent_kernel(scal_ref, q_ref, k_ref, v_ref, acc_ref, stat_ref, *, heads, scale):
    tl = q_ref.shape[0]
    frame_count = k_ref.shape[0]
    valid = lax.broadcasted_iota(jnp.int32, (tl, frame_count), 1) < scal_ref[0]
    stat_ref[...] = jnp.zeros_like(stat_ref)
    for h in range(heads):
        cols = slice(h * HD, (h + 1) * HD)
        s = lax.dot_general(
            q_ref[:, cols], k_ref[:, cols], (((1,), (1,)), ((), ())),
            preferred_element_type=jnp.float32,
        ) * scale
        masked = jnp.where(valid, s, NEG)
        peak = jnp.max(masked, axis=1, keepdims=True)
        weights = jnp.where(valid, jnp.exp(masked - peak), 0.0)
        total = jnp.sum(weights, axis=1, keepdims=True)
        acc_ref[:, cols] = jnp.dot(
            weights.astype(jnp.bfloat16), v_ref[:, cols], preferred_element_type=jnp.float32
        )
        stat_ref[:, h : h + 1] = peak
        stat_ref[:, heads + h : heads + h + 1] = total


def latent_attention(latent_query, keyed, valued, valid_count):
    latent_count, width = latent_query.shape
    heads = width // HD
    tl = min(256, latent_count)
    scal = jnp.reshape(valid_count, (1,)).astype(jnp.int32)
    kernel = functools.partial(latent_kernel, heads=heads, scale=HD ** (-0.5))
    frame_count = keyed.shape[0]
    cost = pl.CostEstimate(
        flops=4 * latent_count * frame_count * width,
        transcendentals=latent_count * frame_count * heads,
        bytes_accessed=2 * (latent_query.size + 2 * keyed.size) + 4 * latent_count * (width + 128),
    )
    acc, stat = pl.pallas_call(
        kernel,
        cost_estimate=cost,
        out_shape=(
            jax.ShapeDtypeStruct((latent_count, width), jnp.float32),
            jax.ShapeDtypeStruct((latent_count, 128), jnp.float32),
        ),
        grid_spec=pltpu.PrefetchScalarGridSpec(
            num_scalar_prefetch=1,
            grid=(latent_count // tl,),
            in_specs=[
                pl.BlockSpec((tl, width), lambda i, s: (i, 0)),
                pl.BlockSpec(keyed.shape, lambda i, s: (0, 0)),
                pl.BlockSpec(valued.shape, lambda i, s: (0, 0)),
            ],
            out_specs=[
                pl.BlockSpec((tl, width), lambda i, s: (i, 0)),
                pl.BlockSpec((tl, 128), lambda i, s: (i, 0)),
            ],
        ),
    )(scal, latent_query, keyed, valued)
    return stat[:, :heads], stat[:, heads : 2 * heads], acc


def shifted_blocks(payload, axis, rows):
    count = lax.axis_size(axis)
    place = lax.axis_index(axis)
    own = lax.dynamic_slice_in_dim(payload, place * rows, rows, 0)
    parts = [own]
    for shift in range(1, count):
        target = (place + shift) % count
        block = lax.dynamic_slice_in_dim(payload, target * rows, rows, 0)
        pairs = [(i, (i + shift) % count) for i in range(count)]
        parts.append(lax.ppermute(block, axis, pairs))
    return jnp.stack(parts)


def column_sum(partial, axis):
    count = lax.axis_size(axis)
    place = lax.axis_index(axis)
    width = partial.shape[1] // count
    own = lax.dynamic_slice_in_dim(partial, place * width, width, 1)
    total = own.astype(jnp.float32)
    for shift in range(1, count):
        target = (place + shift) % count
        block = lax.dynamic_slice_in_dim(partial, target * width, width, 1)
        pairs = [(i, (i + shift) % count) for i in range(count)]
        total = total + lax.ppermute(block, axis, pairs).astype(jnp.float32)
    return total.astype(jnp.bfloat16)


def per_device(
    frames, latents, lengths, w_query, w_key, w_value, w_out, w_latent_query, w_latent_out
):
    frame_count = frames.shape[0]
    head_width = w_query.shape[1]
    heads_here = head_width // HD
    seq_devices = lax.axis_size("seq")
    seq_place = lax.axis_index("seq")
    first_frame = seq_place * frame_count
    length = lengths[0]
    query = project(frames, w_query)
    keyed = project(frames, w_key)
    valued = project(frames, w_value)
    stacked = jnp.concatenate([keyed, valued], axis=1)
    padded = extended(stacked, (("seq", 0),), HALF)
    keys_wide = padded[:, :head_width]
    values_wide = padded[:, head_width:]
    latent_count = latents.shape[0]
    latent_query = project(latents, w_latent_query)
    valid_count = jnp.clip(length - first_frame, 0, frame_count)
    peaks, totals, local_accum = latent_attention(latent_query, keyed, valued, valid_count)
    rows_here = latent_count // seq_devices
    payload = jnp.concatenate([local_accum, peaks, totals], axis=1)
    payload, query, keys_wide, values_wide = lax.optimization_barrier(
        (payload, query, keys_wide, values_wide)
    )
    parts = shifted_blocks(payload, "seq", rows_here)
    frame_terms = window_attention(
        query, keys_wide, values_wide, w_out, first_frame, length, 0, frame_count
    )
    frames_out = lax.psum_scatter(frame_terms, "head", scatter_dimension=1, tiled=True)
    part_accum = parts[:, :, :head_width]
    part_peak = parts[:, :, head_width : head_width + heads_here]
    part_total = parts[:, :, head_width + heads_here :]
    joint = jnp.max(part_peak, axis=0)
    factor = jnp.exp(part_peak - joint[None])
    own_total = jnp.sum(part_total * factor, axis=0)
    own_accum = jnp.sum(part_accum * jnp.repeat(factor, HD, axis=2), axis=0)
    summary = (own_accum / jnp.repeat(own_total, HD, axis=1)).astype(jnp.bfloat16)
    latent_terms = jnp.dot(summary, w_latent_out, preferred_element_type=jnp.float32)
    latents_out = column_sum(latent_terms.astype(jnp.bfloat16), "head")
    return (frames_out, latents_out)


def solution(mesh):
    return jax.shard_map(
        per_device,
        mesh=mesh,
        in_specs=(
            P(("groups", "seq"), None),
            P(),
            P("groups"),
            P(None, "head"),
            P(None, "head"),
            P(None, "head"),
            P("head", None),
            P(None, "head"),
            P("head", None),
        ),
        out_specs=(P(("groups", "seq"), "head"), P(("groups", "seq"), "head")),
        check_vma=False,
    )
```

```python
import functools

import jax
import jax.numpy as jnp
from jax import lax
from jax.experimental import pallas as pl
from jax.experimental.pallas import tpu as pltpu
from jax.sharding import PartitionSpec as P

HD = 64
HALF = 256
NEG = -1e30


def halos(keyed, valued, axis):
    count = lax.axis_size(axis)
    forward = [(i, i + 1) for i in range(count - 1)]
    backward = [(target, source) for source, target in forward]
    tail = jnp.concatenate([keyed[-HALF:], valued[-HALF:]], axis=1)
    head = jnp.concatenate([keyed[:HALF], valued[:HALF]], axis=1)
    return lax.ppermute(tail, axis, forward), lax.ppermute(head, axis, backward)


def project(source, weight):
    return jnp.dot(source, weight, preferred_element_type=jnp.float32).astype(jnp.bfloat16)


def window_kernel(
    scal_ref, q_ref, k_ref, v_ref, low_ref, high_ref, w_ref, o_ref, kbuf, vbuf, att_ref, *,
    heads, scale
):
    tq = q_ref.shape[0]
    frame_count, width = k_ref.shape
    span = tq + 2 * HALF

    @pl.when(pl.program_id(0) == 0)
    def _fill():
        kbuf[0:HALF, :] = low_ref[:, 0:width]
        vbuf[0:HALF, :] = low_ref[:, width : 2 * width]
        kbuf[HALF : HALF + frame_count, :] = k_ref[...]
        vbuf[HALF : HALF + frame_count, :] = v_ref[...]
        kbuf[HALF + frame_count :, :] = high_ref[:, 0:width]
        vbuf[HALF + frame_count :, :] = high_ref[:, width : 2 * width]

    start = pl.multiple_of(scal_ref[2] + pl.program_id(0) * tq, tq)
    first = scal_ref[0]
    length = scal_ref[1]
    row = lax.broadcasted_iota(jnp.int32, (tq, span), 0)
    col = lax.broadcasted_iota(jnp.int32, (tq, span), 1)
    offset = col - row
    key_pos = first + start - HALF + col
    allowed = (offset >= 0) & (offset <= 2 * HALF) & (key_pos >= 0) & (key_pos < length)
    query_pos = first + start + lax.broadcasted_iota(jnp.int32, (tq, 1), 0)
    query_valid = query_pos < length
    for h in range(heads):
        cols = slice(h * HD, (h + 1) * HD)
        q = q_ref[:, cols]
        k = kbuf[pl.ds(start, span), cols]
        v = vbuf[pl.ds(start, span), cols]
        s = lax.dot_general(
            q, k, (((1,), (1,)), ((), ())), preferred_element_type=jnp.float32
        ) * scale
        masked = jnp.where(allowed, s, NEG)
        peak = jnp.max(masked, axis=1, keepdims=True)
        weights = jnp.where(allowed, jnp.exp(masked - peak), 0.0)
        denom = jnp.sum(weights, axis=1, keepdims=True)
        blended = jnp.dot(weights.astype(jnp.bfloat16), v, preferred_element_type=jnp.float32)
        divisor = jnp.where(query_valid, denom, 1.0)
        att_ref[:, cols] = jnp.where(query_valid, blended / divisor, 0.0).astype(jnp.bfloat16)
    o_ref[...] = jnp.dot(
        att_ref[...], w_ref[...], preferred_element_type=jnp.float32
    ).astype(jnp.bfloat16)


def window_attention(query, keyed, valued, low, high, w_out, first_frame, length, row_base, rows):
    frame_count, width = query.shape
    out_width = w_out.shape[1]
    tq = min(256, rows)
    block_base = row_base // tq
    span = tq + 2 * HALF
    scal = jnp.array([0, 0, row_base], jnp.int32).at[0].set(first_frame).at[1].set(length)
    kernel = functools.partial(window_kernel, heads=width // HD, scale=HD ** (-0.5))
    cost = pl.CostEstimate(
        flops=4 * rows * span * width + 2 * rows * width * out_width,
        transcendentals=rows * span * (width // HD),
        bytes_accessed=2 * (2 * query.size + rows * width + 2 * low.size + w_out.size + rows * out_width),
    )
    full = lambda i, s: (0, 0)
    return pl.pallas_call(
        kernel,
        cost_estimate=cost,
        out_shape=jax.ShapeDtypeStruct((rows, out_width), jnp.bfloat16),
        grid_spec=pltpu.PrefetchScalarGridSpec(
            num_scalar_prefetch=1,
            grid=(rows // tq,),
            in_specs=[
                pl.BlockSpec((tq, width), lambda i, s: (i + block_base, 0)),
                pl.BlockSpec(keyed.shape, full),
                pl.BlockSpec(valued.shape, full),
                pl.BlockSpec(low.shape, full),
                pl.BlockSpec(high.shape, full),
                pl.BlockSpec(w_out.shape, full),
            ],
            out_specs=pl.BlockSpec((tq, out_width), lambda i, s: (i, 0)),
            scratch_shapes=[
                pltpu.VMEM((frame_count + 2 * HALF, width), jnp.bfloat16),
                pltpu.VMEM((frame_count + 2 * HALF, width), jnp.bfloat16),
                pltpu.VMEM((tq, width), jnp.bfloat16),
            ],
        ),
        compiler_params=pltpu.CompilerParams(dimension_semantics=("arbitrary",)),
    )(scal, query, keyed, valued, low, high, w_out)


def latent_kernel(scal_ref, q_ref, k_ref, v_ref, acc_ref, stat_ref, *, heads, scale):
    tl = q_ref.shape[0]
    frame_count = k_ref.shape[0]
    valid = lax.broadcasted_iota(jnp.int32, (tl, frame_count), 1) < scal_ref[0]
    stat_ref[...] = jnp.zeros_like(stat_ref)
    for h in range(heads):
        cols = slice(h * HD, (h + 1) * HD)
        s = lax.dot_general(
            q_ref[:, cols], k_ref[:, cols], (((1,), (1,)), ((), ())),
            preferred_element_type=jnp.float32,
        ) * scale
        masked = jnp.where(valid, s, NEG)
        peak = jnp.max(masked, axis=1, keepdims=True)
        weights = jnp.where(valid, jnp.exp(masked - peak), 0.0)
        total = jnp.sum(weights, axis=1, keepdims=True)
        acc_ref[:, cols] = jnp.dot(
            weights.astype(jnp.bfloat16), v_ref[:, cols], preferred_element_type=jnp.float32
        )
        stat_ref[:, h : h + 1] = peak
        stat_ref[:, heads + h : heads + h + 1] = total


def latent_attention(latent_query, keyed, valued, valid_count):
    latent_count, width = latent_query.shape
    heads = width // HD
    tl = min(256, latent_count)
    scal = jnp.reshape(valid_count, (1,)).astype(jnp.int32)
    kernel = functools.partial(latent_kernel, heads=heads, scale=HD ** (-0.5))
    frame_count = keyed.shape[0]
    cost = pl.CostEstimate(
        flops=4 * latent_count * frame_count * width,
        transcendentals=latent_count * frame_count * heads,
        bytes_accessed=2 * (latent_query.size + 2 * keyed.size) + 4 * latent_count * (width + 128),
    )
    acc, stat = pl.pallas_call(
        kernel,
        cost_estimate=cost,
        out_shape=(
            jax.ShapeDtypeStruct((latent_count, width), jnp.float32),
            jax.ShapeDtypeStruct((latent_count, 128), jnp.float32),
        ),
        grid_spec=pltpu.PrefetchScalarGridSpec(
            num_scalar_prefetch=1,
            grid=(latent_count // tl,),
            in_specs=[
                pl.BlockSpec((tl, width), lambda i, s: (i, 0)),
                pl.BlockSpec(keyed.shape, lambda i, s: (0, 0)),
                pl.BlockSpec(valued.shape, lambda i, s: (0, 0)),
            ],
            out_specs=[
                pl.BlockSpec((tl, width), lambda i, s: (i, 0)),
                pl.BlockSpec((tl, 128), lambda i, s: (i, 0)),
            ],
        ),
    )(scal, latent_query, keyed, valued)
    return stat[:, :heads], stat[:, heads : 2 * heads], acc


def shifted_blocks(payload, axis, rows):
    count = lax.axis_size(axis)
    place = lax.axis_index(axis)
    own = lax.dynamic_slice_in_dim(payload, place * rows, rows, 0)
    parts = [own]
    for shift in range(1, count):
        target = (place + shift) % count
        block = lax.dynamic_slice_in_dim(payload, target * rows, rows, 0)
        pairs = [(i, (i + shift) % count) for i in range(count)]
        parts.append(lax.ppermute(block, axis, pairs))
    return jnp.stack(parts)


def column_sum(partial, axis):
    count = lax.axis_size(axis)
    place = lax.axis_index(axis)
    width = partial.shape[1] // count
    own = lax.dynamic_slice_in_dim(partial, place * width, width, 1)
    total = own.astype(jnp.float32)
    for shift in range(1, count):
        target = (place + shift) % count
        block = lax.dynamic_slice_in_dim(partial, target * width, width, 1)
        pairs = [(i, (i + shift) % count) for i in range(count)]
        total = total + lax.ppermute(block, axis, pairs).astype(jnp.float32)
    return total.astype(jnp.bfloat16)


def paired_column_sum(partial, axis):
    count = lax.axis_size(axis)
    if count % 2 != 0:
        return column_sum(partial, axis)
    chips = count // 2
    place = lax.axis_index(axis)
    core = place % 2
    chip = place // 2
    rows = partial.shape[0]
    width = partial.shape[1] // count
    grid = partial.reshape(rows, chips, 2, width)
    mine = lax.dynamic_index_in_dim(grid, core, axis=2, keepdims=False)
    theirs = lax.dynamic_index_in_dim(grid, 1 - core, axis=2, keepdims=False)
    swapped = lax.ppermute(theirs, axis, [(i, i ^ 1) for i in range(count)])
    chip_sum = mine.astype(jnp.float32) + swapped.astype(jnp.float32)
    total = lax.dynamic_index_in_dim(chip_sum, chip, axis=1, keepdims=False)
    for shift in range(1, chips):
        target = (chip + shift) % chips
        block = lax.dynamic_index_in_dim(chip_sum, target, axis=1, keepdims=False)
        pairs = [(2 * c + k, 2 * ((c + shift) % chips) + k) for c in range(chips) for k in range(2)]
        total = total + lax.ppermute(block.astype(jnp.bfloat16), axis, pairs).astype(jnp.float32)
    return total.astype(jnp.bfloat16)


def per_device(
    frames, latents, lengths, w_query, w_key, w_value, w_out, w_latent_query, w_latent_out
):
    frame_count = frames.shape[0]
    head_width = w_query.shape[1]
    heads_here = head_width // HD
    seq_devices = lax.axis_size("seq")
    seq_place = lax.axis_index("seq")
    first_frame = seq_place * frame_count
    length = lengths[0]
    query = project(frames, w_query)
    keyed = project(frames, w_key)
    valued = project(frames, w_value)
    low, high = halos(keyed, valued, "seq")
    chunks = 2 if frame_count % 512 == 0 else 1
    chunk_rows = frame_count // chunks
    frame_parts = []
    for c in range(chunks):
        terms = window_attention(
            query, keyed, valued, low, high, w_out, first_frame, length, c * chunk_rows, chunk_rows
        )
        frame_parts.append(paired_column_sum(terms, "head"))
    terms, keyed, valued = lax.optimization_barrier((terms, keyed, valued))
    frames_out = jnp.concatenate(frame_parts, axis=0)
    latent_count = latents.shape[0]
    latent_query = project(latents, w_latent_query)
    valid_count = jnp.clip(length - first_frame, 0, frame_count)
    peaks, totals, local_accum = latent_attention(latent_query, keyed, valued, valid_count)
    rows_here = latent_count // seq_devices
    payload = jnp.concatenate([local_accum, peaks, totals], axis=1)
    parts = shifted_blocks(payload, "seq", rows_here)
    part_accum = parts[:, :, :head_width]
    part_peak = parts[:, :, head_width : head_width + heads_here]
    part_total = parts[:, :, head_width + heads_here :]
    joint = jnp.max(part_peak, axis=0)
    factor = jnp.exp(part_peak - joint[None])
    own_total = jnp.sum(part_total * factor, axis=0)
    own_accum = jnp.sum(part_accum * jnp.repeat(factor, HD, axis=2), axis=0)
    summary = (own_accum / jnp.repeat(own_total, HD, axis=1)).astype(jnp.bfloat16)
    latent_terms = jnp.dot(summary, w_latent_out, preferred_element_type=jnp.float32)
    latents_out = column_sum(latent_terms.astype(jnp.bfloat16), "head")
    return (frames_out, latents_out)


def solution(mesh):
    return jax.shard_map(
        per_device,
        mesh=mesh,
        in_specs=(
            P(("groups", "seq"), None),
            P(),
            P("groups"),
            P(None, "head"),
            P(None, "head"),
            P(None, "head"),
            P("head", None),
            P(None, "head"),
            P("head", None),
        ),
        out_specs=(P(("groups", "seq"), "head"), P(("groups", "seq"), "head")),
        check_vma=False,
    )
```

```python
import functools

import jax
import jax.numpy as jnp
from jax import lax
from jax.experimental import pallas as pl
from jax.experimental.pallas import tpu as pltpu
from jax.sharding import PartitionSpec as P

HD = 64
HALF = 256
NEG = -1e30


def halos(keyed, valued, axis):
    count = lax.axis_size(axis)
    forward = [(i, i + 1) for i in range(count - 1)]
    backward = [(target, source) for source, target in forward]
    tail = jnp.concatenate([keyed[-HALF:], valued[-HALF:]], axis=1)
    head = jnp.concatenate([keyed[:HALF], valued[:HALF]], axis=1)
    return lax.ppermute(tail, axis, forward), lax.ppermute(head, axis, backward)


def project(source, weight):
    return jnp.dot(source, weight, preferred_element_type=jnp.float32).astype(jnp.bfloat16)


def window_kernel(
    scal_ref, q_ref, k_ref, v_ref, low_ref, high_ref, w_ref, o_ref, kbuf, vbuf, att_ref, *,
    heads, scale
):
    tq = q_ref.shape[0]
    frame_count, width = k_ref.shape
    span = tq + 2 * HALF

    @pl.when(pl.program_id(0) == 0)
    def _fill():
        kbuf[0:HALF, :] = low_ref[:, 0:width]
        vbuf[0:HALF, :] = low_ref[:, width : 2 * width]
        kbuf[HALF : HALF + frame_count, :] = k_ref[...]
        vbuf[HALF : HALF + frame_count, :] = v_ref[...]
        kbuf[HALF + frame_count :, :] = high_ref[:, 0:width]
        vbuf[HALF + frame_count :, :] = high_ref[:, width : 2 * width]

    start = pl.multiple_of(scal_ref[2] + pl.program_id(0) * tq, tq)
    first = scal_ref[0]
    length = scal_ref[1]
    row = lax.broadcasted_iota(jnp.int32, (tq, span), 0)
    col = lax.broadcasted_iota(jnp.int32, (tq, span), 1)
    offset = col - row
    key_pos = first + start - HALF + col
    allowed = (offset >= 0) & (offset <= 2 * HALF) & (key_pos >= 0) & (key_pos < length)
    query_pos = first + start + lax.broadcasted_iota(jnp.int32, (tq, 1), 0)
    query_valid = query_pos < length
    for h in range(heads):
        cols = slice(h * HD, (h + 1) * HD)
        q = q_ref[:, cols]
        k = kbuf[pl.ds(start, span), cols]
        v = vbuf[pl.ds(start, span), cols]
        s = lax.dot_general(
            q, k, (((1,), (1,)), ((), ())), preferred_element_type=jnp.float32
        ) * scale
        masked = jnp.where(allowed, s, NEG)
        peak = jnp.max(masked, axis=1, keepdims=True)
        weights = jnp.where(allowed, jnp.exp(masked - peak), 0.0)
        denom = jnp.sum(weights, axis=1, keepdims=True)
        blended = jnp.dot(weights.astype(jnp.bfloat16), v, preferred_element_type=jnp.float32)
        divisor = jnp.where(query_valid, denom, 1.0)
        att_ref[:, cols] = jnp.where(query_valid, blended / divisor, 0.0).astype(jnp.bfloat16)
    result = jnp.dot(att_ref[...], w_ref[...], preferred_element_type=jnp.float32)
    block_width = o_ref.shape[2]
    for b in range(o_ref.shape[0]):
        o_ref[b] = result[:, b * block_width : (b + 1) * block_width].astype(jnp.bfloat16)


def window_attention(
    query, keyed, valued, low, high, w_out, first_frame, length, row_base, rows, blocks
):
    frame_count, width = query.shape
    out_width = w_out.shape[1]
    block_width = out_width // blocks
    tq = min(256, rows)
    block_base = row_base // tq
    span = tq + 2 * HALF
    scal = jnp.array([0, 0, row_base], jnp.int32).at[0].set(first_frame).at[1].set(length)
    kernel = functools.partial(window_kernel, heads=width // HD, scale=HD ** (-0.5))
    cost = pl.CostEstimate(
        flops=4 * rows * span * width + 2 * rows * width * out_width,
        transcendentals=rows * span * (width // HD),
        bytes_accessed=2 * (2 * query.size + rows * width + 2 * low.size + w_out.size + rows * out_width),
    )
    full = lambda i, s: (0, 0)
    return pl.pallas_call(
        kernel,
        cost_estimate=cost,
        out_shape=jax.ShapeDtypeStruct((blocks, rows, block_width), jnp.bfloat16),
        grid_spec=pltpu.PrefetchScalarGridSpec(
            num_scalar_prefetch=1,
            grid=(rows // tq,),
            in_specs=[
                pl.BlockSpec((tq, width), lambda i, s: (i + block_base, 0)),
                pl.BlockSpec(keyed.shape, full),
                pl.BlockSpec(valued.shape, full),
                pl.BlockSpec(low.shape, full),
                pl.BlockSpec(high.shape, full),
                pl.BlockSpec(w_out.shape, full),
            ],
            out_specs=pl.BlockSpec((blocks, tq, block_width), lambda i, s: (0, i, 0)),
            scratch_shapes=[
                pltpu.VMEM((frame_count + 2 * HALF, width), jnp.bfloat16),
                pltpu.VMEM((frame_count + 2 * HALF, width), jnp.bfloat16),
                pltpu.VMEM((tq, width), jnp.bfloat16),
            ],
        ),
        compiler_params=pltpu.CompilerParams(dimension_semantics=("arbitrary",)),
    )(scal, query, keyed, valued, low, high, w_out)


def latent_kernel(scal_ref, q_ref, k_ref, v_ref, acc_ref, stat_ref, *, heads, scale):
    tl = q_ref.shape[0]
    frame_count = k_ref.shape[0]
    valid = lax.broadcasted_iota(jnp.int32, (tl, frame_count), 1) < scal_ref[0]
    stat_ref[...] = jnp.zeros_like(stat_ref)
    for h in range(heads):
        cols = slice(h * HD, (h + 1) * HD)
        s = lax.dot_general(
            q_ref[:, cols], k_ref[:, cols], (((1,), (1,)), ((), ())),
            preferred_element_type=jnp.float32,
        ) * scale
        masked = jnp.where(valid, s, NEG)
        peak = jnp.max(masked, axis=1, keepdims=True)
        weights = jnp.where(valid, jnp.exp(masked - peak), 0.0)
        total = jnp.sum(weights, axis=1, keepdims=True)
        acc_ref[:, cols] = jnp.dot(
            weights.astype(jnp.bfloat16), v_ref[:, cols], preferred_element_type=jnp.float32
        )
        stat_ref[:, h : h + 1] = peak
        stat_ref[:, heads + h : heads + h + 1] = total


def latent_attention(latent_query, keyed, valued, valid_count):
    latent_count, width = latent_query.shape
    heads = width // HD
    tl = min(256, latent_count)
    scal = jnp.reshape(valid_count, (1,)).astype(jnp.int32)
    kernel = functools.partial(latent_kernel, heads=heads, scale=HD ** (-0.5))
    frame_count = keyed.shape[0]
    cost = pl.CostEstimate(
        flops=4 * latent_count * frame_count * width,
        transcendentals=latent_count * frame_count * heads,
        bytes_accessed=2 * (latent_query.size + 2 * keyed.size) + 4 * latent_count * (width + 128),
    )
    acc, stat = pl.pallas_call(
        kernel,
        cost_estimate=cost,
        out_shape=(
            jax.ShapeDtypeStruct((latent_count, width), jnp.float32),
            jax.ShapeDtypeStruct((latent_count, 128), jnp.float32),
        ),
        grid_spec=pltpu.PrefetchScalarGridSpec(
            num_scalar_prefetch=1,
            grid=(latent_count // tl,),
            in_specs=[
                pl.BlockSpec((tl, width), lambda i, s: (i, 0)),
                pl.BlockSpec(keyed.shape, lambda i, s: (0, 0)),
                pl.BlockSpec(valued.shape, lambda i, s: (0, 0)),
            ],
            out_specs=[
                pl.BlockSpec((tl, width), lambda i, s: (i, 0)),
                pl.BlockSpec((tl, 128), lambda i, s: (i, 0)),
            ],
        ),
    )(scal, latent_query, keyed, valued)
    return stat[:, :heads], stat[:, heads : 2 * heads], acc


def shifted_blocks(payload, axis, rows):
    count = lax.axis_size(axis)
    place = lax.axis_index(axis)
    own = lax.dynamic_slice_in_dim(payload, place * rows, rows, 0)
    parts = [own]
    for shift in range(1, count):
        target = (place + shift) % count
        block = lax.dynamic_slice_in_dim(payload, target * rows, rows, 0)
        pairs = [(i, (i + shift) % count) for i in range(count)]
        parts.append(lax.ppermute(block, axis, pairs))
    return jnp.stack(parts)


def column_sum(partial, axis):
    count = lax.axis_size(axis)
    place = lax.axis_index(axis)
    width = partial.shape[1] // count
    own = lax.dynamic_slice_in_dim(partial, place * width, width, 1)
    total = own.astype(jnp.float32)
    for shift in range(1, count):
        target = (place + shift) % count
        block = lax.dynamic_slice_in_dim(partial, target * width, width, 1)
        pairs = [(i, (i + shift) % count) for i in range(count)]
        total = total + lax.ppermute(block, axis, pairs).astype(jnp.float32)
    return total.astype(jnp.bfloat16)


def send_order(axis):
    count = lax.axis_size(axis)
    place = lax.axis_index(axis)
    if count % 2 != 0:
        return [(place + j) % count for j in range(count)]
    chips = count // 2
    core = place % 2
    chip = place // 2
    theirs = [2 * ((chip + d) % chips) + 1 - core for d in range(chips)]
    mine = [2 * ((chip + d) % chips) + core for d in range(chips)]
    return theirs + mine


def ordered_columns(weight, axis):
    count = lax.axis_size(axis)
    width = weight.shape[1] // count
    return jnp.concatenate(
        [lax.dynamic_slice_in_dim(weight, b * width, width, 1) for b in send_order(axis)], axis=1
    )


def paired_block_sum(blocks, axis):
    count = lax.axis_size(axis)
    if count % 2 != 0:
        total = blocks[0].astype(jnp.float32)
        for shift in range(1, count):
            pairs = [(i, (i + shift) % count) for i in range(count)]
            total = total + lax.ppermute(blocks[shift], axis, pairs).astype(jnp.float32)
        return total.astype(jnp.bfloat16)
    chips = count // 2
    swap = [(i, i ^ 1) for i in range(count)]
    chip_sums = [
        blocks[chips + d].astype(jnp.float32)
        + lax.ppermute(blocks[d], axis, swap).astype(jnp.float32)
        for d in range(chips)
    ]
    total = chip_sums[0]
    for d in range(1, chips):
        pairs = [(2 * c + k, 2 * ((c + d) % chips) + k) for c in range(chips) for k in range(2)]
        total = total + lax.ppermute(chip_sums[d].astype(jnp.bfloat16), axis, pairs).astype(
            jnp.float32
        )
    return total.astype(jnp.bfloat16)


def per_device(
    frames, latents, lengths, w_query, w_key, w_value, w_out, w_latent_query, w_latent_out
):
    frame_count = frames.shape[0]
    head_width = w_query.shape[1]
    heads_here = head_width // HD
    seq_devices = lax.axis_size("seq")
    seq_place = lax.axis_index("seq")
    first_frame = seq_place * frame_count
    length = lengths[0]
    query = project(frames, w_query)
    keyed = project(frames, w_key)
    valued = project(frames, w_value)
    low, high = halos(keyed, valued, "seq")
    chunks = 2 if frame_count % 512 == 0 else 1
    chunk_rows = frame_count // chunks
    head_devices = lax.axis_size("head")
    w_ordered = ordered_columns(w_out, "head")
    frame_parts = []
    for c in range(chunks):
        terms = window_attention(
            query, keyed, valued, low, high, w_ordered, first_frame, length,
            c * chunk_rows, chunk_rows, head_devices,
        )
        frame_parts.append(paired_block_sum(terms, "head"))
    terms, keyed, valued = lax.optimization_barrier((terms, keyed, valued))
    frames_out = jnp.concatenate(frame_parts, axis=0)
    latent_count = latents.shape[0]
    latent_query = project(latents, w_latent_query)
    valid_count = jnp.clip(length - first_frame, 0, frame_count)
    peaks, totals, local_accum = latent_attention(latent_query, keyed, valued, valid_count)
    rows_here = latent_count // seq_devices
    payload = jnp.concatenate([local_accum, peaks, totals], axis=1)
    parts = shifted_blocks(payload, "seq", rows_here)
    part_accum = parts[:, :, :head_width]
    part_peak = parts[:, :, head_width : head_width + heads_here]
    part_total = parts[:, :, head_width + heads_here :]
    joint = jnp.max(part_peak, axis=0)
    factor = jnp.exp(part_peak - joint[None])
    own_total = jnp.sum(part_total * factor, axis=0)
    own_accum = jnp.sum(part_accum * jnp.repeat(factor, HD, axis=2), axis=0)
    summary = (own_accum / jnp.repeat(own_total, HD, axis=1)).astype(jnp.bfloat16)
    latent_terms = jnp.dot(summary, w_latent_out, preferred_element_type=jnp.float32)
    latents_out = column_sum(latent_terms.astype(jnp.bfloat16), "head")
    return (frames_out, latents_out)


def solution(mesh):
    return jax.shard_map(
        per_device,
        mesh=mesh,
        in_specs=(
            P(("groups", "seq"), None),
            P(),
            P("groups"),
            P(None, "head"),
            P(None, "head"),
            P(None, "head"),
            P("head", None),
            P(None, "head"),
            P("head", None),
        ),
        out_specs=(P(("groups", "seq"), "head"), P(("groups", "seq"), "head")),
        check_vma=False,
    )
```

```python
import functools

import jax
import jax.numpy as jnp
from jax import lax
from jax.experimental import pallas as pl
from jax.experimental.pallas import tpu as pltpu
from jax.sharding import PartitionSpec as P

HD = 64
HALF = 256
NEG = -1e30


def halos(keyed, valued, axis):
    count = lax.axis_size(axis)
    forward = [(i, i + 1) for i in range(count - 1)]
    backward = [(target, source) for source, target in forward]
    tail = jnp.concatenate([keyed[-HALF:], valued[-HALF:]], axis=1)
    head = jnp.concatenate([keyed[:HALF], valued[:HALF]], axis=1)
    return lax.ppermute(tail, axis, forward), lax.ppermute(head, axis, backward)


def project(source, weight):
    return jnp.dot(source, weight, preferred_element_type=jnp.float32).astype(jnp.bfloat16)


def window_kernel(
    scal_ref, q_ref, k_ref, v_ref, low_ref, high_ref, w_ref, o_ref, kbuf, vbuf, att_ref, *,
    heads, scale
):
    tq = q_ref.shape[0]
    frame_count, width = k_ref.shape
    span = tq + 2 * HALF

    @pl.when(pl.program_id(0) == 0)
    def _fill():
        kbuf[0:HALF, :] = low_ref[:, 0:width]
        vbuf[0:HALF, :] = low_ref[:, width : 2 * width]
        kbuf[HALF : HALF + frame_count, :] = k_ref[...]
        vbuf[HALF : HALF + frame_count, :] = v_ref[...]
        kbuf[HALF + frame_count :, :] = high_ref[:, 0:width]
        vbuf[HALF + frame_count :, :] = high_ref[:, width : 2 * width]

    start = pl.multiple_of(scal_ref[2] + pl.program_id(0) * tq, tq)
    first = scal_ref[0]
    length = scal_ref[1]
    row = lax.broadcasted_iota(jnp.int32, (tq, span), 0)
    col = lax.broadcasted_iota(jnp.int32, (tq, span), 1)
    offset = col - row
    key_pos = first + start - HALF + col
    allowed = (offset >= 0) & (offset <= 2 * HALF) & (key_pos >= 0) & (key_pos < length)
    query_pos = first + start + lax.broadcasted_iota(jnp.int32, (tq, 1), 0)
    query_valid = query_pos < length
    for h in range(heads):
        cols = slice(h * HD, (h + 1) * HD)
        q = q_ref[:, cols]
        k = kbuf[pl.ds(start, span), cols]
        v = vbuf[pl.ds(start, span), cols]
        s = lax.dot_general(
            q, k, (((1,), (1,)), ((), ())), preferred_element_type=jnp.float32
        ) * scale
        masked = jnp.where(allowed, s, NEG)
        peak = jnp.max(masked, axis=1, keepdims=True)
        weights = jnp.where(allowed, jnp.exp(masked - peak), 0.0)
        denom = jnp.sum(weights, axis=1, keepdims=True)
        blended = jnp.dot(weights.astype(jnp.bfloat16), v, preferred_element_type=jnp.float32)
        divisor = jnp.where(query_valid, denom, 1.0)
        att_ref[:, cols] = jnp.where(query_valid, blended / divisor, 0.0).astype(jnp.bfloat16)
    result = jnp.dot(att_ref[...], w_ref[...], preferred_element_type=jnp.float32)
    block_width = o_ref.shape[2]
    for b in range(o_ref.shape[0]):
        o_ref[b] = result[:, b * block_width : (b + 1) * block_width].astype(jnp.bfloat16)


def window_attention(
    query, keyed, valued, low, high, w_out, first_frame, length, row_base, rows, blocks
):
    frame_count, width = query.shape
    out_width = w_out.shape[1]
    block_width = out_width // blocks
    tq = min(256, rows)
    block_base = row_base // tq
    span = tq + 2 * HALF
    scal = jnp.array([0, 0, row_base], jnp.int32).at[0].set(first_frame).at[1].set(length)
    kernel = functools.partial(window_kernel, heads=width // HD, scale=HD ** (-0.5))
    cost = pl.CostEstimate(
        flops=4 * rows * span * width + 2 * rows * width * out_width,
        transcendentals=rows * span * (width // HD),
        bytes_accessed=2 * (2 * query.size + rows * width + 2 * low.size + w_out.size + rows * out_width),
    )
    full = lambda i, s: (0, 0)
    return pl.pallas_call(
        kernel,
        cost_estimate=cost,
        out_shape=jax.ShapeDtypeStruct((blocks, rows, block_width), jnp.bfloat16),
        grid_spec=pltpu.PrefetchScalarGridSpec(
            num_scalar_prefetch=1,
            grid=(rows // tq,),
            in_specs=[
                pl.BlockSpec((tq, width), lambda i, s: (i + block_base, 0)),
                pl.BlockSpec(keyed.shape, full),
                pl.BlockSpec(valued.shape, full),
                pl.BlockSpec(low.shape, full),
                pl.BlockSpec(high.shape, full),
                pl.BlockSpec(w_out.shape, full),
            ],
            out_specs=pl.BlockSpec((blocks, tq, block_width), lambda i, s: (0, i, 0)),
            scratch_shapes=[
                pltpu.VMEM((frame_count + 2 * HALF, width), jnp.bfloat16),
                pltpu.VMEM((frame_count + 2 * HALF, width), jnp.bfloat16),
                pltpu.VMEM((tq, width), jnp.bfloat16),
            ],
        ),
        compiler_params=pltpu.CompilerParams(dimension_semantics=("arbitrary",)),
    )(scal, query, keyed, valued, low, high, w_out)


def latent_kernel(scal_ref, q_ref, k_ref, v_ref, acc_ref, stat_ref, *, heads, scale):
    tl = q_ref.shape[0]
    frame_count = k_ref.shape[0]
    valid = lax.broadcasted_iota(jnp.int32, (tl, frame_count), 1) < scal_ref[0]
    stat_ref[...] = jnp.zeros_like(stat_ref)
    for h in range(heads):
        cols = slice(h * HD, (h + 1) * HD)
        s = lax.dot_general(
            q_ref[:, cols], k_ref[:, cols], (((1,), (1,)), ((), ())),
            preferred_element_type=jnp.float32,
        ) * scale
        masked = jnp.where(valid, s, NEG)
        peak = jnp.max(masked, axis=1, keepdims=True)
        weights = jnp.where(valid, jnp.exp(masked - peak), 0.0)
        total = jnp.sum(weights, axis=1, keepdims=True)
        acc_ref[:, cols] = jnp.dot(
            weights.astype(jnp.bfloat16), v_ref[:, cols], preferred_element_type=jnp.float32
        )
        stat_ref[:, h : h + 1] = peak
        stat_ref[:, heads + h : heads + h + 1] = total


def latent_attention(latent_query, keyed, valued, valid_count):
    latent_count, width = latent_query.shape
    heads = width // HD
    tl = min(256, latent_count)
    scal = jnp.reshape(valid_count, (1,)).astype(jnp.int32)
    kernel = functools.partial(latent_kernel, heads=heads, scale=HD ** (-0.5))
    frame_count = keyed.shape[0]
    cost = pl.CostEstimate(
        flops=4 * latent_count * frame_count * width,
        transcendentals=latent_count * frame_count * heads,
        bytes_accessed=2 * (latent_query.size + 2 * keyed.size) + 4 * latent_count * (width + 128),
    )
    acc, stat = pl.pallas_call(
        kernel,
        cost_estimate=cost,
        out_shape=(
            jax.ShapeDtypeStruct((latent_count, width), jnp.float32),
            jax.ShapeDtypeStruct((latent_count, 128), jnp.float32),
        ),
        grid_spec=pltpu.PrefetchScalarGridSpec(
            num_scalar_prefetch=1,
            grid=(latent_count // tl,),
            in_specs=[
                pl.BlockSpec((tl, width), lambda i, s: (i, 0)),
                pl.BlockSpec(keyed.shape, lambda i, s: (0, 0)),
                pl.BlockSpec(valued.shape, lambda i, s: (0, 0)),
            ],
            out_specs=[
                pl.BlockSpec((tl, width), lambda i, s: (i, 0)),
                pl.BlockSpec((tl, 128), lambda i, s: (i, 0)),
            ],
        ),
    )(scal, latent_query, keyed, valued)
    return stat[:, :heads], stat[:, heads : 2 * heads], acc


def shifted_blocks(payload, axis, rows):
    count = lax.axis_size(axis)
    place = lax.axis_index(axis)
    own = lax.dynamic_slice_in_dim(payload, place * rows, rows, 0)
    parts = [own]
    for shift in range(1, count):
        target = (place + shift) % count
        block = lax.dynamic_slice_in_dim(payload, target * rows, rows, 0)
        pairs = [(i, (i + shift) % count) for i in range(count)]
        parts.append(lax.ppermute(block, axis, pairs))
    return jnp.stack(parts)


def column_sum(partial, axis):
    count = lax.axis_size(axis)
    place = lax.axis_index(axis)
    width = partial.shape[1] // count
    own = lax.dynamic_slice_in_dim(partial, place * width, width, 1)
    total = own.astype(jnp.float32)
    for shift in range(1, count):
        target = (place + shift) % count
        block = lax.dynamic_slice_in_dim(partial, target * width, width, 1)
        pairs = [(i, (i + shift) % count) for i in range(count)]
        total = total + lax.ppermute(block, axis, pairs).astype(jnp.float32)
    return total.astype(jnp.bfloat16)


def send_order(axis):
    count = lax.axis_size(axis)
    place = lax.axis_index(axis)
    if count % 2 != 0:
        return [(place + j) % count for j in range(count)]
    chips = count // 2
    core = place % 2
    chip = place // 2
    theirs = [2 * ((chip + d) % chips) + 1 - core for d in range(chips)]
    mine = [2 * ((chip + d) % chips) + core for d in range(chips)]
    return theirs + mine


def ordered_columns(weight, axis):
    count = lax.axis_size(axis)
    width = weight.shape[1] // count
    return jnp.concatenate(
        [lax.dynamic_slice_in_dim(weight, b * width, width, 1) for b in send_order(axis)], axis=1
    )


def chip_pair_sums(blocks, axis):
    count = lax.axis_size(axis)
    chips = count // 2
    swap = [(i, i ^ 1) for i in range(count)]
    return [
        (
            blocks[chips + d].astype(jnp.float32)
            + lax.ppermute(blocks[d], axis, swap).astype(jnp.float32)
        ).astype(jnp.bfloat16)
        for d in range(chips)
    ]


def cross_chip_sum(chip_sums, axis):
    count = lax.axis_size(axis)
    chips = count // 2
    total = chip_sums[0].astype(jnp.float32)
    for d in range(1, chips):
        pairs = [(2 * c + k, 2 * ((c + d) % chips) + k) for c in range(chips) for k in range(2)]
        total = total + lax.ppermute(chip_sums[d], axis, pairs).astype(jnp.float32)
    return total.astype(jnp.bfloat16)


def plain_block_sum(blocks, axis):
    count = lax.axis_size(axis)
    total = blocks[0].astype(jnp.float32)
    for shift in range(1, count):
        pairs = [(i, (i + shift) % count) for i in range(count)]
        total = total + lax.ppermute(blocks[shift], axis, pairs).astype(jnp.float32)
    return total.astype(jnp.bfloat16)


def exchange_rows(accum, stats, axis, rows):
    count = lax.axis_size(axis)
    place = lax.axis_index(axis)
    accs = [lax.dynamic_slice_in_dim(accum, place * rows, rows, 0)]
    stat_parts = [lax.dynamic_slice_in_dim(stats, place * rows, rows, 1)]
    for shift in range(1, count):
        target = (place + shift) % count
        pairs = [(i, (i + shift) % count) for i in range(count)]
        accs.append(
            lax.ppermute(lax.dynamic_slice_in_dim(accum, target * rows, rows, 0), axis, pairs)
        )
        stat_parts.append(
            lax.ppermute(lax.dynamic_slice_in_dim(stats, target * rows, rows, 1), axis, pairs)
        )
    return jnp.stack(accs).astype(jnp.float32), jnp.stack(stat_parts)


def per_device(
    frames, latents, lengths, w_query, w_key, w_value, w_out, w_latent_query, w_latent_out
):
    frame_count = frames.shape[0]
    head_width = w_query.shape[1]
    heads_here = head_width // HD
    seq_devices = lax.axis_size("seq")
    seq_place = lax.axis_index("seq")
    first_frame = seq_place * frame_count
    length = lengths[0]
    query = project(frames, w_query)
    keyed = project(frames, w_key)
    valued = project(frames, w_value)
    low, high = halos(keyed, valued, "seq")
    chunks = 2 if frame_count % 512 == 0 else 1
    chunk_rows = frame_count // chunks
    head_devices = lax.axis_size("head")
    paired = head_devices % 2 == 0
    w_ordered = ordered_columns(w_out, "head")
    parts = [
        window_attention(
            query, keyed, valued, low, high, w_ordered, first_frame, length,
            c * chunk_rows, chunk_rows, head_devices,
        )
        for c in range(chunks)
    ]
    latent_count = latents.shape[0]
    latent_query = project(latents, w_latent_query)
    valid_count = jnp.clip(length - first_frame, 0, frame_count)
    frame_parts = []
    if paired:
        first_sums = chip_pair_sums(parts[0], "head")
        first_sums, rest, keyed, valued = lax.optimization_barrier(
            (first_sums, parts[1:], keyed, valued)
        )
        frame_parts.append(cross_chip_sum(first_sums, "head"))
        rest_sums = [chip_pair_sums(blocks, "head") for blocks in rest]
    else:
        frame_parts = [plain_block_sum(blocks, "head") for blocks in parts]
    peaks, totals, local_accum = latent_attention(latent_query, keyed, valued, valid_count)
    stats = jnp.concatenate([peaks, totals], axis=1).T
    local_accum = local_accum.astype(jnp.bfloat16)
    if paired:
        rest_sums, local_accum, stats = lax.optimization_barrier((rest_sums, local_accum, stats))
        frame_parts.extend(cross_chip_sum(sums, "head") for sums in rest_sums)
    frames_out = jnp.concatenate(frame_parts, axis=0)
    rows_here = latent_count // seq_devices
    part_accum, part_stats = exchange_rows(local_accum, stats, "seq", rows_here)
    part_peak = part_stats[:, :heads_here, :]
    part_total = part_stats[:, heads_here:, :]
    joint = jnp.max(part_peak, axis=0)
    factor = jnp.exp(part_peak - joint[None])
    own_total = jnp.sum(part_total * factor, axis=0).T
    factor_rows = jnp.transpose(factor, (0, 2, 1))
    own_accum = jnp.sum(part_accum * jnp.repeat(factor_rows, HD, axis=2), axis=0)
    summary = (own_accum / jnp.repeat(own_total, HD, axis=1)).astype(jnp.bfloat16)
    latent_terms = jnp.dot(summary, w_latent_out, preferred_element_type=jnp.float32)
    latents_out = column_sum(latent_terms.astype(jnp.bfloat16), "head")
    return (frames_out, latents_out)


def solution(mesh):
    return jax.shard_map(
        per_device,
        mesh=mesh,
        in_specs=(
            P(("groups", "seq"), None),
            P(),
            P("groups"),
            P(None, "head"),
            P(None, "head"),
            P(None, "head"),
            P("head", None),
            P(None, "head"),
            P("head", None),
        ),
        out_specs=(P(("groups", "seq"), "head"), P(("groups", "seq"), "head")),
        check_vma=False,
    )
```

```python
import functools

import jax
import jax.numpy as jnp
from jax import lax
from jax.experimental import pallas as pl
from jax.experimental.pallas import tpu as pltpu
from jax.sharding import PartitionSpec as P

HD = 64
HALF = 256
NEG = -1e30


def halos(keyed, valued, axis):
    count = lax.axis_size(axis)
    forward = [(i, i + 1) for i in range(count - 1)]
    backward = [(target, source) for source, target in forward]
    tail = jnp.concatenate([keyed[-HALF:], valued[-HALF:]], axis=1)
    head = jnp.concatenate([keyed[:HALF], valued[:HALF]], axis=1)
    return lax.ppermute(tail, axis, forward), lax.ppermute(head, axis, backward)


def project(source, weight):
    return jnp.dot(source, weight, preferred_element_type=jnp.float32).astype(jnp.bfloat16)


def window_kernel(
    scal_ref, q_ref, k_ref, v_ref, low_ref, high_ref, w_ref, o_ref, kbuf, vbuf, att_ref, *,
    heads, scale
):
    tq = q_ref.shape[0]
    frame_count, width = k_ref.shape
    span = tq + 2 * HALF

    @pl.when(pl.program_id(0) == 0)
    def _fill():
        kbuf[0:HALF, :] = low_ref[:, 0:width]
        vbuf[0:HALF, :] = low_ref[:, width : 2 * width]
        kbuf[HALF : HALF + frame_count, :] = k_ref[...]
        vbuf[HALF : HALF + frame_count, :] = v_ref[...]
        kbuf[HALF + frame_count :, :] = high_ref[:, 0:width]
        vbuf[HALF + frame_count :, :] = high_ref[:, width : 2 * width]

    start = pl.multiple_of(scal_ref[2] + pl.program_id(0) * tq, tq)
    first = scal_ref[0]
    length = scal_ref[1]
    row = lax.broadcasted_iota(jnp.int32, (tq, span), 0)
    col = lax.broadcasted_iota(jnp.int32, (tq, span), 1)
    offset = col - row
    key_pos = first + start - HALF + col
    allowed = (offset >= 0) & (offset <= 2 * HALF) & (key_pos >= 0) & (key_pos < length)
    query_pos = first + start + lax.broadcasted_iota(jnp.int32, (tq, 1), 0)
    query_valid = query_pos < length
    for h in range(heads):
        cols = slice(h * HD, (h + 1) * HD)
        q = q_ref[:, cols]
        k = kbuf[pl.ds(start, span), cols]
        v = vbuf[pl.ds(start, span), cols]
        s = lax.dot_general(
            q, k, (((1,), (1,)), ((), ())), preferred_element_type=jnp.float32
        ) * scale
        masked = jnp.where(allowed, s, NEG)
        peak = jnp.max(masked, axis=1, keepdims=True)
        weights = jnp.where(allowed, jnp.exp(masked - peak), 0.0)
        denom = jnp.sum(weights, axis=1, keepdims=True)
        blended = jnp.dot(weights.astype(jnp.bfloat16), v, preferred_element_type=jnp.float32)
        divisor = jnp.where(query_valid, denom, 1.0)
        att_ref[:, cols] = jnp.where(query_valid, blended / divisor, 0.0).astype(jnp.bfloat16)
    result = jnp.dot(att_ref[...], w_ref[...], preferred_element_type=jnp.float32)
    block_width = o_ref.shape[2]
    for b in range(o_ref.shape[0]):
        o_ref[b] = result[:, b * block_width : (b + 1) * block_width].astype(jnp.bfloat16)


def window_attention(
    query, keyed, valued, low, high, w_out, first_frame, length, row_base, rows, blocks
):
    frame_count, width = query.shape
    out_width = w_out.shape[1]
    block_width = out_width // blocks
    tq = min(256, rows)
    block_base = row_base // tq
    span = tq + 2 * HALF
    scal = jnp.array([0, 0, row_base], jnp.int32).at[0].set(first_frame).at[1].set(length)
    kernel = functools.partial(window_kernel, heads=width // HD, scale=HD ** (-0.5))
    cost = pl.CostEstimate(
        flops=4 * rows * span * width + 2 * rows * width * out_width,
        transcendentals=rows * span * (width // HD),
        bytes_accessed=2 * (2 * query.size + rows * width + 2 * low.size + w_out.size + rows * out_width),
    )
    full = lambda i, s: (0, 0)
    return pl.pallas_call(
        kernel,
        cost_estimate=cost,
        out_shape=jax.ShapeDtypeStruct((blocks, rows, block_width), jnp.bfloat16),
        grid_spec=pltpu.PrefetchScalarGridSpec(
            num_scalar_prefetch=1,
            grid=(rows // tq,),
            in_specs=[
                pl.BlockSpec((tq, width), lambda i, s: (i + block_base, 0)),
                pl.BlockSpec(keyed.shape, full),
                pl.BlockSpec(valued.shape, full),
                pl.BlockSpec(low.shape, full),
                pl.BlockSpec(high.shape, full),
                pl.BlockSpec(w_out.shape, full),
            ],
            out_specs=pl.BlockSpec((blocks, tq, block_width), lambda i, s: (0, i, 0)),
            scratch_shapes=[
                pltpu.VMEM((frame_count + 2 * HALF, width), jnp.bfloat16),
                pltpu.VMEM((frame_count + 2 * HALF, width), jnp.bfloat16),
                pltpu.VMEM((tq, width), jnp.bfloat16),
            ],
        ),
        compiler_params=pltpu.CompilerParams(dimension_semantics=("arbitrary",)),
    )(scal, query, keyed, valued, low, high, w_out)


def latent_kernel(scal_ref, q_ref, k_ref, v_ref, acc_ref, stat_ref, *, heads, scale):
    tl = q_ref.shape[0]
    frame_count = k_ref.shape[0]
    valid = lax.broadcasted_iota(jnp.int32, (tl, frame_count), 1) < scal_ref[0]
    stat_ref[...] = jnp.zeros_like(stat_ref)
    for h in range(heads):
        cols = slice(h * HD, (h + 1) * HD)
        s = lax.dot_general(
            q_ref[:, cols], k_ref[:, cols], (((1,), (1,)), ((), ())),
            preferred_element_type=jnp.float32,
        ) * scale
        masked = jnp.where(valid, s, NEG)
        peak = jnp.max(masked, axis=1, keepdims=True)
        weights = jnp.where(valid, jnp.exp(masked - peak), 0.0)
        total = jnp.sum(weights, axis=1, keepdims=True)
        acc_ref[:, cols] = jnp.dot(
            weights.astype(jnp.bfloat16), v_ref[:, cols], preferred_element_type=jnp.float32
        )
        stat_ref[:, h : h + 1] = peak
        stat_ref[:, heads + h : heads + h + 1] = total


def latent_attention(latent_query, keyed, valued, valid_count):
    latent_count, width = latent_query.shape
    heads = width // HD
    tl = min(256, latent_count)
    scal = jnp.reshape(valid_count, (1,)).astype(jnp.int32)
    kernel = functools.partial(latent_kernel, heads=heads, scale=HD ** (-0.5))
    frame_count = keyed.shape[0]
    cost = pl.CostEstimate(
        flops=4 * latent_count * frame_count * width,
        transcendentals=latent_count * frame_count * heads,
        bytes_accessed=2 * (latent_query.size + 2 * keyed.size) + 4 * latent_count * (width + 128),
    )
    acc, stat = pl.pallas_call(
        kernel,
        cost_estimate=cost,
        out_shape=(
            jax.ShapeDtypeStruct((latent_count, width), jnp.float32),
            jax.ShapeDtypeStruct((latent_count, 128), jnp.float32),
        ),
        grid_spec=pltpu.PrefetchScalarGridSpec(
            num_scalar_prefetch=1,
            grid=(latent_count // tl,),
            in_specs=[
                pl.BlockSpec((tl, width), lambda i, s: (i, 0)),
                pl.BlockSpec(keyed.shape, lambda i, s: (0, 0)),
                pl.BlockSpec(valued.shape, lambda i, s: (0, 0)),
            ],
            out_specs=[
                pl.BlockSpec((tl, width), lambda i, s: (i, 0)),
                pl.BlockSpec((tl, 128), lambda i, s: (i, 0)),
            ],
        ),
    )(scal, latent_query, keyed, valued)
    return stat[:, :heads], stat[:, heads : 2 * heads], acc


def shifted_blocks(payload, axis, rows):
    count = lax.axis_size(axis)
    place = lax.axis_index(axis)
    own = lax.dynamic_slice_in_dim(payload, place * rows, rows, 0)
    parts = [own]
    for shift in range(1, count):
        target = (place + shift) % count
        block = lax.dynamic_slice_in_dim(payload, target * rows, rows, 0)
        pairs = [(i, (i + shift) % count) for i in range(count)]
        parts.append(lax.ppermute(block, axis, pairs))
    return jnp.stack(parts)


def column_sum(partial, axis):
    count = lax.axis_size(axis)
    place = lax.axis_index(axis)
    width = partial.shape[1] // count
    own = lax.dynamic_slice_in_dim(partial, place * width, width, 1)
    total = own.astype(jnp.float32)
    for shift in range(1, count):
        target = (place + shift) % count
        block = lax.dynamic_slice_in_dim(partial, target * width, width, 1)
        pairs = [(i, (i + shift) % count) for i in range(count)]
        total = total + lax.ppermute(block, axis, pairs).astype(jnp.float32)
    return total.astype(jnp.bfloat16)


def send_order(axis):
    count = lax.axis_size(axis)
    place = lax.axis_index(axis)
    if count % 2 != 0:
        return [(place + j) % count for j in range(count)]
    chips = count // 2
    core = place % 2
    chip = place // 2
    theirs = [2 * ((chip + d) % chips) + 1 - core for d in range(chips)]
    mine = [2 * ((chip + d) % chips) + core for d in range(chips)]
    return theirs + mine


def ordered_columns(weight, axis):
    count = lax.axis_size(axis)
    width = weight.shape[1] // count
    return jnp.concatenate(
        [lax.dynamic_slice_in_dim(weight, b * width, width, 1) for b in send_order(axis)], axis=1
    )


def chip_pair_sums(blocks, axis):
    count = lax.axis_size(axis)
    chips = count // 2
    swap = [(i, i ^ 1) for i in range(count)]
    return [
        (
            blocks[chips + d].astype(jnp.float32)
            + lax.ppermute(blocks[d], axis, swap).astype(jnp.float32)
        ).astype(jnp.bfloat16)
        for d in range(chips)
    ]


def cross_chip_sum(chip_sums, axis):
    count = lax.axis_size(axis)
    chips = count // 2
    total = chip_sums[0].astype(jnp.float32)
    for d in range(1, chips):
        pairs = [(2 * c + k, 2 * ((c + d) % chips) + k) for c in range(chips) for k in range(2)]
        total = total + lax.ppermute(chip_sums[d], axis, pairs).astype(jnp.float32)
    return total.astype(jnp.bfloat16)


def plain_block_sum(blocks, axis):
    count = lax.axis_size(axis)
    total = blocks[0].astype(jnp.float32)
    for shift in range(1, count):
        pairs = [(i, (i + shift) % count) for i in range(count)]
        total = total + lax.ppermute(blocks[shift], axis, pairs).astype(jnp.float32)
    return total.astype(jnp.bfloat16)


def exchange_rows(accum, stats, axis, rows):
    count = lax.axis_size(axis)
    place = lax.axis_index(axis)
    accs = [lax.dynamic_slice_in_dim(accum, place * rows, rows, 0)]
    stat_parts = [lax.dynamic_slice_in_dim(stats, place * rows, rows, 1)]
    for shift in range(1, count):
        target = (place + shift) % count
        pairs = [(i, (i + shift) % count) for i in range(count)]
        accs.append(
            lax.ppermute(lax.dynamic_slice_in_dim(accum, target * rows, rows, 0), axis, pairs)
        )
        stat_parts.append(
            lax.ppermute(lax.dynamic_slice_in_dim(stats, target * rows, rows, 1), axis, pairs)
        )
    return jnp.stack(accs).astype(jnp.float32), jnp.stack(stat_parts)


def per_device(
    frames, latents, lengths, w_query, w_key, w_value, w_out, w_latent_query, w_latent_out
):
    frame_count = frames.shape[0]
    head_width = w_query.shape[1]
    heads_here = head_width // HD
    seq_devices = lax.axis_size("seq")
    seq_place = lax.axis_index("seq")
    first_frame = seq_place * frame_count
    length = lengths[0]
    query = project(frames, w_query)
    keyed = project(frames, w_key)
    valued = project(frames, w_value)
    low, high = halos(keyed, valued, "seq")
    chunks = 2 if frame_count % 512 == 0 else 1
    chunk_rows = frame_count // chunks
    head_devices = lax.axis_size("head")
    paired = head_devices % 2 == 0
    w_ordered = ordered_columns(w_out, "head")
    latent_count = latents.shape[0]
    rows_here = latent_count // seq_devices
    latent_query = project(latents, w_latent_query)
    valid_count = jnp.clip(length - first_frame, 0, frame_count)
    peaks, totals, local_accum = latent_attention(latent_query, keyed, valued, valid_count)
    stats = jnp.concatenate([peaks, totals], axis=1).T
    local_accum = local_accum.astype(jnp.bfloat16)
    local_accum, stats, query, keyed, valued, low, high = lax.optimization_barrier(
        (local_accum, stats, query, keyed, valued, low, high)
    )
    part_accum, part_stats = exchange_rows(local_accum, stats, "seq", rows_here)
    parts = [
        window_attention(
            query, keyed, valued, low, high, w_ordered, first_frame, length,
            c * chunk_rows, chunk_rows, head_devices,
        )
        for c in range(chunks)
    ]
    if paired:
        first_sums = chip_pair_sums(parts[0], "head")
        first_sums, rest, part_accum, part_stats = lax.optimization_barrier(
            (first_sums, parts[1:], part_accum, part_stats)
        )
        frame_parts = [cross_chip_sum(first_sums, "head")]
        frame_parts.extend(
            cross_chip_sum(chip_pair_sums(blocks, "head"), "head") for blocks in rest
        )
    else:
        frame_parts = [plain_block_sum(blocks, "head") for blocks in parts]
    frames_out = jnp.concatenate(frame_parts, axis=0)
    part_peak = part_stats[:, :heads_here, :]
    part_total = part_stats[:, heads_here:, :]
    joint = jnp.max(part_peak, axis=0)
    factor = jnp.exp(part_peak - joint[None])
    own_total = jnp.sum(part_total * factor, axis=0).T
    factor_rows = jnp.transpose(factor, (0, 2, 1))
    own_accum = jnp.sum(part_accum * jnp.repeat(factor_rows, HD, axis=2), axis=0)
    summary = (own_accum / jnp.repeat(own_total, HD, axis=1)).astype(jnp.bfloat16)
    latent_terms = jnp.dot(summary, w_latent_out, preferred_element_type=jnp.float32)
    latents_out = column_sum(latent_terms.astype(jnp.bfloat16), "head")
    return (frames_out, latents_out)


def solution(mesh):
    return jax.shard_map(
        per_device,
        mesh=mesh,
        in_specs=(
            P(("groups", "seq"), None),
            P(),
            P("groups"),
            P(None, "head"),
            P(None, "head"),
            P(None, "head"),
            P("head", None),
            P(None, "head"),
            P("head", None),
        ),
        out_specs=(P(("groups", "seq"), "head"), P(("groups", "seq"), "head")),
        check_vma=False,
    )
```

```python
import functools

import jax
import jax.numpy as jnp
from jax import lax
from jax.experimental import pallas as pl
from jax.experimental.pallas import tpu as pltpu
from jax.sharding import PartitionSpec as P

HD = 64
HALF = 256
NEG = -1e30


def halos(keyed, valued, axis):
    count = lax.axis_size(axis)
    forward = [(i, i + 1) for i in range(count - 1)]
    backward = [(target, source) for source, target in forward]
    tail = jnp.concatenate([keyed[-HALF:], valued[-HALF:]], axis=1)
    head = jnp.concatenate([keyed[:HALF], valued[:HALF]], axis=1)
    return lax.ppermute(tail, axis, forward), lax.ppermute(head, axis, backward)


def project(source, weight):
    return jnp.dot(source, weight, preferred_element_type=jnp.float32).astype(jnp.bfloat16)


def window_kernel(
    scal_ref, q_ref, k_ref, v_ref, low_ref, high_ref, w_ref, o_ref, kbuf, vbuf, att_ref, *,
    heads, scale
):
    tq = q_ref.shape[0]
    frame_count, width = k_ref.shape
    span = tq + 2 * HALF

    @pl.when(pl.program_id(0) == 0)
    def _fill():
        kbuf[0:HALF, :] = low_ref[:, 0:width]
        vbuf[0:HALF, :] = low_ref[:, width : 2 * width]
        kbuf[HALF : HALF + frame_count, :] = k_ref[...]
        vbuf[HALF : HALF + frame_count, :] = v_ref[...]
        kbuf[HALF + frame_count :, :] = high_ref[:, 0:width]
        vbuf[HALF + frame_count :, :] = high_ref[:, width : 2 * width]

    start = pl.multiple_of(scal_ref[2] + pl.program_id(0) * tq, tq)
    first = scal_ref[0]
    length = scal_ref[1]
    row = lax.broadcasted_iota(jnp.int32, (tq, span), 0)
    col = lax.broadcasted_iota(jnp.int32, (tq, span), 1)
    offset = col - row
    key_pos = first + start - HALF + col
    allowed = (offset >= 0) & (offset <= 2 * HALF) & (key_pos >= 0) & (key_pos < length)
    query_pos = first + start + lax.broadcasted_iota(jnp.int32, (tq, 1), 0)
    query_valid = query_pos < length
    for h in range(heads):
        cols = slice(h * HD, (h + 1) * HD)
        q = q_ref[:, cols]
        k = kbuf[pl.ds(start, span), cols]
        v = vbuf[pl.ds(start, span), cols]
        s = lax.dot_general(
            q, k, (((1,), (1,)), ((), ())), preferred_element_type=jnp.float32
        ) * scale
        masked = jnp.where(allowed, s, NEG)
        peak = jnp.max(masked, axis=1, keepdims=True)
        weights = jnp.where(allowed, jnp.exp(masked - peak), 0.0)
        denom = jnp.sum(weights, axis=1, keepdims=True)
        blended = jnp.dot(weights.astype(jnp.bfloat16), v, preferred_element_type=jnp.float32)
        divisor = jnp.where(query_valid, denom, 1.0)
        att_ref[:, cols] = jnp.where(query_valid, blended / divisor, 0.0).astype(jnp.bfloat16)
    result = jnp.dot(att_ref[...], w_ref[...], preferred_element_type=jnp.float32)
    block_width = o_ref.shape[2]
    for b in range(o_ref.shape[0]):
        o_ref[b] = result[:, b * block_width : (b + 1) * block_width].astype(jnp.bfloat16)


def window_attention(
    query, keyed, valued, low, high, w_out, first_frame, length, row_base, rows, blocks
):
    frame_count, width = query.shape
    out_width = w_out.shape[1]
    block_width = out_width // blocks
    tq = min(256, rows)
    block_base = row_base // tq
    span = tq + 2 * HALF
    scal = jnp.array([0, 0, row_base], jnp.int32).at[0].set(first_frame).at[1].set(length)
    kernel = functools.partial(window_kernel, heads=width // HD, scale=HD ** (-0.5))
    cost = pl.CostEstimate(
        flops=4 * rows * span * width + 2 * rows * width * out_width,
        transcendentals=rows * span * (width // HD),
        bytes_accessed=2 * (2 * query.size + rows * width + 2 * low.size + w_out.size + rows * out_width),
    )
    full = lambda i, s: (0, 0)
    return pl.pallas_call(
        kernel,
        cost_estimate=cost,
        out_shape=jax.ShapeDtypeStruct((blocks, rows, block_width), jnp.bfloat16),
        grid_spec=pltpu.PrefetchScalarGridSpec(
            num_scalar_prefetch=1,
            grid=(rows // tq,),
            in_specs=[
                pl.BlockSpec((tq, width), lambda i, s: (i + block_base, 0)),
                pl.BlockSpec(keyed.shape, full),
                pl.BlockSpec(valued.shape, full),
                pl.BlockSpec(low.shape, full),
                pl.BlockSpec(high.shape, full),
                pl.BlockSpec(w_out.shape, full),
            ],
            out_specs=pl.BlockSpec((blocks, tq, block_width), lambda i, s: (0, i, 0)),
            scratch_shapes=[
                pltpu.VMEM((frame_count + 2 * HALF, width), jnp.bfloat16),
                pltpu.VMEM((frame_count + 2 * HALF, width), jnp.bfloat16),
                pltpu.VMEM((tq, width), jnp.bfloat16),
            ],
        ),
        compiler_params=pltpu.CompilerParams(dimension_semantics=("arbitrary",)),
    )(scal, query, keyed, valued, low, high, w_out)


def latent_kernel(scal_ref, q_ref, k_ref, v_ref, acc_ref, stat_ref, *, heads, scale):
    tl = q_ref.shape[0]
    frame_count = k_ref.shape[0]
    valid = lax.broadcasted_iota(jnp.int32, (tl, frame_count), 1) < scal_ref[0]
    stat_ref[...] = jnp.zeros_like(stat_ref)
    for h in range(heads):
        cols = slice(h * HD, (h + 1) * HD)
        s = lax.dot_general(
            q_ref[:, cols], k_ref[:, cols], (((1,), (1,)), ((), ())),
            preferred_element_type=jnp.float32,
        ) * scale
        masked = jnp.where(valid, s, NEG)
        peak = jnp.max(masked, axis=1, keepdims=True)
        weights = jnp.where(valid, jnp.exp(masked - peak), 0.0)
        total = jnp.sum(weights, axis=1, keepdims=True)
        acc_ref[:, cols] = jnp.dot(
            weights.astype(jnp.bfloat16), v_ref[:, cols], preferred_element_type=jnp.float32
        )
        stat_ref[:, h : h + 1] = peak
        stat_ref[:, heads + h : heads + h + 1] = total


def latent_attention(latent_query, keyed, valued, valid_count):
    latent_count, width = latent_query.shape
    heads = width // HD
    tl = min(256, latent_count)
    scal = jnp.reshape(valid_count, (1,)).astype(jnp.int32)
    kernel = functools.partial(latent_kernel, heads=heads, scale=HD ** (-0.5))
    frame_count = keyed.shape[0]
    cost = pl.CostEstimate(
        flops=4 * latent_count * frame_count * width,
        transcendentals=latent_count * frame_count * heads,
        bytes_accessed=2 * (latent_query.size + 2 * keyed.size) + 4 * latent_count * (width + 128),
    )
    acc, stat = pl.pallas_call(
        kernel,
        cost_estimate=cost,
        out_shape=(
            jax.ShapeDtypeStruct((latent_count, width), jnp.float32),
            jax.ShapeDtypeStruct((latent_count, 128), jnp.float32),
        ),
        grid_spec=pltpu.PrefetchScalarGridSpec(
            num_scalar_prefetch=1,
            grid=(latent_count // tl,),
            in_specs=[
                pl.BlockSpec((tl, width), lambda i, s: (i, 0)),
                pl.BlockSpec(keyed.shape, lambda i, s: (0, 0)),
                pl.BlockSpec(valued.shape, lambda i, s: (0, 0)),
            ],
            out_specs=[
                pl.BlockSpec((tl, width), lambda i, s: (i, 0)),
                pl.BlockSpec((tl, 128), lambda i, s: (i, 0)),
            ],
        ),
    )(scal, latent_query, keyed, valued)
    return stat[:, :heads], stat[:, heads : 2 * heads], acc


def shifted_blocks(payload, axis, rows):
    count = lax.axis_size(axis)
    place = lax.axis_index(axis)
    own = lax.dynamic_slice_in_dim(payload, place * rows, rows, 0)
    parts = [own]
    for shift in range(1, count):
        target = (place + shift) % count
        block = lax.dynamic_slice_in_dim(payload, target * rows, rows, 0)
        pairs = [(i, (i + shift) % count) for i in range(count)]
        parts.append(lax.ppermute(block, axis, pairs))
    return jnp.stack(parts)


def column_sum(partial, axis):
    count = lax.axis_size(axis)
    place = lax.axis_index(axis)
    width = partial.shape[1] // count
    own = lax.dynamic_slice_in_dim(partial, place * width, width, 1)
    total = own.astype(jnp.float32)
    for shift in range(1, count):
        target = (place + shift) % count
        block = lax.dynamic_slice_in_dim(partial, target * width, width, 1)
        pairs = [(i, (i + shift) % count) for i in range(count)]
        total = total + lax.ppermute(block, axis, pairs).astype(jnp.float32)
    return total.astype(jnp.bfloat16)


def send_order(axis):
    count = lax.axis_size(axis)
    place = lax.axis_index(axis)
    if count % 2 != 0:
        return [(place + j) % count for j in range(count)]
    chips = count // 2
    core = place % 2
    chip = place // 2
    theirs = [2 * ((chip + d) % chips) + 1 - core for d in range(chips)]
    mine = [2 * ((chip + d) % chips) + core for d in range(chips)]
    return theirs + mine


def ordered_columns(weight, axis):
    count = lax.axis_size(axis)
    width = weight.shape[1] // count
    return jnp.concatenate(
        [lax.dynamic_slice_in_dim(weight, b * width, width, 1) for b in send_order(axis)], axis=1
    )


def chip_pair_sums(blocks, axis):
    count = lax.axis_size(axis)
    chips = count // 2
    swap = [(i, i ^ 1) for i in range(count)]
    received = lax.ppermute(blocks[:chips], axis, swap)
    return [
        (blocks[chips + d].astype(jnp.float32) + received[d].astype(jnp.float32)).astype(
            jnp.bfloat16
        )
        for d in range(chips)
    ]


def cross_chip_sum(chip_sums, axis):
    count = lax.axis_size(axis)
    chips = count // 2
    total = chip_sums[0].astype(jnp.float32)
    for d in range(1, chips):
        pairs = [(2 * c + k, 2 * ((c + d) % chips) + k) for c in range(chips) for k in range(2)]
        total = total + lax.ppermute(chip_sums[d], axis, pairs).astype(jnp.float32)
    return total.astype(jnp.bfloat16)


def plain_block_sum(blocks, axis):
    count = lax.axis_size(axis)
    total = blocks[0].astype(jnp.float32)
    for shift in range(1, count):
        pairs = [(i, (i + shift) % count) for i in range(count)]
        total = total + lax.ppermute(blocks[shift], axis, pairs).astype(jnp.float32)
    return total.astype(jnp.bfloat16)


def split_three(values):
    hi = values.astype(jnp.bfloat16)
    rest = values - hi.astype(jnp.float32)
    mid = rest.astype(jnp.bfloat16)
    lo = (rest - mid.astype(jnp.float32)).astype(jnp.bfloat16)
    return [hi, mid, lo]


def exchange_rows(accum, stats, axis, rows):
    count = lax.axis_size(axis)
    place = lax.axis_index(axis)
    width = accum.shape[1]
    packed = (stats.shape[0] * rows) % width == 0

    def payload(target):
        acc = lax.dynamic_slice_in_dim(accum, target * rows, rows, 0)
        stat = lax.dynamic_slice_in_dim(stats, target * rows, rows, 1)
        if not packed:
            return acc, stat
        return jnp.concatenate([acc] + split_three(stat.reshape(-1, width)), axis=0), None

    def unpack(block, stat):
        if not packed:
            return block[:rows], stat
        k = (block.shape[0] - rows) // 3
        pieces = [block[rows + i * k : rows + (i + 1) * k].astype(jnp.float32) for i in range(3)]
        return block[:rows], (pieces[0] + pieces[1] + pieces[2]).reshape(stats.shape[0], rows)

    accs, stat_parts = [], []
    own, own_stat = payload(place)
    a, b = unpack(own, own_stat)
    accs.append(a)
    stat_parts.append(b)
    for shift in range(1, count):
        pairs = [(i, (i + shift) % count) for i in range(count)]
        block, stat = payload((place + shift) % count)
        block = lax.ppermute(block, axis, pairs)
        if stat is not None:
            stat = lax.ppermute(stat, axis, pairs)
        a, b = unpack(block, stat)
        accs.append(a)
        stat_parts.append(b)
    return jnp.stack(accs).astype(jnp.float32), jnp.stack(stat_parts)


def per_device(
    frames, latents, lengths, w_query, w_key, w_value, w_out, w_latent_query, w_latent_out
):
    frame_count = frames.shape[0]
    head_width = w_query.shape[1]
    heads_here = head_width // HD
    seq_devices = lax.axis_size("seq")
    seq_place = lax.axis_index("seq")
    first_frame = seq_place * frame_count
    length = lengths[0]
    query = project(frames, w_query)
    keyed = project(frames, w_key)
    valued = project(frames, w_value)
    low, high = halos(keyed, valued, "seq")
    chunks = 2 if frame_count % 512 == 0 else 1
    chunk_rows = frame_count // chunks
    head_devices = lax.axis_size("head")
    paired = head_devices % 2 == 0
    w_ordered = ordered_columns(w_out, "head")
    parts = [
        window_attention(
            query, keyed, valued, low, high, w_ordered, first_frame, length,
            c * chunk_rows, chunk_rows, head_devices,
        )
        for c in range(chunks)
    ]
    latent_count = latents.shape[0]
    latent_query = project(latents, w_latent_query)
    valid_count = jnp.clip(length - first_frame, 0, frame_count)
    frame_parts = []
    if paired:
        first_sums = chip_pair_sums(parts[0], "head")
        first_sums, rest, keyed, valued = lax.optimization_barrier(
            (first_sums, parts[1:], keyed, valued)
        )
        frame_parts.append(cross_chip_sum(first_sums, "head"))
        rest_sums = [chip_pair_sums(blocks, "head") for blocks in rest]
    else:
        frame_parts = [plain_block_sum(blocks, "head") for blocks in parts]
    peaks, totals, local_accum = latent_attention(latent_query, keyed, valued, valid_count)
    stats = jnp.concatenate([peaks, totals], axis=1).T
    local_accum = local_accum.astype(jnp.bfloat16)
    if paired:
        rest_sums, local_accum, stats = lax.optimization_barrier((rest_sums, local_accum, stats))
        frame_parts.extend(cross_chip_sum(sums, "head") for sums in rest_sums)
    frames_out = jnp.concatenate(frame_parts, axis=0)
    rows_here = latent_count // seq_devices
    part_accum, part_stats = exchange_rows(local_accum, stats, "seq", rows_here)
    part_peak = part_stats[:, :heads_here, :]
    part_total = part_stats[:, heads_here:, :]
    joint = jnp.max(part_peak, axis=0)
    factor = jnp.exp(part_peak - joint[None])
    own_total = jnp.sum(part_total * factor, axis=0).T
    factor_rows = jnp.transpose(factor, (0, 2, 1))
    own_accum = jnp.sum(part_accum * jnp.repeat(factor_rows, HD, axis=2), axis=0)
    summary = (own_accum / jnp.repeat(own_total, HD, axis=1)).astype(jnp.bfloat16)
    if paired:
        latent_terms = jnp.dot(
            summary, ordered_columns(w_latent_out, "head"), preferred_element_type=jnp.float32
        ).astype(jnp.bfloat16)
        block_width = latent_terms.shape[1] // head_devices
        latent_blocks = jnp.stack(
            [latent_terms[:, j * block_width : (j + 1) * block_width] for j in range(head_devices)]
        )
        latents_out = cross_chip_sum(chip_pair_sums(latent_blocks, "head"), "head")
    else:
        latent_terms = jnp.dot(summary, w_latent_out, preferred_element_type=jnp.float32)
        latents_out = column_sum(latent_terms.astype(jnp.bfloat16), "head")
    return (frames_out, latents_out)


def solution(mesh):
    return jax.shard_map(
        per_device,
        mesh=mesh,
        in_specs=(
            P(("groups", "seq"), None),
            P(),
            P("groups"),
            P(None, "head"),
            P(None, "head"),
            P(None, "head"),
            P("head", None),
            P(None, "head"),
            P("head", None),
        ),
        out_specs=(P(("groups", "seq"), "head"), P(("groups", "seq"), "head")),
        check_vma=False,
    )
```

```python
import functools

import jax
import jax.numpy as jnp
from jax import lax
from jax.experimental import pallas as pl
from jax.experimental.pallas import tpu as pltpu
from jax.sharding import PartitionSpec as P

HD = 64
HALF = 256
NEG = -1e30


def halos(keyed, valued, axis):
    count = lax.axis_size(axis)
    forward = [(i, i + 1) for i in range(count - 1)]
    backward = [(target, source) for source, target in forward]
    tail = jnp.concatenate([keyed[-HALF:], valued[-HALF:]], axis=1)
    head = jnp.concatenate([keyed[:HALF], valued[:HALF]], axis=1)
    return lax.ppermute(tail, axis, forward), lax.ppermute(head, axis, backward)


def project(source, weight):
    return jnp.dot(source, weight, preferred_element_type=jnp.float32).astype(jnp.bfloat16)


def window_kernel(
    scal_ref, q_ref, k_ref, v_ref, low_ref, high_ref, w_ref, o_ref, kbuf, vbuf, att_ref, *,
    heads, scale
):
    tq = q_ref.shape[0]
    frame_count, width = k_ref.shape
    span = tq + 2 * HALF

    @pl.when(pl.program_id(0) == 0)
    def _fill():
        kbuf[0:HALF, :] = low_ref[:, 0:width]
        vbuf[0:HALF, :] = low_ref[:, width : 2 * width]
        kbuf[HALF : HALF + frame_count, :] = k_ref[...]
        vbuf[HALF : HALF + frame_count, :] = v_ref[...]
        kbuf[HALF + frame_count :, :] = high_ref[:, 0:width]
        vbuf[HALF + frame_count :, :] = high_ref[:, width : 2 * width]

    start = pl.multiple_of(scal_ref[2] + pl.program_id(0) * tq, tq)
    first = scal_ref[0]
    length = scal_ref[1]
    row = lax.broadcasted_iota(jnp.int32, (tq, span), 0)
    col = lax.broadcasted_iota(jnp.int32, (tq, span), 1)
    offset = col - row
    key_pos = first + start - HALF + col
    allowed = (offset >= 0) & (offset <= 2 * HALF) & (key_pos >= 0) & (key_pos < length)
    query_pos = first + start + lax.broadcasted_iota(jnp.int32, (tq, 1), 0)
    query_valid = query_pos < length
    for h in range(heads):
        cols = slice(h * HD, (h + 1) * HD)
        q = q_ref[:, cols]
        k = kbuf[pl.ds(start, span), cols]
        v = vbuf[pl.ds(start, span), cols]
        s = lax.dot_general(
            q, k, (((1,), (1,)), ((), ())), preferred_element_type=jnp.float32
        ) * scale
        masked = jnp.where(allowed, s, NEG)
        peak = jnp.max(masked, axis=1, keepdims=True)
        weights = jnp.exp(masked - peak)
        denom = jnp.sum(weights, axis=1, keepdims=True)
        blended = jnp.dot(weights.astype(jnp.bfloat16), v, preferred_element_type=jnp.float32)
        divisor = jnp.where(query_valid, denom, 1.0)
        att_ref[:, cols] = jnp.where(query_valid, blended / divisor, 0.0).astype(jnp.bfloat16)
    result = jnp.dot(att_ref[...], w_ref[...], preferred_element_type=jnp.float32)
    block_width = o_ref.shape[2]
    for b in range(o_ref.shape[0]):
        o_ref[b] = result[:, b * block_width : (b + 1) * block_width].astype(jnp.bfloat16)


def window_attention(
    query, keyed, valued, low, high, w_out, first_frame, length, row_base, rows, blocks
):
    frame_count, width = query.shape
    out_width = w_out.shape[1]
    block_width = out_width // blocks
    tq = min(256, rows)
    block_base = row_base // tq
    span = tq + 2 * HALF
    scal = jnp.array([0, 0, row_base], jnp.int32).at[0].set(first_frame).at[1].set(length)
    kernel = functools.partial(window_kernel, heads=width // HD, scale=HD ** (-0.5))
    cost = pl.CostEstimate(
        flops=4 * rows * span * width + 2 * rows * width * out_width,
        transcendentals=rows * span * (width // HD),
        bytes_accessed=2 * (2 * query.size + rows * width + 2 * low.size + w_out.size + rows * out_width),
    )
    full = lambda i, s: (0, 0)
    return pl.pallas_call(
        kernel,
        cost_estimate=cost,
        out_shape=jax.ShapeDtypeStruct((blocks, rows, block_width), jnp.bfloat16),
        grid_spec=pltpu.PrefetchScalarGridSpec(
            num_scalar_prefetch=1,
            grid=(rows // tq,),
            in_specs=[
                pl.BlockSpec((tq, width), lambda i, s: (i + block_base, 0)),
                pl.BlockSpec(keyed.shape, full),
                pl.BlockSpec(valued.shape, full),
                pl.BlockSpec(low.shape, full),
                pl.BlockSpec(high.shape, full),
                pl.BlockSpec(w_out.shape, full),
            ],
            out_specs=pl.BlockSpec((blocks, tq, block_width), lambda i, s: (0, i, 0)),
            scratch_shapes=[
                pltpu.VMEM((frame_count + 2 * HALF, width), jnp.bfloat16),
                pltpu.VMEM((frame_count + 2 * HALF, width), jnp.bfloat16),
                pltpu.VMEM((tq, width), jnp.bfloat16),
            ],
        ),
        compiler_params=pltpu.CompilerParams(dimension_semantics=("arbitrary",)),
    )(scal, query, keyed, valued, low, high, w_out)


def latent_kernel(scal_ref, q_ref, k_ref, v_ref, acc_ref, stat_ref, *, heads, scale):
    tl = q_ref.shape[0]
    frame_count = k_ref.shape[0]
    valid = lax.broadcasted_iota(jnp.int32, (tl, frame_count), 1) < scal_ref[0]
    stat_ref[...] = jnp.zeros_like(stat_ref)
    for h in range(heads):
        cols = slice(h * HD, (h + 1) * HD)
        s = lax.dot_general(
            q_ref[:, cols], k_ref[:, cols], (((1,), (1,)), ((), ())),
            preferred_element_type=jnp.float32,
        ) * scale
        masked = jnp.where(valid, s, NEG)
        peak = jnp.max(masked, axis=1, keepdims=True)
        weights = jnp.exp(masked - peak)
        total = jnp.sum(weights, axis=1, keepdims=True)
        acc_ref[:, cols] = jnp.dot(
            weights.astype(jnp.bfloat16), v_ref[:, cols], preferred_element_type=jnp.float32
        )
        stat_ref[:, h : h + 1] = peak
        stat_ref[:, heads + h : heads + h + 1] = total


def latent_attention(latent_query, keyed, valued, valid_count):
    latent_count, width = latent_query.shape
    heads = width // HD
    tl = min(256, latent_count)
    scal = jnp.reshape(valid_count, (1,)).astype(jnp.int32)
    kernel = functools.partial(latent_kernel, heads=heads, scale=HD ** (-0.5))
    frame_count = keyed.shape[0]
    cost = pl.CostEstimate(
        flops=4 * latent_count * frame_count * width,
        transcendentals=latent_count * frame_count * heads,
        bytes_accessed=2 * (latent_query.size + 2 * keyed.size) + 4 * latent_count * (width + 128),
    )
    acc, stat = pl.pallas_call(
        kernel,
        cost_estimate=cost,
        out_shape=(
            jax.ShapeDtypeStruct((latent_count, width), jnp.float32),
            jax.ShapeDtypeStruct((latent_count, 128), jnp.float32),
        ),
        grid_spec=pltpu.PrefetchScalarGridSpec(
            num_scalar_prefetch=1,
            grid=(latent_count // tl,),
            in_specs=[
                pl.BlockSpec((tl, width), lambda i, s: (i, 0)),
                pl.BlockSpec(keyed.shape, lambda i, s: (0, 0)),
                pl.BlockSpec(valued.shape, lambda i, s: (0, 0)),
            ],
            out_specs=[
                pl.BlockSpec((tl, width), lambda i, s: (i, 0)),
                pl.BlockSpec((tl, 128), lambda i, s: (i, 0)),
            ],
        ),
    )(scal, latent_query, keyed, valued)
    return stat[:, :heads], stat[:, heads : 2 * heads], acc


def shifted_blocks(payload, axis, rows):
    count = lax.axis_size(axis)
    place = lax.axis_index(axis)
    own = lax.dynamic_slice_in_dim(payload, place * rows, rows, 0)
    parts = [own]
    for shift in range(1, count):
        target = (place + shift) % count
        block = lax.dynamic_slice_in_dim(payload, target * rows, rows, 0)
        pairs = [(i, (i + shift) % count) for i in range(count)]
        parts.append(lax.ppermute(block, axis, pairs))
    return jnp.stack(parts)


def column_sum(partial, axis):
    count = lax.axis_size(axis)
    place = lax.axis_index(axis)
    width = partial.shape[1] // count
    own = lax.dynamic_slice_in_dim(partial, place * width, width, 1)
    total = own.astype(jnp.float32)
    for shift in range(1, count):
        target = (place + shift) % count
        block = lax.dynamic_slice_in_dim(partial, target * width, width, 1)
        pairs = [(i, (i + shift) % count) for i in range(count)]
        total = total + lax.ppermute(block, axis, pairs).astype(jnp.float32)
    return total.astype(jnp.bfloat16)


def send_order(axis):
    count = lax.axis_size(axis)
    place = lax.axis_index(axis)
    if count % 2 != 0:
        return [(place + j) % count for j in range(count)]
    chips = count // 2
    core = place % 2
    chip = place // 2
    theirs = [2 * ((chip + d) % chips) + 1 - core for d in range(chips)]
    mine = [2 * ((chip + d) % chips) + core for d in range(chips)]
    return theirs + mine


def ordered_columns(weight, axis):
    count = lax.axis_size(axis)
    width = weight.shape[1] // count
    return jnp.concatenate(
        [lax.dynamic_slice_in_dim(weight, b * width, width, 1) for b in send_order(axis)], axis=1
    )


def chip_pair_sums(blocks, axis):
    count = lax.axis_size(axis)
    chips = count // 2
    swap = [(i, i ^ 1) for i in range(count)]
    received = lax.ppermute(blocks[:chips], axis, swap)
    return [
        (blocks[chips + d].astype(jnp.float32) + received[d].astype(jnp.float32)).astype(
            jnp.bfloat16
        )
        for d in range(chips)
    ]


def cross_chip_sum(chip_sums, axis):
    count = lax.axis_size(axis)
    chips = count // 2
    total = chip_sums[0].astype(jnp.float32)
    for d in range(1, chips):
        pairs = [(2 * c + k, 2 * ((c + d) % chips) + k) for c in range(chips) for k in range(2)]
        total = total + lax.ppermute(chip_sums[d], axis, pairs).astype(jnp.float32)
    return total.astype(jnp.bfloat16)


def plain_block_sum(blocks, axis):
    count = lax.axis_size(axis)
    total = blocks[0].astype(jnp.float32)
    for shift in range(1, count):
        pairs = [(i, (i + shift) % count) for i in range(count)]
        total = total + lax.ppermute(blocks[shift], axis, pairs).astype(jnp.float32)
    return total.astype(jnp.bfloat16)


def split_three(values):
    hi = values.astype(jnp.bfloat16)
    rest = values - hi.astype(jnp.float32)
    mid = rest.astype(jnp.bfloat16)
    lo = (rest - mid.astype(jnp.float32)).astype(jnp.bfloat16)
    return [hi, mid, lo]


def exchange_rows(accum, stats, axis, rows):
    count = lax.axis_size(axis)
    place = lax.axis_index(axis)
    width = accum.shape[1]
    packed = (stats.shape[0] * rows) % width == 0

    def payload(target):
        acc = lax.dynamic_slice_in_dim(accum, target * rows, rows, 0)
        stat = lax.dynamic_slice_in_dim(stats, target * rows, rows, 1)
        if not packed:
            return acc, stat
        return jnp.concatenate([acc] + split_three(stat.reshape(-1, width)), axis=0), None

    def unpack(block, stat):
        if not packed:
            return block[:rows], stat
        k = (block.shape[0] - rows) // 3
        pieces = [block[rows + i * k : rows + (i + 1) * k].astype(jnp.float32) for i in range(3)]
        return block[:rows], (pieces[0] + pieces[1] + pieces[2]).reshape(stats.shape[0], rows)

    accs, stat_parts = [], []
    own, own_stat = payload(place)
    a, b = unpack(own, own_stat)
    accs.append(a)
    stat_parts.append(b)
    for shift in range(1, count):
        pairs = [(i, (i + shift) % count) for i in range(count)]
        block, stat = payload((place + shift) % count)
        block = lax.ppermute(block, axis, pairs)
        if stat is not None:
            stat = lax.ppermute(stat, axis, pairs)
        a, b = unpack(block, stat)
        accs.append(a)
        stat_parts.append(b)
    return jnp.stack(accs).astype(jnp.float32), jnp.stack(stat_parts)


def per_device(
    frames, latents, lengths, w_query, w_key, w_value, w_out, w_latent_query, w_latent_out
):
    frame_count = frames.shape[0]
    head_width = w_query.shape[1]
    heads_here = head_width // HD
    seq_devices = lax.axis_size("seq")
    seq_place = lax.axis_index("seq")
    first_frame = seq_place * frame_count
    length = lengths[0]
    query = project(frames, w_query)
    keyed = project(frames, w_key)
    valued = project(frames, w_value)
    low, high = halos(keyed, valued, "seq")
    chunks = 2 if frame_count % 512 == 0 else 1
    chunk_rows = frame_count // chunks
    head_devices = lax.axis_size("head")
    paired = head_devices % 2 == 0
    w_ordered = ordered_columns(w_out, "head")
    parts = [
        window_attention(
            query, keyed, valued, low, high, w_ordered, first_frame, length,
            c * chunk_rows, chunk_rows, head_devices,
        )
        for c in range(chunks)
    ]
    latent_count = latents.shape[0]
    latent_query = project(latents, w_latent_query)
    valid_count = jnp.clip(length - first_frame, 0, frame_count)
    frame_parts = []
    if paired:
        first_sums = chip_pair_sums(parts[0], "head")
        first_sums, rest, keyed, valued = lax.optimization_barrier(
            (first_sums, parts[1:], keyed, valued)
        )
        frame_parts.append(cross_chip_sum(first_sums, "head"))
        rest_sums = [chip_pair_sums(blocks, "head") for blocks in rest]
    else:
        frame_parts = [plain_block_sum(blocks, "head") for blocks in parts]
    peaks, totals, local_accum = latent_attention(latent_query, keyed, valued, valid_count)
    stats = jnp.concatenate([peaks, totals], axis=1).T
    local_accum = local_accum.astype(jnp.bfloat16)
    if paired:
        rest_sums, local_accum, stats = lax.optimization_barrier((rest_sums, local_accum, stats))
        frame_parts.extend(cross_chip_sum(sums, "head") for sums in rest_sums)
    frames_out = jnp.concatenate(frame_parts, axis=0)
    rows_here = latent_count // seq_devices
    part_accum, part_stats = exchange_rows(local_accum, stats, "seq", rows_here)
    part_peak = part_stats[:, :heads_here, :]
    part_total = part_stats[:, heads_here:, :]
    joint = jnp.max(part_peak, axis=0)
    factor = jnp.exp(part_peak - joint[None])
    own_total = jnp.sum(part_total * factor, axis=0).T
    factor_rows = jnp.transpose(factor, (0, 2, 1))
    own_accum = jnp.sum(part_accum * jnp.repeat(factor_rows, HD, axis=2), axis=0)
    summary = (own_accum / jnp.repeat(own_total, HD, axis=1)).astype(jnp.bfloat16)
    if paired:
        latent_terms = jnp.dot(
            summary, ordered_columns(w_latent_out, "head"), preferred_element_type=jnp.float32
        ).astype(jnp.bfloat16)
        block_width = latent_terms.shape[1] // head_devices
        latent_blocks = jnp.stack(
            [latent_terms[:, j * block_width : (j + 1) * block_width] for j in range(head_devices)]
        )
        latents_out = cross_chip_sum(chip_pair_sums(latent_blocks, "head"), "head")
    else:
        latent_terms = jnp.dot(summary, w_latent_out, preferred_element_type=jnp.float32)
        latents_out = column_sum(latent_terms.astype(jnp.bfloat16), "head")
    return (frames_out, latents_out)


def solution(mesh):
    return jax.shard_map(
        per_device,
        mesh=mesh,
        in_specs=(
            P(("groups", "seq"), None),
            P(),
            P("groups"),
            P(None, "head"),
            P(None, "head"),
            P(None, "head"),
            P("head", None),
            P(None, "head"),
            P("head", None),
        ),
        out_specs=(P(("groups", "seq"), "head"), P(("groups", "seq"), "head")),
        check_vma=False,
    )
```

```python
import functools

import jax
import jax.numpy as jnp
from jax import lax
from jax.experimental import pallas as pl
from jax.experimental.pallas import tpu as pltpu
from jax.sharding import PartitionSpec as P

HD = 64
HALF = 256
NEG = -1e30


def halos(keyed, valued, axis):
    count = lax.axis_size(axis)
    forward = [(i, i + 1) for i in range(count - 1)]
    backward = [(target, source) for source, target in forward]
    tail = jnp.concatenate([keyed[-HALF:], valued[-HALF:]], axis=1)
    head = jnp.concatenate([keyed[:HALF], valued[:HALF]], axis=1)
    return lax.ppermute(tail, axis, forward), lax.ppermute(head, axis, backward)


def project(source, weight):
    return jnp.dot(source, weight, preferred_element_type=jnp.float32).astype(jnp.bfloat16)


def window_kernel(
    scal_ref, q_ref, k_ref, v_ref, low_ref, high_ref, w_ref, o_ref, kbuf, vbuf, att_ref, *,
    heads, scale
):
    tq = q_ref.shape[0]
    frame_count, width = k_ref.shape
    span = tq + 2 * HALF

    @pl.when(pl.program_id(0) == 0)
    def _fill():
        kbuf[0:HALF, :] = low_ref[:, 0:width]
        vbuf[0:HALF, :] = low_ref[:, width : 2 * width]
        kbuf[HALF : HALF + frame_count, :] = k_ref[...]
        vbuf[HALF : HALF + frame_count, :] = v_ref[...]
        kbuf[HALF + frame_count :, :] = high_ref[:, 0:width]
        vbuf[HALF + frame_count :, :] = high_ref[:, width : 2 * width]

    start = pl.multiple_of(scal_ref[2] + pl.program_id(0) * tq, tq)
    first = scal_ref[0]
    length = scal_ref[1]
    row = lax.broadcasted_iota(jnp.int32, (tq, span), 0)
    col = lax.broadcasted_iota(jnp.int32, (tq, span), 1)
    offset = col - row
    key_pos = first + start - HALF + col
    allowed = (offset >= 0) & (offset <= 2 * HALF) & (key_pos >= 0) & (key_pos < length)
    query_pos = first + start + lax.broadcasted_iota(jnp.int32, (tq, 1), 0)
    query_valid = query_pos < length
    for h in range(heads):
        cols = slice(h * HD, (h + 1) * HD)
        q = q_ref[:, cols]
        k = kbuf[pl.ds(start, span), cols]
        v = vbuf[pl.ds(start, span), cols]
        s = lax.dot_general(
            q, k, (((1,), (1,)), ((), ())), preferred_element_type=jnp.float32
        ) * scale
        masked = jnp.where(allowed, s, NEG)
        peak = jnp.max(masked, axis=1, keepdims=True)
        weights = jnp.exp(masked - peak)
        denom = jnp.sum(weights, axis=1, keepdims=True)
        blended = jnp.dot(weights.astype(jnp.bfloat16), v, preferred_element_type=jnp.float32)
        divisor = jnp.where(query_valid, denom, 1.0)
        att_ref[:, cols] = jnp.where(query_valid, blended / divisor, 0.0).astype(jnp.bfloat16)
    result = jnp.dot(att_ref[...], w_ref[...], preferred_element_type=jnp.float32)
    block_width = o_ref.shape[2]
    for b in range(o_ref.shape[0]):
        o_ref[b] = result[:, b * block_width : (b + 1) * block_width].astype(jnp.bfloat16)


def window_attention(
    query, keyed, valued, low, high, w_out, first_frame, length, row_base, rows, blocks
):
    frame_count, width = query.shape
    out_width = w_out.shape[1]
    block_width = out_width // blocks
    tq = min(256, rows)
    block_base = row_base // tq
    span = tq + 2 * HALF
    scal = jnp.array([0, 0, row_base], jnp.int32).at[0].set(first_frame).at[1].set(length)
    kernel = functools.partial(window_kernel, heads=width // HD, scale=HD ** (-0.5))
    cost = pl.CostEstimate(
        flops=4 * rows * span * width + 2 * rows * width * out_width,
        transcendentals=rows * span * (width // HD),
        bytes_accessed=2 * (2 * query.size + rows * width + 2 * low.size + w_out.size + rows * out_width),
    )
    full = lambda i, s: (0, 0)
    return pl.pallas_call(
        kernel,
        cost_estimate=cost,
        out_shape=jax.ShapeDtypeStruct((blocks, rows, block_width), jnp.bfloat16),
        grid_spec=pltpu.PrefetchScalarGridSpec(
            num_scalar_prefetch=1,
            grid=(rows // tq,),
            in_specs=[
                pl.BlockSpec((tq, width), lambda i, s: (i + block_base, 0)),
                pl.BlockSpec(keyed.shape, full),
                pl.BlockSpec(valued.shape, full),
                pl.BlockSpec(low.shape, full),
                pl.BlockSpec(high.shape, full),
                pl.BlockSpec(w_out.shape, full),
            ],
            out_specs=pl.BlockSpec((blocks, tq, block_width), lambda i, s: (0, i, 0)),
            scratch_shapes=[
                pltpu.VMEM((frame_count + 2 * HALF, width), jnp.bfloat16),
                pltpu.VMEM((frame_count + 2 * HALF, width), jnp.bfloat16),
                pltpu.VMEM((tq, width), jnp.bfloat16),
            ],
        ),
        compiler_params=pltpu.CompilerParams(dimension_semantics=("arbitrary",)),
    )(scal, query, keyed, valued, low, high, w_out)


def latent_kernel(scal_ref, q_ref, k_ref, v_ref, acc_ref, stat_ref, *, heads, scale):
    tl = q_ref.shape[0]
    frame_count = k_ref.shape[0]
    valid = lax.broadcasted_iota(jnp.int32, (tl, frame_count), 1) < scal_ref[0]
    stat_ref[...] = jnp.zeros_like(stat_ref)
    for h in range(heads):
        cols = slice(h * HD, (h + 1) * HD)
        s = lax.dot_general(
            q_ref[:, cols], k_ref[:, cols], (((1,), (1,)), ((), ())),
            preferred_element_type=jnp.float32,
        ) * scale
        masked = jnp.where(valid, s, NEG)
        peak = jnp.max(masked, axis=1, keepdims=True)
        weights = jnp.exp(masked - peak)
        total = jnp.sum(weights, axis=1, keepdims=True)
        acc_ref[:, cols] = jnp.dot(
            weights.astype(jnp.bfloat16), v_ref[:, cols], preferred_element_type=jnp.float32
        )
        stat_ref[:, h : h + 1] = peak
        stat_ref[:, heads + h : heads + h + 1] = total


def latent_attention(latent_query, keyed, valued, valid_count):
    latent_count, width = latent_query.shape
    heads = width // HD
    tl = min(256, latent_count)
    scal = jnp.reshape(valid_count, (1,)).astype(jnp.int32)
    kernel = functools.partial(latent_kernel, heads=heads, scale=HD ** (-0.5))
    frame_count = keyed.shape[0]
    cost = pl.CostEstimate(
        flops=4 * latent_count * frame_count * width,
        transcendentals=latent_count * frame_count * heads,
        bytes_accessed=2 * (latent_query.size + 2 * keyed.size) + 4 * latent_count * (width + 128),
    )
    acc, stat = pl.pallas_call(
        kernel,
        cost_estimate=cost,
        out_shape=(
            jax.ShapeDtypeStruct((latent_count, width), jnp.float32),
            jax.ShapeDtypeStruct((latent_count, 128), jnp.float32),
        ),
        grid_spec=pltpu.PrefetchScalarGridSpec(
            num_scalar_prefetch=1,
            grid=(latent_count // tl,),
            in_specs=[
                pl.BlockSpec((tl, width), lambda i, s: (i, 0)),
                pl.BlockSpec(keyed.shape, lambda i, s: (0, 0)),
                pl.BlockSpec(valued.shape, lambda i, s: (0, 0)),
            ],
            out_specs=[
                pl.BlockSpec((tl, width), lambda i, s: (i, 0)),
                pl.BlockSpec((tl, 128), lambda i, s: (i, 0)),
            ],
        ),
    )(scal, latent_query, keyed, valued)
    return stat[:, :heads], stat[:, heads : 2 * heads], acc


def shifted_blocks(payload, axis, rows):
    count = lax.axis_size(axis)
    place = lax.axis_index(axis)
    own = lax.dynamic_slice_in_dim(payload, place * rows, rows, 0)
    parts = [own]
    for shift in range(1, count):
        target = (place + shift) % count
        block = lax.dynamic_slice_in_dim(payload, target * rows, rows, 0)
        pairs = [(i, (i + shift) % count) for i in range(count)]
        parts.append(lax.ppermute(block, axis, pairs))
    return jnp.stack(parts)


def column_sum(partial, axis):
    count = lax.axis_size(axis)
    place = lax.axis_index(axis)
    width = partial.shape[1] // count
    own = lax.dynamic_slice_in_dim(partial, place * width, width, 1)
    total = own.astype(jnp.float32)
    for shift in range(1, count):
        target = (place + shift) % count
        block = lax.dynamic_slice_in_dim(partial, target * width, width, 1)
        pairs = [(i, (i + shift) % count) for i in range(count)]
        total = total + lax.ppermute(block, axis, pairs).astype(jnp.float32)
    return total.astype(jnp.bfloat16)


def send_order(axis):
    count = lax.axis_size(axis)
    place = lax.axis_index(axis)
    if count % 2 != 0:
        return [(place + j) % count for j in range(count)]
    chips = count // 2
    core = place % 2
    chip = place // 2
    theirs = [2 * ((chip + d) % chips) + 1 - core for d in range(chips)]
    mine = [2 * ((chip + d) % chips) + core for d in range(chips)]
    return theirs + mine


def ordered_columns(weight, axis):
    count = lax.axis_size(axis)
    width = weight.shape[1] // count
    return jnp.concatenate(
        [lax.dynamic_slice_in_dim(weight, b * width, width, 1) for b in send_order(axis)], axis=1
    )


def chip_pair_sums(blocks, axis):
    count = lax.axis_size(axis)
    chips = count // 2
    swap = [(i, i ^ 1) for i in range(count)]
    received = lax.ppermute(blocks[:chips], axis, swap)
    return [
        (blocks[chips + d].astype(jnp.float32) + received[d].astype(jnp.float32)).astype(
            jnp.bfloat16
        )
        for d in range(chips)
    ]


def cross_chip_sum(chip_sums, axis):
    count = lax.axis_size(axis)
    chips = count // 2
    total = chip_sums[0].astype(jnp.float32)
    for d in range(1, chips):
        pairs = [(2 * c + k, 2 * ((c + d) % chips) + k) for c in range(chips) for k in range(2)]
        total = total + lax.ppermute(chip_sums[d], axis, pairs).astype(jnp.float32)
    return total.astype(jnp.bfloat16)


def plain_block_sum(blocks, axis):
    count = lax.axis_size(axis)
    total = blocks[0].astype(jnp.float32)
    for shift in range(1, count):
        pairs = [(i, (i + shift) % count) for i in range(count)]
        total = total + lax.ppermute(blocks[shift], axis, pairs).astype(jnp.float32)
    return total.astype(jnp.bfloat16)


def split_three(values):
    hi = values.astype(jnp.bfloat16)
    rest = values - hi.astype(jnp.float32)
    mid = rest.astype(jnp.bfloat16)
    lo = (rest - mid.astype(jnp.float32)).astype(jnp.bfloat16)
    return [hi, mid, lo]


def exchange_rows(payload, axis, rows):
    count = lax.axis_size(axis)
    place = lax.axis_index(axis)
    parts = [lax.dynamic_slice_in_dim(payload, place * rows, rows, 0)]
    for shift in range(1, count):
        pairs = [(i, (i + shift) % count) for i in range(count)]
        block = lax.dynamic_slice_in_dim(payload, ((place + shift) % count) * rows, rows, 0)
        parts.append(lax.ppermute(block, axis, pairs))
    return parts


def per_device(
    frames, latents, lengths, w_query, w_key, w_value, w_out, w_latent_query, w_latent_out
):
    frame_count = frames.shape[0]
    head_width = w_query.shape[1]
    heads_here = head_width // HD
    seq_devices = lax.axis_size("seq")
    seq_place = lax.axis_index("seq")
    first_frame = seq_place * frame_count
    length = lengths[0]
    query = project(frames, w_query)
    keyed = project(frames, w_key)
    valued = project(frames, w_value)
    low, high = halos(keyed, valued, "seq")
    chunks = 2 if frame_count % 512 == 0 else 1
    chunk_rows = frame_count // chunks
    head_devices = lax.axis_size("head")
    paired = head_devices % 2 == 0
    w_ordered = ordered_columns(w_out, "head")
    parts = [
        window_attention(
            query, keyed, valued, low, high, w_ordered, first_frame, length,
            c * chunk_rows, chunk_rows, head_devices,
        )
        for c in range(chunks)
    ]
    latent_count = latents.shape[0]
    latent_query = project(latents, w_latent_query)
    valid_count = jnp.clip(length - first_frame, 0, frame_count)
    frame_parts = []
    if paired:
        first_sums = chip_pair_sums(parts[0], "head")
        first_sums, rest, keyed, valued = lax.optimization_barrier(
            (first_sums, parts[1:], keyed, valued)
        )
        frame_parts.append(cross_chip_sum(first_sums, "head"))
        rest_sums = [chip_pair_sums(blocks, "head") for blocks in rest]
    else:
        frame_parts = [plain_block_sum(blocks, "head") for blocks in parts]
    peaks, totals, local_accum = latent_attention(latent_query, keyed, valued, valid_count)
    payload = jnp.concatenate(
        [local_accum.astype(jnp.bfloat16)] + split_three(jnp.concatenate([peaks, totals], axis=1)),
        axis=1,
    )
    if paired:
        rest_sums, payload = lax.optimization_barrier((rest_sums, payload))
        frame_parts.extend(cross_chip_sum(sums, "head") for sums in rest_sums)
    frames_out = jnp.concatenate(frame_parts, axis=0)
    rows_here = latent_count // seq_devices
    parts = exchange_rows(payload, "seq", rows_here)
    stat_width = 2 * heads_here

    def stats_of(part):
        pieces = [
            part[:, head_width + i * stat_width : head_width + (i + 1) * stat_width].astype(
                jnp.float32
            )
            for i in range(3)
        ]
        return pieces[0] + pieces[1] + pieces[2]

    part_stats = [stats_of(part) for part in parts]
    joint = part_stats[0][:, :heads_here]
    for stat in part_stats[1:]:
        joint = jnp.maximum(joint, stat[:, :heads_here])
    own_total = jnp.zeros_like(joint)
    own_accum = jnp.zeros((rows_here, head_width), jnp.float32)
    for part, stat in zip(parts, part_stats):
        factor = jnp.exp(stat[:, :heads_here] - joint)
        own_total = own_total + stat[:, heads_here:] * factor
        own_accum = own_accum + part[:, :head_width].astype(jnp.float32) * jnp.repeat(
            factor, HD, axis=1
        )
    summary = (own_accum / jnp.repeat(own_total, HD, axis=1)).astype(jnp.bfloat16)
    if paired:
        latent_terms = jnp.dot(
            summary, ordered_columns(w_latent_out, "head"), preferred_element_type=jnp.float32
        ).astype(jnp.bfloat16)
        block_width = latent_terms.shape[1] // head_devices
        latent_blocks = jnp.stack(
            [latent_terms[:, j * block_width : (j + 1) * block_width] for j in range(head_devices)]
        )
        latents_out = cross_chip_sum(chip_pair_sums(latent_blocks, "head"), "head")
    else:
        latent_terms = jnp.dot(summary, w_latent_out, preferred_element_type=jnp.float32)
        latents_out = column_sum(latent_terms.astype(jnp.bfloat16), "head")
    return (frames_out, latents_out)


def solution(mesh):
    return jax.shard_map(
        per_device,
        mesh=mesh,
        in_specs=(
            P(("groups", "seq"), None),
            P(),
            P("groups"),
            P(None, "head"),
            P(None, "head"),
            P(None, "head"),
            P("head", None),
            P(None, "head"),
            P("head", None),
        ),
        out_specs=(P(("groups", "seq"), "head"), P(("groups", "seq"), "head")),
        check_vma=False,
    )
```

```python
import functools

import jax
import jax.numpy as jnp
from jax import lax
from jax.experimental import pallas as pl
from jax.experimental.pallas import tpu as pltpu
from jax.sharding import PartitionSpec as P

HD = 64
HALF = 256
NEG = -1e30


def halos(keyed, valued, axis):
    count = lax.axis_size(axis)
    forward = [(i, i + 1) for i in range(count - 1)]
    backward = [(target, source) for source, target in forward]
    tail = jnp.concatenate([keyed[-HALF:], valued[-HALF:]], axis=1)
    head = jnp.concatenate([keyed[:HALF], valued[:HALF]], axis=1)
    return lax.ppermute(tail, axis, forward), lax.ppermute(head, axis, backward)


def project(source, weight):
    return jnp.dot(source, weight, preferred_element_type=jnp.float32).astype(jnp.bfloat16)


def window_kernel(
    scal_ref, q_ref, k_ref, v_ref, low_ref, high_ref, w_ref, o_ref, kbuf, vbuf, att_ref, *,
    heads, scale
):
    tq = q_ref.shape[0]
    frame_count, width = k_ref.shape
    span = tq + 2 * HALF

    @pl.when(pl.program_id(0) == 0)
    def _fill():
        kbuf[0:HALF, :] = low_ref[:, 0:width]
        vbuf[0:HALF, :] = low_ref[:, width : 2 * width]
        kbuf[HALF : HALF + frame_count, :] = k_ref[...]
        vbuf[HALF : HALF + frame_count, :] = v_ref[...]
        kbuf[HALF + frame_count :, :] = high_ref[:, 0:width]
        vbuf[HALF + frame_count :, :] = high_ref[:, width : 2 * width]

    start = pl.multiple_of(scal_ref[2] + pl.program_id(0) * tq, tq)
    first = scal_ref[0]
    length = scal_ref[1]
    row = lax.broadcasted_iota(jnp.int32, (tq, span), 0)
    col = lax.broadcasted_iota(jnp.int32, (tq, span), 1)
    offset = col - row
    key_pos = first + start - HALF + col
    allowed = (offset >= 0) & (offset <= 2 * HALF) & (key_pos >= 0) & (key_pos < length)
    query_pos = first + start + lax.broadcasted_iota(jnp.int32, (tq, 1), 0)
    query_valid = query_pos < length
    for h in range(heads):
        cols = slice(h * HD, (h + 1) * HD)
        q = q_ref[:, cols]
        k = kbuf[pl.ds(start, span), cols]
        v = vbuf[pl.ds(start, span), cols]
        s = lax.dot_general(
            q, k, (((1,), (1,)), ((), ())), preferred_element_type=jnp.float32
        ) * scale
        masked = jnp.where(allowed, s, NEG)
        peak = jnp.max(masked, axis=1, keepdims=True)
        weights = jnp.exp(masked - peak)
        denom = jnp.sum(weights, axis=1, keepdims=True)
        blended = jnp.dot(weights.astype(jnp.bfloat16), v, preferred_element_type=jnp.float32)
        divisor = jnp.where(query_valid, denom, 1.0)
        att_ref[:, cols] = jnp.where(query_valid, blended / divisor, 0.0).astype(jnp.bfloat16)
    result = jnp.dot(att_ref[...], w_ref[...], preferred_element_type=jnp.float32)
    block_width = o_ref.shape[2]
    for b in range(o_ref.shape[0]):
        o_ref[b] = result[:, b * block_width : (b + 1) * block_width].astype(jnp.bfloat16)


def window_attention(
    query, keyed, valued, low, high, w_out, first_frame, length, row_base, rows, blocks
):
    frame_count, width = query.shape
    out_width = w_out.shape[1]
    block_width = out_width // blocks
    tq = min(256, rows)
    block_base = row_base // tq
    span = tq + 2 * HALF
    scal = jnp.array([0, 0, row_base], jnp.int32).at[0].set(first_frame).at[1].set(length)
    kernel = functools.partial(window_kernel, heads=width // HD, scale=HD ** (-0.5))
    cost = pl.CostEstimate(
        flops=4 * rows * span * width + 2 * rows * width * out_width,
        transcendentals=rows * span * (width // HD),
        bytes_accessed=2 * (2 * query.size + rows * width + 2 * low.size + w_out.size + rows * out_width),
    )
    full = lambda i, s: (0, 0)
    return pl.pallas_call(
        kernel,
        cost_estimate=cost,
        out_shape=jax.ShapeDtypeStruct((blocks, rows, block_width), jnp.bfloat16),
        grid_spec=pltpu.PrefetchScalarGridSpec(
            num_scalar_prefetch=1,
            grid=(rows // tq,),
            in_specs=[
                pl.BlockSpec((tq, width), lambda i, s: (i + block_base, 0)),
                pl.BlockSpec(keyed.shape, full),
                pl.BlockSpec(valued.shape, full),
                pl.BlockSpec(low.shape, full),
                pl.BlockSpec(high.shape, full),
                pl.BlockSpec(w_out.shape, full),
            ],
            out_specs=pl.BlockSpec((blocks, tq, block_width), lambda i, s: (0, i, 0)),
            scratch_shapes=[
                pltpu.VMEM((frame_count + 2 * HALF, width), jnp.bfloat16),
                pltpu.VMEM((frame_count + 2 * HALF, width), jnp.bfloat16),
                pltpu.VMEM((tq, width), jnp.bfloat16),
            ],
        ),
        compiler_params=pltpu.CompilerParams(dimension_semantics=("arbitrary",)),
    )(scal, query, keyed, valued, low, high, w_out)


def latent_kernel(scal_ref, q_ref, k_ref, v_ref, acc_ref, stat_ref, *, heads, scale):
    tl = q_ref.shape[0]
    frame_count = k_ref.shape[0]
    valid = lax.broadcasted_iota(jnp.int32, (tl, frame_count), 1) < scal_ref[0]
    stat_ref[...] = jnp.zeros_like(stat_ref)
    for h in range(heads):
        cols = slice(h * HD, (h + 1) * HD)
        s = lax.dot_general(
            q_ref[:, cols], k_ref[:, cols], (((1,), (1,)), ((), ())),
            preferred_element_type=jnp.float32,
        ) * scale
        masked = jnp.where(valid, s, NEG)
        peak = jnp.max(masked, axis=1, keepdims=True)
        weights = jnp.exp(masked - peak)
        total = jnp.sum(weights, axis=1, keepdims=True)
        acc_ref[:, cols] = jnp.dot(
            weights.astype(jnp.bfloat16), v_ref[:, cols], preferred_element_type=jnp.float32
        )
        stat_ref[:, h : h + 1] = peak
        stat_ref[:, heads + h : heads + h + 1] = total


def latent_attention(latent_query, keyed, valued, valid_count):
    latent_count, width = latent_query.shape
    heads = width // HD
    tl = min(256, latent_count)
    scal = jnp.reshape(valid_count, (1,)).astype(jnp.int32)
    kernel = functools.partial(latent_kernel, heads=heads, scale=HD ** (-0.5))
    frame_count = keyed.shape[0]
    cost = pl.CostEstimate(
        flops=4 * latent_count * frame_count * width,
        transcendentals=latent_count * frame_count * heads,
        bytes_accessed=2 * (latent_query.size + 2 * keyed.size) + 4 * latent_count * (width + 128),
    )
    acc, stat = pl.pallas_call(
        kernel,
        cost_estimate=cost,
        out_shape=(
            jax.ShapeDtypeStruct((latent_count, width), jnp.float32),
            jax.ShapeDtypeStruct((latent_count, 128), jnp.float32),
        ),
        grid_spec=pltpu.PrefetchScalarGridSpec(
            num_scalar_prefetch=1,
            grid=(latent_count // tl,),
            in_specs=[
                pl.BlockSpec((tl, width), lambda i, s: (i, 0)),
                pl.BlockSpec(keyed.shape, lambda i, s: (0, 0)),
                pl.BlockSpec(valued.shape, lambda i, s: (0, 0)),
            ],
            out_specs=[
                pl.BlockSpec((tl, width), lambda i, s: (i, 0)),
                pl.BlockSpec((tl, 128), lambda i, s: (i, 0)),
            ],
        ),
    )(scal, latent_query, keyed, valued)
    return stat[:, :heads], stat[:, heads : 2 * heads], acc


def shifted_blocks(payload, axis, rows):
    count = lax.axis_size(axis)
    place = lax.axis_index(axis)
    own = lax.dynamic_slice_in_dim(payload, place * rows, rows, 0)
    parts = [own]
    for shift in range(1, count):
        target = (place + shift) % count
        block = lax.dynamic_slice_in_dim(payload, target * rows, rows, 0)
        pairs = [(i, (i + shift) % count) for i in range(count)]
        parts.append(lax.ppermute(block, axis, pairs))
    return jnp.stack(parts)


def column_sum(partial, axis):
    count = lax.axis_size(axis)
    place = lax.axis_index(axis)
    width = partial.shape[1] // count
    own = lax.dynamic_slice_in_dim(partial, place * width, width, 1)
    total = own.astype(jnp.float32)
    for shift in range(1, count):
        target = (place + shift) % count
        block = lax.dynamic_slice_in_dim(partial, target * width, width, 1)
        pairs = [(i, (i + shift) % count) for i in range(count)]
        total = total + lax.ppermute(block, axis, pairs).astype(jnp.float32)
    return total.astype(jnp.bfloat16)


def send_order(axis):
    count = lax.axis_size(axis)
    place = lax.axis_index(axis)
    if count % 2 != 0:
        return [(place + j) % count for j in range(count)]
    chips = count // 2
    core = place % 2
    chip = place // 2
    theirs = [2 * ((chip + d) % chips) + 1 - core for d in range(chips)]
    mine = [2 * ((chip + d) % chips) + core for d in range(chips)]
    return theirs + mine


def ordered_columns(weight, axis):
    count = lax.axis_size(axis)
    width = weight.shape[1] // count
    return jnp.concatenate(
        [lax.dynamic_slice_in_dim(weight, b * width, width, 1) for b in send_order(axis)], axis=1
    )


def chip_pair_sums(blocks, axis):
    count = lax.axis_size(axis)
    chips = count // 2
    swap = [(i, i ^ 1) for i in range(count)]
    received = lax.ppermute(blocks[:chips], axis, swap)
    return [
        (blocks[chips + d].astype(jnp.float32) + received[d].astype(jnp.float32)).astype(
            jnp.bfloat16
        )
        for d in range(chips)
    ]


def cross_chip_sum(chip_sums, axis):
    count = lax.axis_size(axis)
    chips = count // 2
    total = chip_sums[0].astype(jnp.float32)
    for d in range(1, chips):
        pairs = [(2 * c + k, 2 * ((c + d) % chips) + k) for c in range(chips) for k in range(2)]
        total = total + lax.ppermute(chip_sums[d], axis, pairs).astype(jnp.float32)
    return total.astype(jnp.bfloat16)


def plain_block_sum(blocks, axis):
    count = lax.axis_size(axis)
    total = blocks[0].astype(jnp.float32)
    for shift in range(1, count):
        pairs = [(i, (i + shift) % count) for i in range(count)]
        total = total + lax.ppermute(blocks[shift], axis, pairs).astype(jnp.float32)
    return total.astype(jnp.bfloat16)


def split_three(values):
    hi = values.astype(jnp.bfloat16)
    rest = values - hi.astype(jnp.float32)
    mid = rest.astype(jnp.bfloat16)
    lo = (rest - mid.astype(jnp.float32)).astype(jnp.bfloat16)
    return [hi, mid, lo]


def exchange_rows(payload, axis, rows):
    count = lax.axis_size(axis)
    place = lax.axis_index(axis)
    parts = [lax.dynamic_slice_in_dim(payload, place * rows, rows, 0)]
    for shift in range(1, count):
        pairs = [(i, (i + shift) % count) for i in range(count)]
        block = lax.dynamic_slice_in_dim(payload, ((place + shift) % count) * rows, rows, 0)
        parts.append(lax.ppermute(block, axis, pairs))
    return parts


def merge_kernel(*refs, heads):
    part_refs, out_ref = refs[:-1], refs[-1]
    width = out_ref.shape[1]
    stat_width = 2 * heads

    def column(ref, c):
        pieces = [
            ref[:, width + i * stat_width + c : width + i * stat_width + c + 1].astype(jnp.float32)
            for i in range(3)
        ]
        return pieces[0] + pieces[1] + pieces[2]

    for h in range(heads):
        peaks = [column(ref, h) for ref in part_refs]
        joint = peaks[0]
        for peak in peaks[1:]:
            joint = jnp.maximum(joint, peak)
        total = jnp.zeros_like(joint)
        accum = jnp.zeros((out_ref.shape[0], HD), jnp.float32)
        for ref, peak in zip(part_refs, peaks):
            factor = jnp.exp(peak - joint)
            total = total + column(ref, heads + h) * factor
            accum = accum + ref[:, h * HD : (h + 1) * HD].astype(jnp.float32) * factor
        out_ref[:, h * HD : (h + 1) * HD] = (accum / total).astype(jnp.bfloat16)


def merge_parts(parts, width, heads):
    rows = parts[0].shape[0]
    return pl.pallas_call(
        functools.partial(merge_kernel, heads=heads),
        out_shape=jax.ShapeDtypeStruct((rows, width), jnp.bfloat16),
        in_specs=[pl.BlockSpec(memory_space=pltpu.VMEM)] * len(parts),
        out_specs=pl.BlockSpec(memory_space=pltpu.VMEM),
    )(*parts)


def per_device(
    frames, latents, lengths, w_query, w_key, w_value, w_out, w_latent_query, w_latent_out
):
    frame_count = frames.shape[0]
    head_width = w_query.shape[1]
    heads_here = head_width // HD
    seq_devices = lax.axis_size("seq")
    seq_place = lax.axis_index("seq")
    first_frame = seq_place * frame_count
    length = lengths[0]
    query = project(frames, w_query)
    keyed = project(frames, w_key)
    valued = project(frames, w_value)
    low, high = halos(keyed, valued, "seq")
    chunks = 2 if frame_count % 512 == 0 else 1
    chunk_rows = frame_count // chunks
    head_devices = lax.axis_size("head")
    paired = head_devices % 2 == 0
    w_ordered = ordered_columns(w_out, "head")
    parts = [
        window_attention(
            query, keyed, valued, low, high, w_ordered, first_frame, length,
            c * chunk_rows, chunk_rows, head_devices,
        )
        for c in range(chunks)
    ]
    latent_count = latents.shape[0]
    latent_query = project(latents, w_latent_query)
    valid_count = jnp.clip(length - first_frame, 0, frame_count)
    frame_parts = []
    if paired:
        first_sums = chip_pair_sums(parts[0], "head")
        first_sums, rest, keyed, valued = lax.optimization_barrier(
            (first_sums, parts[1:], keyed, valued)
        )
        frame_parts.append(cross_chip_sum(first_sums, "head"))
        rest_sums = [chip_pair_sums(blocks, "head") for blocks in rest]
    else:
        frame_parts = [plain_block_sum(blocks, "head") for blocks in parts]
    peaks, totals, local_accum = latent_attention(latent_query, keyed, valued, valid_count)
    payload = jnp.concatenate(
        [local_accum.astype(jnp.bfloat16)] + split_three(jnp.concatenate([peaks, totals], axis=1)),
        axis=1,
    )
    if paired:
        rest_sums, payload = lax.optimization_barrier((rest_sums, payload))
        frame_parts.extend(cross_chip_sum(sums, "head") for sums in rest_sums)
    frames_out = jnp.concatenate(frame_parts, axis=0)
    rows_here = latent_count // seq_devices
    parts = exchange_rows(payload, "seq", rows_here)
    summary = merge_parts(parts, head_width, heads_here)
    if paired:
        latent_terms = jnp.dot(
            summary, ordered_columns(w_latent_out, "head"), preferred_element_type=jnp.float32
        ).astype(jnp.bfloat16)
        block_width = latent_terms.shape[1] // head_devices
        latent_blocks = jnp.stack(
            [latent_terms[:, j * block_width : (j + 1) * block_width] for j in range(head_devices)]
        )
        latents_out = cross_chip_sum(chip_pair_sums(latent_blocks, "head"), "head")
    else:
        latent_terms = jnp.dot(summary, w_latent_out, preferred_element_type=jnp.float32)
        latents_out = column_sum(latent_terms.astype(jnp.bfloat16), "head")
    return (frames_out, latents_out)


def solution(mesh):
    return jax.shard_map(
        per_device,
        mesh=mesh,
        in_specs=(
            P(("groups", "seq"), None),
            P(),
            P("groups"),
            P(None, "head"),
            P(None, "head"),
            P(None, "head"),
            P("head", None),
            P(None, "head"),
            P("head", None),
        ),
        out_specs=(P(("groups", "seq"), "head"), P(("groups", "seq"), "head")),
        check_vma=False,
    )
```

```python
import functools

import jax
import jax.numpy as jnp
from jax import lax
from jax.experimental import pallas as pl
from jax.experimental.pallas import tpu as pltpu
from jax.sharding import PartitionSpec as P

HD = 64
HALF = 256
NEG = -1e30


def halos(keyed, valued, axis):
    count = lax.axis_size(axis)
    forward = [(i, i + 1) for i in range(count - 1)]
    backward = [(target, source) for source, target in forward]
    tail = jnp.concatenate([keyed[-HALF:], valued[-HALF:]], axis=1)
    head = jnp.concatenate([keyed[:HALF], valued[:HALF]], axis=1)
    return lax.ppermute(tail, axis, forward), lax.ppermute(head, axis, backward)


def project(source, weight):
    return jnp.dot(source, weight, preferred_element_type=jnp.float32).astype(jnp.bfloat16)


def window_kernel(
    scal_ref, q_ref, k_ref, v_ref, low_ref, high_ref, w_ref, o_ref, kbuf, vbuf, att_ref, *,
    heads, scale
):
    tq = q_ref.shape[0]
    frame_count, width = k_ref.shape
    span = tq + 2 * HALF

    @pl.when(pl.program_id(0) == 0)
    def _fill():
        kbuf[0:HALF, :] = low_ref[:, 0:width]
        vbuf[0:HALF, :] = low_ref[:, width : 2 * width]
        kbuf[HALF : HALF + frame_count, :] = k_ref[...]
        vbuf[HALF : HALF + frame_count, :] = v_ref[...]
        kbuf[HALF + frame_count :, :] = high_ref[:, 0:width]
        vbuf[HALF + frame_count :, :] = high_ref[:, width : 2 * width]

    start = pl.multiple_of(scal_ref[2] + pl.program_id(0) * tq, tq)
    first = scal_ref[0]
    length = scal_ref[1]
    row = lax.broadcasted_iota(jnp.int32, (tq, span), 0)
    col = lax.broadcasted_iota(jnp.int32, (tq, span), 1)
    offset = col - row
    key_pos = first + start - HALF + col
    allowed = (offset >= 0) & (offset <= 2 * HALF) & (key_pos >= 0) & (key_pos < length)
    query_pos = first + start + lax.broadcasted_iota(jnp.int32, (tq, 1), 0)
    query_valid = query_pos < length
    for h in range(heads):
        cols = slice(h * HD, (h + 1) * HD)
        q = q_ref[:, cols]
        k = kbuf[pl.ds(start, span), cols]
        v = vbuf[pl.ds(start, span), cols]
        s = lax.dot_general(
            q, k, (((1,), (1,)), ((), ())), preferred_element_type=jnp.float32
        ) * scale
        masked = jnp.where(allowed, s, NEG)
        peak = jnp.max(masked, axis=1, keepdims=True)
        weights = jnp.exp(masked - peak)
        denom = jnp.sum(weights, axis=1, keepdims=True)
        blended = jnp.dot(weights.astype(jnp.bfloat16), v, preferred_element_type=jnp.float32)
        divisor = jnp.where(query_valid, denom, 1.0)
        att_ref[:, cols] = jnp.where(query_valid, blended / divisor, 0.0).astype(jnp.bfloat16)
    result = jnp.dot(att_ref[...], w_ref[...], preferred_element_type=jnp.float32)
    block_width = o_ref.shape[2]
    for b in range(o_ref.shape[0]):
        o_ref[b] = result[:, b * block_width : (b + 1) * block_width].astype(jnp.bfloat16)


def window_attention(
    query, keyed, valued, low, high, w_out, first_frame, length, row_base, rows, blocks
):
    frame_count, width = query.shape
    out_width = w_out.shape[1]
    block_width = out_width // blocks
    tq = min(256, rows)
    block_base = row_base // tq
    span = tq + 2 * HALF
    scal = jnp.array([0, 0, row_base], jnp.int32).at[0].set(first_frame).at[1].set(length)
    kernel = functools.partial(window_kernel, heads=width // HD, scale=HD ** (-0.5))
    cost = pl.CostEstimate(
        flops=4 * rows * span * width + 2 * rows * width * out_width,
        transcendentals=rows * span * (width // HD),
        bytes_accessed=2 * (2 * query.size + rows * width + 2 * low.size + w_out.size + rows * out_width),
    )
    full = lambda i, s: (0, 0)
    return pl.pallas_call(
        kernel,
        cost_estimate=cost,
        out_shape=jax.ShapeDtypeStruct((blocks, rows, block_width), jnp.bfloat16),
        grid_spec=pltpu.PrefetchScalarGridSpec(
            num_scalar_prefetch=1,
            grid=(rows // tq,),
            in_specs=[
                pl.BlockSpec((tq, width), lambda i, s: (i + block_base, 0)),
                pl.BlockSpec(keyed.shape, full),
                pl.BlockSpec(valued.shape, full),
                pl.BlockSpec(low.shape, full),
                pl.BlockSpec(high.shape, full),
                pl.BlockSpec(w_out.shape, full),
            ],
            out_specs=pl.BlockSpec((blocks, tq, block_width), lambda i, s: (0, i, 0)),
            scratch_shapes=[
                pltpu.VMEM((frame_count + 2 * HALF, width), jnp.bfloat16),
                pltpu.VMEM((frame_count + 2 * HALF, width), jnp.bfloat16),
                pltpu.VMEM((tq, width), jnp.bfloat16),
            ],
        ),
        compiler_params=pltpu.CompilerParams(dimension_semantics=("arbitrary",)),
    )(scal, query, keyed, valued, low, high, w_out)


def latent_kernel(scal_ref, q_ref, k_ref, v_ref, acc_ref, stat_ref, *, heads, scale):
    tl = q_ref.shape[0]
    frame_count = k_ref.shape[0]
    valid = lax.broadcasted_iota(jnp.int32, (tl, frame_count), 1) < scal_ref[0]
    stat_ref[...] = jnp.zeros_like(stat_ref)
    for h in range(heads):
        cols = slice(h * HD, (h + 1) * HD)
        s = lax.dot_general(
            q_ref[:, cols], k_ref[:, cols], (((1,), (1,)), ((), ())),
            preferred_element_type=jnp.float32,
        ) * scale
        masked = jnp.where(valid, s, NEG)
        peak = jnp.max(masked, axis=1, keepdims=True)
        weights = jnp.exp(masked - peak)
        total = jnp.sum(weights, axis=1, keepdims=True)
        acc_ref[:, cols] = jnp.dot(
            weights.astype(jnp.bfloat16), v_ref[:, cols], preferred_element_type=jnp.float32
        )
        stat_ref[:, h : h + 1] = peak
        stat_ref[:, heads + h : heads + h + 1] = total


def latent_attention(latent_query, keyed, valued, valid_count):
    latent_count, width = latent_query.shape
    heads = width // HD
    tl = min(256, latent_count)
    scal = jnp.reshape(valid_count, (1,)).astype(jnp.int32)
    kernel = functools.partial(latent_kernel, heads=heads, scale=HD ** (-0.5))
    frame_count = keyed.shape[0]
    cost = pl.CostEstimate(
        flops=4 * latent_count * frame_count * width,
        transcendentals=latent_count * frame_count * heads,
        bytes_accessed=2 * (latent_query.size + 2 * keyed.size) + 4 * latent_count * (width + 128),
    )
    acc, stat = pl.pallas_call(
        kernel,
        cost_estimate=cost,
        out_shape=(
            jax.ShapeDtypeStruct((latent_count, width), jnp.float32),
            jax.ShapeDtypeStruct((latent_count, 128), jnp.float32),
        ),
        grid_spec=pltpu.PrefetchScalarGridSpec(
            num_scalar_prefetch=1,
            grid=(latent_count // tl,),
            in_specs=[
                pl.BlockSpec((tl, width), lambda i, s: (i, 0)),
                pl.BlockSpec(keyed.shape, lambda i, s: (0, 0)),
                pl.BlockSpec(valued.shape, lambda i, s: (0, 0)),
            ],
            out_specs=[
                pl.BlockSpec((tl, width), lambda i, s: (i, 0)),
                pl.BlockSpec((tl, 128), lambda i, s: (i, 0)),
            ],
        ),
    )(scal, latent_query, keyed, valued)
    return stat[:, :heads], stat[:, heads : 2 * heads], acc


def shifted_blocks(payload, axis, rows):
    count = lax.axis_size(axis)
    place = lax.axis_index(axis)
    own = lax.dynamic_slice_in_dim(payload, place * rows, rows, 0)
    parts = [own]
    for shift in range(1, count):
        target = (place + shift) % count
        block = lax.dynamic_slice_in_dim(payload, target * rows, rows, 0)
        pairs = [(i, (i + shift) % count) for i in range(count)]
        parts.append(lax.ppermute(block, axis, pairs))
    return jnp.stack(parts)


def column_sum(partial, axis):
    count = lax.axis_size(axis)
    place = lax.axis_index(axis)
    width = partial.shape[1] // count
    own = lax.dynamic_slice_in_dim(partial, place * width, width, 1)
    total = own.astype(jnp.float32)
    for shift in range(1, count):
        target = (place + shift) % count
        block = lax.dynamic_slice_in_dim(partial, target * width, width, 1)
        pairs = [(i, (i + shift) % count) for i in range(count)]
        total = total + lax.ppermute(block, axis, pairs).astype(jnp.float32)
    return total.astype(jnp.bfloat16)


def send_order(axis):
    count = lax.axis_size(axis)
    place = lax.axis_index(axis)
    if count % 2 != 0:
        return [(place + j) % count for j in range(count)]
    chips = count // 2
    core = place % 2
    chip = place // 2
    theirs = [2 * ((chip + d) % chips) + 1 - core for d in range(chips)]
    mine = [2 * ((chip + d) % chips) + core for d in range(chips)]
    return theirs + mine


def ordered_columns(weight, axis):
    count = lax.axis_size(axis)
    width = weight.shape[1] // count
    return jnp.concatenate(
        [lax.dynamic_slice_in_dim(weight, b * width, width, 1) for b in send_order(axis)], axis=1
    )


def chip_pair_sums(blocks, axis):
    count = lax.axis_size(axis)
    chips = count // 2
    swap = [(i, i ^ 1) for i in range(count)]
    received = lax.ppermute(blocks[:chips], axis, swap)
    return [
        (blocks[chips + d].astype(jnp.float32) + received[d].astype(jnp.float32)).astype(
            jnp.bfloat16
        )
        for d in range(chips)
    ]


def cross_chip_sum(chip_sums, axis):
    count = lax.axis_size(axis)
    chips = count // 2
    total = chip_sums[0].astype(jnp.float32)
    for d in range(1, chips):
        pairs = [(2 * c + k, 2 * ((c + d) % chips) + k) for c in range(chips) for k in range(2)]
        total = total + lax.ppermute(chip_sums[d], axis, pairs).astype(jnp.float32)
    return total.astype(jnp.bfloat16)


def plain_block_sum(blocks, axis):
    count = lax.axis_size(axis)
    total = blocks[0].astype(jnp.float32)
    for shift in range(1, count):
        pairs = [(i, (i + shift) % count) for i in range(count)]
        total = total + lax.ppermute(blocks[shift], axis, pairs).astype(jnp.float32)
    return total.astype(jnp.bfloat16)


def split_three(values):
    hi = values.astype(jnp.bfloat16)
    rest = values - hi.astype(jnp.float32)
    mid = rest.astype(jnp.bfloat16)
    lo = (rest - mid.astype(jnp.float32)).astype(jnp.bfloat16)
    return [hi, mid, lo]


def exchange_rows(payload, axis, rows):
    count = lax.axis_size(axis)
    place = lax.axis_index(axis)
    parts = [lax.dynamic_slice_in_dim(payload, place * rows, rows, 0)]
    for shift in range(1, count):
        pairs = [(i, (i + shift) % count) for i in range(count)]
        block = lax.dynamic_slice_in_dim(payload, ((place + shift) % count) * rows, rows, 0)
        parts.append(lax.ppermute(block, axis, pairs))
    return parts


def merge_kernel(*refs, heads):
    part_refs, out_ref = refs[:-1], refs[-1]
    width = out_ref.shape[1]
    stat_width = 2 * heads

    def column(ref, c):
        pieces = [
            ref[:, width + i * stat_width + c : width + i * stat_width + c + 1].astype(jnp.float32)
            for i in range(3)
        ]
        return pieces[0] + pieces[1] + pieces[2]

    for h in range(heads):
        peaks = [column(ref, h) for ref in part_refs]
        joint = peaks[0]
        for peak in peaks[1:]:
            joint = jnp.maximum(joint, peak)
        total = jnp.zeros_like(joint)
        accum = jnp.zeros((out_ref.shape[0], HD), jnp.float32)
        for ref, peak in zip(part_refs, peaks):
            factor = jnp.exp(peak - joint)
            total = total + column(ref, heads + h) * factor
            accum = accum + ref[:, h * HD : (h + 1) * HD].astype(jnp.float32) * factor
        out_ref[:, h * HD : (h + 1) * HD] = (accum / total).astype(jnp.bfloat16)


def merge_parts(parts, width, heads):
    rows = parts[0].shape[0]
    return pl.pallas_call(
        functools.partial(merge_kernel, heads=heads),
        out_shape=jax.ShapeDtypeStruct((rows, width), jnp.bfloat16),
        in_specs=[pl.BlockSpec(memory_space=pltpu.VMEM)] * len(parts),
        out_specs=pl.BlockSpec(memory_space=pltpu.VMEM),
    )(*parts)


def per_device(
    frames, latents, lengths, w_query, w_key, w_value, w_out, w_latent_query, w_latent_out
):
    frame_count = frames.shape[0]
    head_width = w_query.shape[1]
    heads_here = head_width // HD
    seq_devices = lax.axis_size("seq")
    seq_place = lax.axis_index("seq")
    first_frame = seq_place * frame_count
    length = lengths[0]
    query = project(frames, w_query)
    keyed = project(frames, w_key)
    valued = project(frames, w_value)
    low, high = halos(keyed, valued, "seq")
    chunks = 2 if frame_count % 512 == 0 else 1
    chunk_rows = frame_count // chunks
    head_devices = lax.axis_size("head")
    paired = head_devices % 2 == 0
    w_ordered = ordered_columns(w_out, "head")
    def window_chunk(c, query, keyed, valued, low, high):
        return window_attention(
            query, keyed, valued, low, high, w_ordered, first_frame, length,
            c * chunk_rows, chunk_rows, head_devices,
        )

    latent_count = latents.shape[0]
    latent_query = project(latents, w_latent_query)
    valid_count = jnp.clip(length - first_frame, 0, frame_count)
    if paired and chunks == 2:
        first = window_chunk(0, query, keyed, valued, low, high)
        first_sums = chip_pair_sums(first, "head")
        first_sums, query, keyed, valued, low, high = lax.optimization_barrier(
            (first_sums, query, keyed, valued, low, high)
        )
        first_out = cross_chip_sum(first_sums, "head")
        second = window_chunk(1, query, keyed, valued, low, high)
        rest_sums = [chip_pair_sums(second, "head")]
        first_out, keyed, valued = lax.optimization_barrier((first_out, keyed, valued))
        frame_parts = [first_out]
    else:
        parts = [window_chunk(c, query, keyed, valued, low, high) for c in range(chunks)]
        if paired:
            rest_sums = [chip_pair_sums(blocks, "head") for blocks in parts]
            frame_parts = []
        else:
            frame_parts = [plain_block_sum(blocks, "head") for blocks in parts]
    peaks, totals, local_accum = latent_attention(latent_query, keyed, valued, valid_count)
    payload = jnp.concatenate(
        [local_accum.astype(jnp.bfloat16)] + split_three(jnp.concatenate([peaks, totals], axis=1)),
        axis=1,
    )
    if paired:
        rest_sums, payload = lax.optimization_barrier((rest_sums, payload))
        frame_parts.extend(cross_chip_sum(sums, "head") for sums in rest_sums)
    frames_out = jnp.concatenate(frame_parts, axis=0)
    rows_here = latent_count // seq_devices
    parts = exchange_rows(payload, "seq", rows_here)
    summary = merge_parts(parts, head_width, heads_here)
    if paired:
        latent_terms = jnp.dot(
            summary, ordered_columns(w_latent_out, "head"), preferred_element_type=jnp.float32
        ).astype(jnp.bfloat16)
        block_width = latent_terms.shape[1] // head_devices
        latent_blocks = jnp.stack(
            [latent_terms[:, j * block_width : (j + 1) * block_width] for j in range(head_devices)]
        )
        latents_out = cross_chip_sum(chip_pair_sums(latent_blocks, "head"), "head")
    else:
        latent_terms = jnp.dot(summary, w_latent_out, preferred_element_type=jnp.float32)
        latents_out = column_sum(latent_terms.astype(jnp.bfloat16), "head")
    return (frames_out, latents_out)


def solution(mesh):
    return jax.shard_map(
        per_device,
        mesh=mesh,
        in_specs=(
            P(("groups", "seq"), None),
            P(),
            P("groups"),
            P(None, "head"),
            P(None, "head"),
            P(None, "head"),
            P("head", None),
            P(None, "head"),
            P("head", None),
        ),
        out_specs=(P(("groups", "seq"), "head"), P(("groups", "seq"), "head")),
        check_vma=False,
    )
```

```python
import functools

import jax
import jax.numpy as jnp
from jax import lax
from jax.experimental import pallas as pl
from jax.experimental.pallas import tpu as pltpu
from jax.sharding import PartitionSpec as P

HD = 64
HALF = 256
NEG = -1e30


def halos(keyed, valued, axis):
    count = lax.axis_size(axis)
    forward = [(i, i + 1) for i in range(count - 1)]
    backward = [(target, source) for source, target in forward]
    tail = jnp.concatenate([keyed[-HALF:], valued[-HALF:]], axis=1)
    head = jnp.concatenate([keyed[:HALF], valued[:HALF]], axis=1)
    return lax.ppermute(tail, axis, forward), lax.ppermute(head, axis, backward)


def project(source, weight):
    return jnp.dot(source, weight, preferred_element_type=jnp.float32).astype(jnp.bfloat16)


def window_kernel(
    scal_ref, q_ref, k_ref, v_ref, low_ref, high_ref, w_ref, o_ref, kbuf, vbuf, att_ref, *,
    heads, scale
):
    tq = q_ref.shape[0]
    frame_count, width = k_ref.shape
    span = tq + 2 * HALF

    @pl.when(pl.program_id(0) == 0)
    def _fill():
        kbuf[0:HALF, :] = low_ref[:, 0:width]
        vbuf[0:HALF, :] = low_ref[:, width : 2 * width]
        kbuf[HALF : HALF + frame_count, :] = k_ref[...]
        vbuf[HALF : HALF + frame_count, :] = v_ref[...]
        kbuf[HALF + frame_count :, :] = high_ref[:, 0:width]
        vbuf[HALF + frame_count :, :] = high_ref[:, width : 2 * width]

    start = pl.multiple_of(scal_ref[2] + pl.program_id(0) * tq, tq)
    first = scal_ref[0]
    length = scal_ref[1]
    row = lax.broadcasted_iota(jnp.int32, (tq, span), 0)
    col = lax.broadcasted_iota(jnp.int32, (tq, span), 1)
    offset = col - row
    key_pos = first + start - HALF + col
    allowed = (offset >= 0) & (offset <= 2 * HALF) & (key_pos >= 0) & (key_pos < length)
    query_pos = first + start + lax.broadcasted_iota(jnp.int32, (tq, 1), 0)
    query_valid = query_pos < length
    for h in range(heads):
        cols = slice(h * HD, (h + 1) * HD)
        q = q_ref[:, cols]
        k = kbuf[pl.ds(start, span), cols]
        v = vbuf[pl.ds(start, span), cols]
        s = lax.dot_general(
            q, k, (((1,), (1,)), ((), ())), preferred_element_type=jnp.float32
        ) * scale
        masked = jnp.where(allowed, s, NEG)
        peak = jnp.max(masked, axis=1, keepdims=True)
        weights = jnp.exp(masked - peak)
        denom = jnp.sum(weights, axis=1, keepdims=True)
        blended = jnp.dot(weights.astype(jnp.bfloat16), v, preferred_element_type=jnp.float32)
        divisor = jnp.where(query_valid, denom, 1.0)
        att_ref[:, cols] = jnp.where(query_valid, blended / divisor, 0.0).astype(jnp.bfloat16)
    result = jnp.dot(att_ref[...], w_ref[...], preferred_element_type=jnp.float32)
    block_width = o_ref.shape[2]
    for b in range(o_ref.shape[0]):
        o_ref[b] = result[:, b * block_width : (b + 1) * block_width].astype(jnp.bfloat16)


def window_attention(
    query, keyed, valued, low, high, w_out, first_frame, length, row_base, rows, blocks
):
    frame_count, width = query.shape
    out_width = w_out.shape[1]
    block_width = out_width // blocks
    tq = min(128, rows)
    block_base = row_base // tq
    span = tq + 2 * HALF
    scal = jnp.array([0, 0, row_base], jnp.int32).at[0].set(first_frame).at[1].set(length)
    kernel = functools.partial(window_kernel, heads=width // HD, scale=HD ** (-0.5))
    cost = pl.CostEstimate(
        flops=4 * rows * span * width + 2 * rows * width * out_width,
        transcendentals=rows * span * (width // HD),
        bytes_accessed=2 * (2 * query.size + rows * width + 2 * low.size + w_out.size + rows * out_width),
    )
    full = lambda i, s: (0, 0)
    return pl.pallas_call(
        kernel,
        cost_estimate=cost,
        out_shape=jax.ShapeDtypeStruct((blocks, rows, block_width), jnp.bfloat16),
        grid_spec=pltpu.PrefetchScalarGridSpec(
            num_scalar_prefetch=1,
            grid=(rows // tq,),
            in_specs=[
                pl.BlockSpec((tq, width), lambda i, s: (i + block_base, 0)),
                pl.BlockSpec(keyed.shape, full),
                pl.BlockSpec(valued.shape, full),
                pl.BlockSpec(low.shape, full),
                pl.BlockSpec(high.shape, full),
                pl.BlockSpec(w_out.shape, full),
            ],
            out_specs=pl.BlockSpec((blocks, tq, block_width), lambda i, s: (0, i, 0)),
            scratch_shapes=[
                pltpu.VMEM((frame_count + 2 * HALF, width), jnp.bfloat16),
                pltpu.VMEM((frame_count + 2 * HALF, width), jnp.bfloat16),
                pltpu.VMEM((tq, width), jnp.bfloat16),
            ],
        ),
        compiler_params=pltpu.CompilerParams(dimension_semantics=("arbitrary",)),
    )(scal, query, keyed, valued, low, high, w_out)


def latent_kernel(scal_ref, q_ref, k_ref, v_ref, acc_ref, stat_ref, *, heads, scale):
    tl = q_ref.shape[0]
    frame_count = k_ref.shape[0]
    valid = lax.broadcasted_iota(jnp.int32, (tl, frame_count), 1) < scal_ref[0]
    stat_ref[...] = jnp.zeros_like(stat_ref)
    for h in range(heads):
        cols = slice(h * HD, (h + 1) * HD)
        s = lax.dot_general(
            q_ref[:, cols], k_ref[:, cols], (((1,), (1,)), ((), ())),
            preferred_element_type=jnp.float32,
        ) * scale
        masked = jnp.where(valid, s, NEG)
        peak = jnp.max(masked, axis=1, keepdims=True)
        weights = jnp.exp(masked - peak)
        total = jnp.sum(weights, axis=1, keepdims=True)
        acc_ref[:, cols] = jnp.dot(
            weights.astype(jnp.bfloat16), v_ref[:, cols], preferred_element_type=jnp.float32
        )
        stat_ref[:, h : h + 1] = peak
        stat_ref[:, heads + h : heads + h + 1] = total


def latent_attention(latent_query, keyed, valued, valid_count):
    latent_count, width = latent_query.shape
    heads = width // HD
    tl = min(256, latent_count)
    scal = jnp.reshape(valid_count, (1,)).astype(jnp.int32)
    kernel = functools.partial(latent_kernel, heads=heads, scale=HD ** (-0.5))
    frame_count = keyed.shape[0]
    cost = pl.CostEstimate(
        flops=4 * latent_count * frame_count * width,
        transcendentals=latent_count * frame_count * heads,
        bytes_accessed=2 * (latent_query.size + 2 * keyed.size) + 4 * latent_count * (width + 128),
    )
    acc, stat = pl.pallas_call(
        kernel,
        cost_estimate=cost,
        out_shape=(
            jax.ShapeDtypeStruct((latent_count, width), jnp.float32),
            jax.ShapeDtypeStruct((latent_count, 128), jnp.float32),
        ),
        grid_spec=pltpu.PrefetchScalarGridSpec(
            num_scalar_prefetch=1,
            grid=(latent_count // tl,),
            in_specs=[
                pl.BlockSpec((tl, width), lambda i, s: (i, 0)),
                pl.BlockSpec(keyed.shape, lambda i, s: (0, 0)),
                pl.BlockSpec(valued.shape, lambda i, s: (0, 0)),
            ],
            out_specs=[
                pl.BlockSpec((tl, width), lambda i, s: (i, 0)),
                pl.BlockSpec((tl, 128), lambda i, s: (i, 0)),
            ],
        ),
    )(scal, latent_query, keyed, valued)
    return stat[:, :heads], stat[:, heads : 2 * heads], acc


def shifted_blocks(payload, axis, rows):
    count = lax.axis_size(axis)
    place = lax.axis_index(axis)
    own = lax.dynamic_slice_in_dim(payload, place * rows, rows, 0)
    parts = [own]
    for shift in range(1, count):
        target = (place + shift) % count
        block = lax.dynamic_slice_in_dim(payload, target * rows, rows, 0)
        pairs = [(i, (i + shift) % count) for i in range(count)]
        parts.append(lax.ppermute(block, axis, pairs))
    return jnp.stack(parts)


def column_sum(partial, axis):
    count = lax.axis_size(axis)
    place = lax.axis_index(axis)
    width = partial.shape[1] // count
    own = lax.dynamic_slice_in_dim(partial, place * width, width, 1)
    total = own.astype(jnp.float32)
    for shift in range(1, count):
        target = (place + shift) % count
        block = lax.dynamic_slice_in_dim(partial, target * width, width, 1)
        pairs = [(i, (i + shift) % count) for i in range(count)]
        total = total + lax.ppermute(block, axis, pairs).astype(jnp.float32)
    return total.astype(jnp.bfloat16)


def send_order(axis):
    count = lax.axis_size(axis)
    place = lax.axis_index(axis)
    if count % 2 != 0:
        return [(place + j) % count for j in range(count)]
    chips = count // 2
    core = place % 2
    chip = place // 2
    theirs = [2 * ((chip + d) % chips) + 1 - core for d in range(chips)]
    mine = [2 * ((chip + d) % chips) + core for d in range(chips)]
    return theirs + mine


def ordered_columns(weight, axis):
    count = lax.axis_size(axis)
    width = weight.shape[1] // count
    return jnp.concatenate(
        [lax.dynamic_slice_in_dim(weight, b * width, width, 1) for b in send_order(axis)], axis=1
    )


def chip_pair_sums(blocks, axis):
    count = lax.axis_size(axis)
    chips = count // 2
    swap = [(i, i ^ 1) for i in range(count)]
    received = lax.ppermute(blocks[:chips], axis, swap)
    return [
        (blocks[chips + d].astype(jnp.float32) + received[d].astype(jnp.float32)).astype(
            jnp.bfloat16
        )
        for d in range(chips)
    ]


def cross_chip_sum(chip_sums, axis):
    count = lax.axis_size(axis)
    chips = count // 2
    total = chip_sums[0].astype(jnp.float32)
    for d in range(1, chips):
        pairs = [(2 * c + k, 2 * ((c + d) % chips) + k) for c in range(chips) for k in range(2)]
        total = total + lax.ppermute(chip_sums[d], axis, pairs).astype(jnp.float32)
    return total.astype(jnp.bfloat16)


def plain_block_sum(blocks, axis):
    count = lax.axis_size(axis)
    total = blocks[0].astype(jnp.float32)
    for shift in range(1, count):
        pairs = [(i, (i + shift) % count) for i in range(count)]
        total = total + lax.ppermute(blocks[shift], axis, pairs).astype(jnp.float32)
    return total.astype(jnp.bfloat16)


def split_three(values):
    hi = values.astype(jnp.bfloat16)
    rest = values - hi.astype(jnp.float32)
    mid = rest.astype(jnp.bfloat16)
    lo = (rest - mid.astype(jnp.float32)).astype(jnp.bfloat16)
    return [hi, mid, lo]


def exchange_rows(payload, axis, rows):
    count = lax.axis_size(axis)
    place = lax.axis_index(axis)
    parts = [lax.dynamic_slice_in_dim(payload, place * rows, rows, 0)]
    for shift in range(1, count):
        pairs = [(i, (i + shift) % count) for i in range(count)]
        block = lax.dynamic_slice_in_dim(payload, ((place + shift) % count) * rows, rows, 0)
        parts.append(lax.ppermute(block, axis, pairs))
    return parts


def merge_kernel(*refs, heads):
    part_refs, out_ref = refs[:-1], refs[-1]
    width = out_ref.shape[1]
    stat_width = 2 * heads

    stat_blocks = []
    for ref in part_refs:
        raw = ref[:, width : width + 3 * stat_width].astype(jnp.float32)
        stat_blocks.append(
            raw[:, 0:stat_width]
            + raw[:, stat_width : 2 * stat_width]
            + raw[:, 2 * stat_width : 3 * stat_width]
        )

    def column(k, c):
        return stat_blocks[k][:, c : c + 1]

    for h in range(heads):
        peaks = [column(k, h) for k in range(len(part_refs))]
        joint = peaks[0]
        for peak in peaks[1:]:
            joint = jnp.maximum(joint, peak)
        total = jnp.zeros_like(joint)
        accum = jnp.zeros((out_ref.shape[0], HD), jnp.float32)
        for k, (ref, peak) in enumerate(zip(part_refs, peaks)):
            factor = jnp.exp(peak - joint)
            total = total + column(k, heads + h) * factor
            accum = accum + ref[:, h * HD : (h + 1) * HD].astype(jnp.float32) * factor
        out_ref[:, h * HD : (h + 1) * HD] = (accum / total).astype(jnp.bfloat16)


def merge_parts(parts, width, heads):
    rows = parts[0].shape[0]
    return pl.pallas_call(
        functools.partial(merge_kernel, heads=heads),
        out_shape=jax.ShapeDtypeStruct((rows, width), jnp.bfloat16),
        in_specs=[pl.BlockSpec(memory_space=pltpu.VMEM)] * len(parts),
        out_specs=pl.BlockSpec(memory_space=pltpu.VMEM),
    )(*parts)


def per_device(
    frames, latents, lengths, w_query, w_key, w_value, w_out, w_latent_query, w_latent_out
):
    frame_count = frames.shape[0]
    head_width = w_query.shape[1]
    heads_here = head_width // HD
    seq_devices = lax.axis_size("seq")
    seq_place = lax.axis_index("seq")
    first_frame = seq_place * frame_count
    length = lengths[0]
    query = project(frames, w_query)
    keyed = project(frames, w_key)
    valued = project(frames, w_value)
    low, high = halos(keyed, valued, "seq")
    chunks = 2 if frame_count % 512 == 0 else 1
    chunk_rows = frame_count // chunks
    head_devices = lax.axis_size("head")
    paired = head_devices % 2 == 0
    w_ordered = ordered_columns(w_out, "head")
    parts = [
        window_attention(
            query, keyed, valued, low, high, w_ordered, first_frame, length,
            c * chunk_rows, chunk_rows, head_devices,
        )
        for c in range(chunks)
    ]
    latent_count = latents.shape[0]
    latent_query = project(latents, w_latent_query)
    valid_count = jnp.clip(length - first_frame, 0, frame_count)
    frame_parts = []
    if paired:
        first_sums = chip_pair_sums(parts[0], "head")
        first_sums, rest, keyed, valued = lax.optimization_barrier(
            (first_sums, parts[1:], keyed, valued)
        )
        frame_parts.append(cross_chip_sum(first_sums, "head"))
        rest_sums = [chip_pair_sums(blocks, "head") for blocks in rest]
    else:
        frame_parts = [plain_block_sum(blocks, "head") for blocks in parts]
    peaks, totals, local_accum = latent_attention(latent_query, keyed, valued, valid_count)
    payload = jnp.concatenate(
        [local_accum.astype(jnp.bfloat16)] + split_three(jnp.concatenate([peaks, totals], axis=1)),
        axis=1,
    )
    if paired:
        rest_sums, payload = lax.optimization_barrier((rest_sums, payload))
        frame_parts.extend(cross_chip_sum(sums, "head") for sums in rest_sums)
    frames_out = jnp.concatenate(frame_parts, axis=0)
    rows_here = latent_count // seq_devices
    parts = exchange_rows(payload, "seq", rows_here)
    summary = merge_parts(parts, head_width, heads_here)
    if paired:
        latent_terms = jnp.dot(
            summary, ordered_columns(w_latent_out, "head"), preferred_element_type=jnp.float32
        ).astype(jnp.bfloat16)
        block_width = latent_terms.shape[1] // head_devices
        latent_blocks = jnp.stack(
            [latent_terms[:, j * block_width : (j + 1) * block_width] for j in range(head_devices)]
        )
        latents_out = cross_chip_sum(chip_pair_sums(latent_blocks, "head"), "head")
    else:
        latent_terms = jnp.dot(summary, w_latent_out, preferred_element_type=jnp.float32)
        latents_out = column_sum(latent_terms.astype(jnp.bfloat16), "head")
    return (frames_out, latents_out)


def solution(mesh):
    return jax.shard_map(
        per_device,
        mesh=mesh,
        in_specs=(
            P(("groups", "seq"), None),
            P(),
            P("groups"),
            P(None, "head"),
            P(None, "head"),
            P(None, "head"),
            P("head", None),
            P(None, "head"),
            P("head", None),
        ),
        out_specs=(P(("groups", "seq"), "head"), P(("groups", "seq"), "head")),
        check_vma=False,
    )
```

```python
import functools

import jax
import jax.numpy as jnp
from jax import lax
from jax.experimental import pallas as pl
from jax.experimental.pallas import tpu as pltpu
from jax.sharding import PartitionSpec as P

HD = 64
HALF = 256
NEG = -1e30


def halos(keyed, valued, axis):
    count = lax.axis_size(axis)
    forward = [(i, i + 1) for i in range(count - 1)]
    backward = [(target, source) for source, target in forward]
    tail = jnp.concatenate([keyed[-HALF:], valued[-HALF:]], axis=1)
    head = jnp.concatenate([keyed[:HALF], valued[:HALF]], axis=1)
    return lax.ppermute(tail, axis, forward), lax.ppermute(head, axis, backward)


def project(source, weight):
    return jnp.dot(source, weight, preferred_element_type=jnp.float32).astype(jnp.bfloat16)


def window_kernel(
    scal_ref, q_ref, k_ref, v_ref, low_ref, high_ref, w_ref, o_ref, kbuf, vbuf, att_ref, *,
    heads, scale
):
    tq = q_ref.shape[0]
    frame_count, width = k_ref.shape
    span = tq + 2 * HALF

    @pl.when(pl.program_id(0) == 0)
    def _fill():
        kbuf[0:HALF, :] = low_ref[:, 0:width]
        vbuf[0:HALF, :] = low_ref[:, width : 2 * width]
        kbuf[HALF : HALF + frame_count, :] = k_ref[...]
        vbuf[HALF : HALF + frame_count, :] = v_ref[...]
        kbuf[HALF + frame_count :, :] = high_ref[:, 0:width]
        vbuf[HALF + frame_count :, :] = high_ref[:, width : 2 * width]

    start = pl.multiple_of(scal_ref[2] + pl.program_id(0) * tq, tq)
    first = scal_ref[0]
    length = scal_ref[1]
    row = lax.broadcasted_iota(jnp.int32, (tq, span), 0)
    col = lax.broadcasted_iota(jnp.int32, (tq, span), 1)
    offset = col - row
    key_pos = first + start - HALF + col
    allowed = (offset >= 0) & (offset <= 2 * HALF) & (key_pos >= 0) & (key_pos < length)
    query_pos = first + start + lax.broadcasted_iota(jnp.int32, (tq, 1), 0)
    query_valid = query_pos < length
    for h in range(heads):
        cols = slice(h * HD, (h + 1) * HD)
        q = q_ref[:, cols]
        k = kbuf[pl.ds(start, span), cols]
        v = vbuf[pl.ds(start, span), cols]
        s = lax.dot_general(
            q, k, (((1,), (1,)), ((), ())), preferred_element_type=jnp.float32
        ) * scale
        masked = jnp.where(allowed, s, NEG)
        peak = jnp.max(masked, axis=1, keepdims=True)
        weights = jnp.exp(masked - peak)
        denom = jnp.sum(weights, axis=1, keepdims=True)
        blended = jnp.dot(weights.astype(jnp.bfloat16), v, preferred_element_type=jnp.float32)
        divisor = jnp.where(query_valid, denom, 1.0)
        att_ref[:, cols] = jnp.where(query_valid, blended / divisor, 0.0).astype(jnp.bfloat16)
    result = jnp.dot(att_ref[...], w_ref[...], preferred_element_type=jnp.float32)
    block_width = o_ref.shape[2]
    for b in range(o_ref.shape[0]):
        o_ref[b] = result[:, b * block_width : (b + 1) * block_width].astype(jnp.bfloat16)


def window_attention(
    query, keyed, valued, low, high, w_out, first_frame, length, row_base, rows, blocks
):
    frame_count, width = query.shape
    out_width = w_out.shape[1]
    block_width = out_width // blocks
    tq = min(256, rows)
    block_base = row_base // tq
    span = tq + 2 * HALF
    scal = jnp.array([0, 0, row_base], jnp.int32).at[0].set(first_frame).at[1].set(length)
    kernel = functools.partial(window_kernel, heads=width // HD, scale=HD ** (-0.5))
    cost = pl.CostEstimate(
        flops=4 * rows * span * width + 2 * rows * width * out_width,
        transcendentals=rows * span * (width // HD),
        bytes_accessed=2 * (2 * query.size + rows * width + 2 * low.size + w_out.size + rows * out_width),
    )
    full = lambda i, s: (0, 0)
    return pl.pallas_call(
        kernel,
        cost_estimate=cost,
        out_shape=jax.ShapeDtypeStruct((blocks, rows, block_width), jnp.bfloat16),
        grid_spec=pltpu.PrefetchScalarGridSpec(
            num_scalar_prefetch=1,
            grid=(rows // tq,),
            in_specs=[
                pl.BlockSpec((tq, width), lambda i, s: (i + block_base, 0)),
                pl.BlockSpec(keyed.shape, full),
                pl.BlockSpec(valued.shape, full),
                pl.BlockSpec(low.shape, full),
                pl.BlockSpec(high.shape, full),
                pl.BlockSpec(w_out.shape, full),
            ],
            out_specs=pl.BlockSpec((blocks, tq, block_width), lambda i, s: (0, i, 0)),
            scratch_shapes=[
                pltpu.VMEM((frame_count + 2 * HALF, width), jnp.bfloat16),
                pltpu.VMEM((frame_count + 2 * HALF, width), jnp.bfloat16),
                pltpu.VMEM((tq, width), jnp.bfloat16),
            ],
        ),
        compiler_params=pltpu.CompilerParams(dimension_semantics=("arbitrary",)),
    )(scal, query, keyed, valued, low, high, w_out)


def latent_kernel(scal_ref, q_ref, k_ref, v_ref, acc_ref, stat_ref, *, heads, scale):
    tl = q_ref.shape[0]
    frame_count = k_ref.shape[0]
    valid = lax.broadcasted_iota(jnp.int32, (tl, frame_count), 1) < scal_ref[0]
    stat_ref[...] = jnp.zeros_like(stat_ref)
    for h in range(heads):
        cols = slice(h * HD, (h + 1) * HD)
        s = lax.dot_general(
            q_ref[:, cols], k_ref[:, cols], (((1,), (1,)), ((), ())),
            preferred_element_type=jnp.float32,
        ) * scale
        masked = jnp.where(valid, s, NEG)
        peak = jnp.max(masked, axis=1, keepdims=True)
        weights = jnp.exp(masked - peak)
        total = jnp.sum(weights, axis=1, keepdims=True)
        acc_ref[:, cols] = jnp.dot(
            weights.astype(jnp.bfloat16), v_ref[:, cols], preferred_element_type=jnp.float32
        )
        stat_ref[:, h : h + 1] = peak
        stat_ref[:, heads + h : heads + h + 1] = total


def latent_attention(latent_query, keyed, valued, valid_count):
    latent_count, width = latent_query.shape
    heads = width // HD
    tl = min(256, latent_count)
    scal = jnp.reshape(valid_count, (1,)).astype(jnp.int32)
    kernel = functools.partial(latent_kernel, heads=heads, scale=HD ** (-0.5))
    frame_count = keyed.shape[0]
    cost = pl.CostEstimate(
        flops=4 * latent_count * frame_count * width,
        transcendentals=latent_count * frame_count * heads,
        bytes_accessed=2 * (latent_query.size + 2 * keyed.size) + 4 * latent_count * (width + 128),
    )
    acc, stat = pl.pallas_call(
        kernel,
        cost_estimate=cost,
        out_shape=(
            jax.ShapeDtypeStruct((latent_count, width), jnp.float32),
            jax.ShapeDtypeStruct((latent_count, 128), jnp.float32),
        ),
        grid_spec=pltpu.PrefetchScalarGridSpec(
            num_scalar_prefetch=1,
            grid=(latent_count // tl,),
            in_specs=[
                pl.BlockSpec((tl, width), lambda i, s: (i, 0)),
                pl.BlockSpec(keyed.shape, lambda i, s: (0, 0)),
                pl.BlockSpec(valued.shape, lambda i, s: (0, 0)),
            ],
            out_specs=[
                pl.BlockSpec((tl, width), lambda i, s: (i, 0)),
                pl.BlockSpec((tl, 128), lambda i, s: (i, 0)),
            ],
        ),
    )(scal, latent_query, keyed, valued)
    return stat[:, :heads], stat[:, heads : 2 * heads], acc


def shifted_blocks(payload, axis, rows):
    count = lax.axis_size(axis)
    place = lax.axis_index(axis)
    own = lax.dynamic_slice_in_dim(payload, place * rows, rows, 0)
    parts = [own]
    for shift in range(1, count):
        target = (place + shift) % count
        block = lax.dynamic_slice_in_dim(payload, target * rows, rows, 0)
        pairs = [(i, (i + shift) % count) for i in range(count)]
        parts.append(lax.ppermute(block, axis, pairs))
    return jnp.stack(parts)


def column_sum(partial, axis):
    count = lax.axis_size(axis)
    place = lax.axis_index(axis)
    width = partial.shape[1] // count
    own = lax.dynamic_slice_in_dim(partial, place * width, width, 1)
    total = own.astype(jnp.float32)
    for shift in range(1, count):
        target = (place + shift) % count
        block = lax.dynamic_slice_in_dim(partial, target * width, width, 1)
        pairs = [(i, (i + shift) % count) for i in range(count)]
        total = total + lax.ppermute(block, axis, pairs).astype(jnp.float32)
    return total.astype(jnp.bfloat16)


def send_order(axis):
    count = lax.axis_size(axis)
    place = lax.axis_index(axis)
    if count % 2 != 0:
        return [(place + j) % count for j in range(count)]
    chips = count // 2
    core = place % 2
    chip = place // 2
    theirs = [2 * ((chip + d) % chips) + 1 - core for d in range(chips)]
    mine = [2 * ((chip + d) % chips) + core for d in range(chips)]
    return theirs + mine


def ordered_columns(weight, axis):
    count = lax.axis_size(axis)
    width = weight.shape[1] // count
    return jnp.concatenate(
        [lax.dynamic_slice_in_dim(weight, b * width, width, 1) for b in send_order(axis)], axis=1
    )


def chip_pair_sums(blocks, axis):
    count = lax.axis_size(axis)
    chips = count // 2
    swap = [(i, i ^ 1) for i in range(count)]
    received = lax.ppermute(blocks[:chips], axis, swap)
    return [
        (blocks[chips + d].astype(jnp.float32) + received[d].astype(jnp.float32)).astype(
            jnp.bfloat16
        )
        for d in range(chips)
    ]


def cross_chip_sum(chip_sums, axis):
    count = lax.axis_size(axis)
    chips = count // 2
    total = chip_sums[0].astype(jnp.float32)
    for d in range(1, chips):
        pairs = [(2 * c + k, 2 * ((c + d) % chips) + k) for c in range(chips) for k in range(2)]
        total = total + lax.ppermute(chip_sums[d], axis, pairs).astype(jnp.float32)
    return total.astype(jnp.bfloat16)


def plain_block_sum(blocks, axis):
    count = lax.axis_size(axis)
    total = blocks[0].astype(jnp.float32)
    for shift in range(1, count):
        pairs = [(i, (i + shift) % count) for i in range(count)]
        total = total + lax.ppermute(blocks[shift], axis, pairs).astype(jnp.float32)
    return total.astype(jnp.bfloat16)


def split_three(values):
    hi = values.astype(jnp.bfloat16)
    rest = values - hi.astype(jnp.float32)
    mid = rest.astype(jnp.bfloat16)
    lo = (rest - mid.astype(jnp.float32)).astype(jnp.bfloat16)
    return [hi, mid, lo]


def exchange_rows(payload, axis, rows):
    count = lax.axis_size(axis)
    place = lax.axis_index(axis)
    parts = [lax.dynamic_slice_in_dim(payload, place * rows, rows, 0)]
    for shift in range(1, count):
        pairs = [(i, (i + shift) % count) for i in range(count)]
        block = lax.dynamic_slice_in_dim(payload, ((place + shift) % count) * rows, rows, 0)
        parts.append(lax.ppermute(block, axis, pairs))
    return parts


def merge_kernel(*refs, heads):
    part_refs, out_ref = refs[:-1], refs[-1]
    width = out_ref.shape[1]
    stat_width = 2 * heads

    stat_blocks = []
    for ref in part_refs:
        raw = ref[:, width : width + 3 * stat_width].astype(jnp.float32)
        stat_blocks.append(
            raw[:, 0:stat_width]
            + raw[:, stat_width : 2 * stat_width]
            + raw[:, 2 * stat_width : 3 * stat_width]
        )

    def column(k, c):
        return stat_blocks[k][:, c : c + 1]

    for h in range(heads):
        peaks = [column(k, h) for k in range(len(part_refs))]
        joint = peaks[0]
        for peak in peaks[1:]:
            joint = jnp.maximum(joint, peak)
        total = jnp.zeros_like(joint)
        accum = jnp.zeros((out_ref.shape[0], HD), jnp.float32)
        for k, (ref, peak) in enumerate(zip(part_refs, peaks)):
            factor = jnp.exp(peak - joint)
            total = total + column(k, heads + h) * factor
            accum = accum + ref[:, h * HD : (h + 1) * HD].astype(jnp.float32) * factor
        out_ref[:, h * HD : (h + 1) * HD] = (accum / total).astype(jnp.bfloat16)


def merge_parts(parts, width, heads):
    rows = parts[0].shape[0]
    return pl.pallas_call(
        functools.partial(merge_kernel, heads=heads),
        out_shape=jax.ShapeDtypeStruct((rows, width), jnp.bfloat16),
        in_specs=[pl.BlockSpec(memory_space=pltpu.VMEM)] * len(parts),
        out_specs=pl.BlockSpec(memory_space=pltpu.VMEM),
    )(*parts)


def per_device(
    frames, latents, lengths, w_query, w_key, w_value, w_out, w_latent_query, w_latent_out
):
    frame_count = frames.shape[0]
    head_width = w_query.shape[1]
    heads_here = head_width // HD
    seq_devices = lax.axis_size("seq")
    seq_place = lax.axis_index("seq")
    first_frame = seq_place * frame_count
    length = lengths[0]
    query = project(frames, w_query)
    keyed = project(frames, w_key)
    valued = project(frames, w_value)
    low, high = halos(keyed, valued, "seq")
    chunks = 2 if frame_count % 512 == 0 else 1
    chunk_rows = frame_count // chunks
    head_devices = lax.axis_size("head")
    paired = head_devices % 2 == 0
    w_ordered = ordered_columns(w_out, "head")
    parts = [
        window_attention(
            query, keyed, valued, low, high, w_ordered, first_frame, length,
            c * chunk_rows, chunk_rows, head_devices,
        )
        for c in range(chunks)
    ]
    latent_count = latents.shape[0]
    latent_query = project(latents, w_latent_query)
    valid_count = jnp.clip(length - first_frame, 0, frame_count)
    frame_parts = []
    if paired:
        first_sums = chip_pair_sums(parts[0], "head")
        first_sums, rest, keyed, valued = lax.optimization_barrier(
            (first_sums, parts[1:], keyed, valued)
        )
        frame_parts.append(cross_chip_sum(first_sums, "head"))
        rest_sums = [chip_pair_sums(blocks, "head") for blocks in rest]
    else:
        frame_parts = [plain_block_sum(blocks, "head") for blocks in parts]
    peaks, totals, local_accum = latent_attention(latent_query, keyed, valued, valid_count)
    payload = jnp.concatenate(
        [local_accum.astype(jnp.bfloat16)] + split_three(jnp.concatenate([peaks, totals], axis=1)),
        axis=1,
    )
    if paired:
        rest_sums, payload = lax.optimization_barrier((rest_sums, payload))
        frame_parts.extend(cross_chip_sum(sums, "head") for sums in rest_sums)
    frames_out = jnp.concatenate(frame_parts, axis=0)
    rows_here = latent_count // seq_devices
    parts = exchange_rows(payload, "seq", rows_here)
    summary = merge_parts(parts, head_width, heads_here)
    if paired:
        latent_terms = jnp.dot(
            summary, ordered_columns(w_latent_out, "head"), preferred_element_type=jnp.float32
        ).astype(jnp.bfloat16)
        block_width = latent_terms.shape[1] // head_devices
        latent_blocks = jnp.stack(
            [latent_terms[:, j * block_width : (j + 1) * block_width] for j in range(head_devices)]
        )
        latents_out = cross_chip_sum(chip_pair_sums(latent_blocks, "head"), "head")
    else:
        latent_terms = jnp.dot(summary, w_latent_out, preferred_element_type=jnp.float32)
        latents_out = column_sum(latent_terms.astype(jnp.bfloat16), "head")
    return (frames_out, latents_out)


def solution(mesh):
    return jax.shard_map(
        per_device,
        mesh=mesh,
        in_specs=(
            P(("groups", "seq"), None),
            P(),
            P("groups"),
            P(None, "head"),
            P(None, "head"),
            P(None, "head"),
            P("head", None),
            P(None, "head"),
            P("head", None),
        ),
        out_specs=(P(("groups", "seq"), "head"), P(("groups", "seq"), "head")),
        check_vma=False,
    )
```

```python
import functools

import jax
import jax.numpy as jnp
from jax import lax
from jax.experimental import pallas as pl
from jax.experimental.pallas import tpu as pltpu
from jax.sharding import PartitionSpec as P

HD = 64
HALF = 256
NEG = -1e30


def halos(keyed, valued, axis):
    count = lax.axis_size(axis)
    forward = [(i, i + 1) for i in range(count - 1)]
    backward = [(target, source) for source, target in forward]
    tail = jnp.concatenate([keyed[-HALF:], valued[-HALF:]], axis=1)
    head = jnp.concatenate([keyed[:HALF], valued[:HALF]], axis=1)
    return lax.ppermute(tail, axis, forward), lax.ppermute(head, axis, backward)


def project(source, weight):
    return jnp.dot(source, weight, preferred_element_type=jnp.float32).astype(jnp.bfloat16)


def window_kernel(
    scal_ref, q_ref, k_ref, v_ref, low_ref, high_ref, w_ref, o_ref, kbuf, vbuf, att_ref, *,
    heads, scale
):
    tq = q_ref.shape[0]
    frame_count, width = k_ref.shape
    span = tq + 2 * HALF

    @pl.when(pl.program_id(0) == 0)
    def _fill():
        kbuf[0:HALF, :] = low_ref[:, 0:width]
        vbuf[0:HALF, :] = low_ref[:, width : 2 * width]
        kbuf[HALF : HALF + frame_count, :] = k_ref[...]
        vbuf[HALF : HALF + frame_count, :] = v_ref[...]
        kbuf[HALF + frame_count :, :] = high_ref[:, 0:width]
        vbuf[HALF + frame_count :, :] = high_ref[:, width : 2 * width]

    start = pl.multiple_of(scal_ref[2] + pl.program_id(0) * tq, tq)
    first = scal_ref[0]
    length = scal_ref[1]
    row = lax.broadcasted_iota(jnp.int32, (tq, span), 0)
    col = lax.broadcasted_iota(jnp.int32, (tq, span), 1)
    offset = col - row
    key_pos = first + start - HALF + col
    allowed = (offset >= 0) & (offset <= 2 * HALF) & (key_pos >= 0) & (key_pos < length)
    query_pos = first + start + lax.broadcasted_iota(jnp.int32, (tq, 1), 0)
    query_valid = query_pos < length
    for h in range(heads):
        cols = slice(h * HD, (h + 1) * HD)
        q = q_ref[:, cols]
        k = kbuf[pl.ds(start, span), cols]
        v = vbuf[pl.ds(start, span), cols]
        s = lax.dot_general(
            q, k, (((1,), (1,)), ((), ())), preferred_element_type=jnp.float32
        ) * scale
        masked = jnp.where(allowed, s, NEG)
        peak = jnp.max(masked, axis=1, keepdims=True)
        weights = jnp.exp(masked - peak)
        denom = jnp.sum(weights, axis=1, keepdims=True)
        blended = jnp.dot(weights.astype(jnp.bfloat16), v, preferred_element_type=jnp.float32)
        divisor = jnp.where(query_valid, denom, 1.0)
        att_ref[:, cols] = jnp.where(query_valid, blended / divisor, 0.0).astype(jnp.bfloat16)
    result = jnp.dot(att_ref[...], w_ref[...], preferred_element_type=jnp.float32)
    block_width = o_ref.shape[2]
    for b in range(o_ref.shape[0]):
        o_ref[b] = result[:, b * block_width : (b + 1) * block_width].astype(jnp.bfloat16)


def window_attention(
    query, keyed, valued, low, high, w_out, first_frame, length, row_base, rows, blocks
):
    frame_count, width = query.shape
    out_width = w_out.shape[1]
    block_width = out_width // blocks
    tq = min(512, rows)
    block_base = row_base // tq
    span = tq + 2 * HALF
    scal = jnp.array([0, 0, row_base], jnp.int32).at[0].set(first_frame).at[1].set(length)
    kernel = functools.partial(window_kernel, heads=width // HD, scale=HD ** (-0.5))
    cost = pl.CostEstimate(
        flops=4 * rows * span * width + 2 * rows * width * out_width,
        transcendentals=rows * span * (width // HD),
        bytes_accessed=2 * (2 * query.size + rows * width + 2 * low.size + w_out.size + rows * out_width),
    )
    full = lambda i, s: (0, 0)
    return pl.pallas_call(
        kernel,
        cost_estimate=cost,
        out_shape=jax.ShapeDtypeStruct((blocks, rows, block_width), jnp.bfloat16),
        grid_spec=pltpu.PrefetchScalarGridSpec(
            num_scalar_prefetch=1,
            grid=(rows // tq,),
            in_specs=[
                pl.BlockSpec((tq, width), lambda i, s: (i + block_base, 0)),
                pl.BlockSpec(keyed.shape, full),
                pl.BlockSpec(valued.shape, full),
                pl.BlockSpec(low.shape, full),
                pl.BlockSpec(high.shape, full),
                pl.BlockSpec(w_out.shape, full),
            ],
            out_specs=pl.BlockSpec((blocks, tq, block_width), lambda i, s: (0, i, 0)),
            scratch_shapes=[
                pltpu.VMEM((frame_count + 2 * HALF, width), jnp.bfloat16),
                pltpu.VMEM((frame_count + 2 * HALF, width), jnp.bfloat16),
                pltpu.VMEM((tq, width), jnp.bfloat16),
            ],
        ),
        compiler_params=pltpu.CompilerParams(dimension_semantics=("arbitrary",)),
    )(scal, query, keyed, valued, low, high, w_out)


def latent_kernel(scal_ref, q_ref, k_ref, v_ref, acc_ref, stat_ref, *, heads, scale):
    tl = q_ref.shape[0]
    frame_count = k_ref.shape[0]
    valid = lax.broadcasted_iota(jnp.int32, (tl, frame_count), 1) < scal_ref[0]
    stat_ref[...] = jnp.zeros_like(stat_ref)
    for h in range(heads):
        cols = slice(h * HD, (h + 1) * HD)
        s = lax.dot_general(
            q_ref[:, cols], k_ref[:, cols], (((1,), (1,)), ((), ())),
            preferred_element_type=jnp.float32,
        ) * scale
        masked = jnp.where(valid, s, NEG)
        peak = jnp.max(masked, axis=1, keepdims=True)
        weights = jnp.exp(masked - peak)
        total = jnp.sum(weights, axis=1, keepdims=True)
        acc_ref[:, cols] = jnp.dot(
            weights.astype(jnp.bfloat16), v_ref[:, cols], preferred_element_type=jnp.float32
        )
        stat_ref[:, h : h + 1] = peak
        stat_ref[:, heads + h : heads + h + 1] = total


def latent_attention(latent_query, keyed, valued, valid_count):
    latent_count, width = latent_query.shape
    heads = width // HD
    tl = min(256, latent_count)
    scal = jnp.reshape(valid_count, (1,)).astype(jnp.int32)
    kernel = functools.partial(latent_kernel, heads=heads, scale=HD ** (-0.5))
    frame_count = keyed.shape[0]
    cost = pl.CostEstimate(
        flops=4 * latent_count * frame_count * width,
        transcendentals=latent_count * frame_count * heads,
        bytes_accessed=2 * (latent_query.size + 2 * keyed.size) + 4 * latent_count * (width + 128),
    )
    acc, stat = pl.pallas_call(
        kernel,
        cost_estimate=cost,
        out_shape=(
            jax.ShapeDtypeStruct((latent_count, width), jnp.float32),
            jax.ShapeDtypeStruct((latent_count, 128), jnp.float32),
        ),
        grid_spec=pltpu.PrefetchScalarGridSpec(
            num_scalar_prefetch=1,
            grid=(latent_count // tl,),
            in_specs=[
                pl.BlockSpec((tl, width), lambda i, s: (i, 0)),
                pl.BlockSpec(keyed.shape, lambda i, s: (0, 0)),
                pl.BlockSpec(valued.shape, lambda i, s: (0, 0)),
            ],
            out_specs=[
                pl.BlockSpec((tl, width), lambda i, s: (i, 0)),
                pl.BlockSpec((tl, 128), lambda i, s: (i, 0)),
            ],
        ),
    )(scal, latent_query, keyed, valued)
    return stat[:, :heads], stat[:, heads : 2 * heads], acc


def shifted_blocks(payload, axis, rows):
    count = lax.axis_size(axis)
    place = lax.axis_index(axis)
    own = lax.dynamic_slice_in_dim(payload, place * rows, rows, 0)
    parts = [own]
    for shift in range(1, count):
        target = (place + shift) % count
        block = lax.dynamic_slice_in_dim(payload, target * rows, rows, 0)
        pairs = [(i, (i + shift) % count) for i in range(count)]
        parts.append(lax.ppermute(block, axis, pairs))
    return jnp.stack(parts)


def column_sum(partial, axis):
    count = lax.axis_size(axis)
    place = lax.axis_index(axis)
    width = partial.shape[1] // count
    own = lax.dynamic_slice_in_dim(partial, place * width, width, 1)
    total = own.astype(jnp.float32)
    for shift in range(1, count):
        target = (place + shift) % count
        block = lax.dynamic_slice_in_dim(partial, target * width, width, 1)
        pairs = [(i, (i + shift) % count) for i in range(count)]
        total = total + lax.ppermute(block, axis, pairs).astype(jnp.float32)
    return total.astype(jnp.bfloat16)


def send_order(axis):
    count = lax.axis_size(axis)
    place = lax.axis_index(axis)
    if count % 2 != 0:
        return [(place + j) % count for j in range(count)]
    chips = count // 2
    core = place % 2
    chip = place // 2
    theirs = [2 * ((chip + d) % chips) + 1 - core for d in range(chips)]
    mine = [2 * ((chip + d) % chips) + core for d in range(chips)]
    return theirs + mine


def ordered_columns(weight, axis):
    count = lax.axis_size(axis)
    width = weight.shape[1] // count
    return jnp.concatenate(
        [lax.dynamic_slice_in_dim(weight, b * width, width, 1) for b in send_order(axis)], axis=1
    )


def chip_pair_sums(blocks, axis):
    count = lax.axis_size(axis)
    chips = count // 2
    swap = [(i, i ^ 1) for i in range(count)]
    received = lax.ppermute(blocks[:chips], axis, swap)
    return [
        (blocks[chips + d].astype(jnp.float32) + received[d].astype(jnp.float32)).astype(
            jnp.bfloat16
        )
        for d in range(chips)
    ]


def cross_chip_sum(chip_sums, axis):
    count = lax.axis_size(axis)
    chips = count // 2
    total = chip_sums[0].astype(jnp.float32)
    for d in range(1, chips):
        pairs = [(2 * c + k, 2 * ((c + d) % chips) + k) for c in range(chips) for k in range(2)]
        total = total + lax.ppermute(chip_sums[d], axis, pairs).astype(jnp.float32)
    return total.astype(jnp.bfloat16)


def plain_block_sum(blocks, axis):
    count = lax.axis_size(axis)
    total = blocks[0].astype(jnp.float32)
    for shift in range(1, count):
        pairs = [(i, (i + shift) % count) for i in range(count)]
        total = total + lax.ppermute(blocks[shift], axis, pairs).astype(jnp.float32)
    return total.astype(jnp.bfloat16)


def split_three(values):
    hi = values.astype(jnp.bfloat16)
    rest = values - hi.astype(jnp.float32)
    mid = rest.astype(jnp.bfloat16)
    lo = (rest - mid.astype(jnp.float32)).astype(jnp.bfloat16)
    return [hi, mid, lo]


def exchange_rows(payload, axis, rows):
    count = lax.axis_size(axis)
    place = lax.axis_index(axis)
    parts = [lax.dynamic_slice_in_dim(payload, place * rows, rows, 0)]
    for shift in range(1, count):
        pairs = [(i, (i + shift) % count) for i in range(count)]
        block = lax.dynamic_slice_in_dim(payload, ((place + shift) % count) * rows, rows, 0)
        parts.append(lax.ppermute(block, axis, pairs))
    return parts


def merge_kernel(*refs, heads):
    part_refs, out_ref = refs[:-1], refs[-1]
    width = out_ref.shape[1]
    stat_width = 2 * heads

    stat_blocks = []
    for ref in part_refs:
        raw = ref[:, width : width + 3 * stat_width].astype(jnp.float32)
        stat_blocks.append(
            raw[:, 0:stat_width]
            + raw[:, stat_width : 2 * stat_width]
            + raw[:, 2 * stat_width : 3 * stat_width]
        )

    def column(k, c):
        return stat_blocks[k][:, c : c + 1]

    for h in range(heads):
        peaks = [column(k, h) for k in range(len(part_refs))]
        joint = peaks[0]
        for peak in peaks[1:]:
            joint = jnp.maximum(joint, peak)
        total = jnp.zeros_like(joint)
        accum = jnp.zeros((out_ref.shape[0], HD), jnp.float32)
        for k, (ref, peak) in enumerate(zip(part_refs, peaks)):
            factor = jnp.exp(peak - joint)
            total = total + column(k, heads + h) * factor
            accum = accum + ref[:, h * HD : (h + 1) * HD].astype(jnp.float32) * factor
        out_ref[:, h * HD : (h + 1) * HD] = (accum / total).astype(jnp.bfloat16)


def merge_parts(parts, width, heads):
    rows = parts[0].shape[0]
    return pl.pallas_call(
        functools.partial(merge_kernel, heads=heads),
        out_shape=jax.ShapeDtypeStruct((rows, width), jnp.bfloat16),
        in_specs=[pl.BlockSpec(memory_space=pltpu.VMEM)] * len(parts),
        out_specs=pl.BlockSpec(memory_space=pltpu.VMEM),
    )(*parts)


def per_device(
    frames, latents, lengths, w_query, w_key, w_value, w_out, w_latent_query, w_latent_out
):
    frame_count = frames.shape[0]
    head_width = w_query.shape[1]
    heads_here = head_width // HD
    seq_devices = lax.axis_size("seq")
    seq_place = lax.axis_index("seq")
    first_frame = seq_place * frame_count
    length = lengths[0]
    query = project(frames, w_query)
    keyed = project(frames, w_key)
    valued = project(frames, w_value)
    low, high = halos(keyed, valued, "seq")
    chunks = 2 if frame_count % 512 == 0 else 1
    chunk_rows = frame_count // chunks
    head_devices = lax.axis_size("head")
    paired = head_devices % 2 == 0
    w_ordered = ordered_columns(w_out, "head")
    parts = [
        window_attention(
            query, keyed, valued, low, high, w_ordered, first_frame, length,
            c * chunk_rows, chunk_rows, head_devices,
        )
        for c in range(chunks)
    ]
    latent_count = latents.shape[0]
    latent_query = project(latents, w_latent_query)
    valid_count = jnp.clip(length - first_frame, 0, frame_count)
    frame_parts = []
    if paired:
        first_sums = chip_pair_sums(parts[0], "head")
        first_sums, rest, keyed, valued = lax.optimization_barrier(
            (first_sums, parts[1:], keyed, valued)
        )
        frame_parts.append(cross_chip_sum(first_sums, "head"))
        rest_sums = [chip_pair_sums(blocks, "head") for blocks in rest]
    else:
        frame_parts = [plain_block_sum(blocks, "head") for blocks in parts]
    peaks, totals, local_accum = latent_attention(latent_query, keyed, valued, valid_count)
    payload = jnp.concatenate(
        [local_accum.astype(jnp.bfloat16)] + split_three(jnp.concatenate([peaks, totals], axis=1)),
        axis=1,
    )
    if paired:
        rest_sums, payload = lax.optimization_barrier((rest_sums, payload))
        frame_parts.extend(cross_chip_sum(sums, "head") for sums in rest_sums)
    frames_out = jnp.concatenate(frame_parts, axis=0)
    rows_here = latent_count // seq_devices
    parts = exchange_rows(payload, "seq", rows_here)
    summary = merge_parts(parts, head_width, heads_here)
    if paired:
        latent_terms = jnp.dot(
            summary, ordered_columns(w_latent_out, "head"), preferred_element_type=jnp.float32
        ).astype(jnp.bfloat16)
        block_width = latent_terms.shape[1] // head_devices
        latent_blocks = jnp.stack(
            [latent_terms[:, j * block_width : (j + 1) * block_width] for j in range(head_devices)]
        )
        latents_out = cross_chip_sum(chip_pair_sums(latent_blocks, "head"), "head")
    else:
        latent_terms = jnp.dot(summary, w_latent_out, preferred_element_type=jnp.float32)
        latents_out = column_sum(latent_terms.astype(jnp.bfloat16), "head")
    return (frames_out, latents_out)


def solution(mesh):
    return jax.shard_map(
        per_device,
        mesh=mesh,
        in_specs=(
            P(("groups", "seq"), None),
            P(),
            P("groups"),
            P(None, "head"),
            P(None, "head"),
            P(None, "head"),
            P("head", None),
            P(None, "head"),
            P("head", None),
        ),
        out_specs=(P(("groups", "seq"), "head"), P(("groups", "seq"), "head")),
        check_vma=False,
    )
```

```python
import functools

import jax
import jax.numpy as jnp
from jax import lax
from jax.experimental import pallas as pl
from jax.experimental.pallas import tpu as pltpu
from jax.sharding import PartitionSpec as P

HD = 64
HALF = 256
NEG = -1e30


def halos(keyed, valued, axis):
    count = lax.axis_size(axis)
    forward = [(i, i + 1) for i in range(count - 1)]
    backward = [(target, source) for source, target in forward]
    tail = jnp.concatenate([keyed[-HALF:], valued[-HALF:]], axis=1)
    head = jnp.concatenate([keyed[:HALF], valued[:HALF]], axis=1)
    return lax.ppermute(tail, axis, forward), lax.ppermute(head, axis, backward)


def project(source, weight):
    return jnp.dot(source, weight, preferred_element_type=jnp.float32).astype(jnp.bfloat16)


def window_kernel(
    scal_ref, q_ref, k_ref, v_ref, low_ref, high_ref, w_ref, o_ref, kbuf, vbuf, att_ref, *,
    heads, scale
):
    tq = q_ref.shape[0]
    frame_count, width = k_ref.shape
    span = tq + 2 * HALF

    @pl.when(pl.program_id(0) == 0)
    def _fill():
        kbuf[0:HALF, :] = low_ref[:, 0:width]
        vbuf[0:HALF, :] = low_ref[:, width : 2 * width]
        kbuf[HALF : HALF + frame_count, :] = k_ref[...]
        vbuf[HALF : HALF + frame_count, :] = v_ref[...]
        kbuf[HALF + frame_count :, :] = high_ref[:, 0:width]
        vbuf[HALF + frame_count :, :] = high_ref[:, width : 2 * width]

    start = pl.multiple_of(scal_ref[2] + pl.program_id(0) * tq, tq)
    first = scal_ref[0]
    length = scal_ref[1]
    row = lax.broadcasted_iota(jnp.int32, (tq, span), 0)
    col = lax.broadcasted_iota(jnp.int32, (tq, span), 1)
    offset = col - row
    key_pos = first + start - HALF + col
    allowed = (offset >= 0) & (offset <= 2 * HALF) & (key_pos >= 0) & (key_pos < length)
    query_pos = first + start + lax.broadcasted_iota(jnp.int32, (tq, 1), 0)
    query_valid = query_pos < length
    for h in range(heads):
        cols = slice(h * HD, (h + 1) * HD)
        q = q_ref[:, cols]
        k = kbuf[pl.ds(start, span), cols]
        v = vbuf[pl.ds(start, span), cols]
        s = lax.dot_general(
            q, k, (((1,), (1,)), ((), ())), preferred_element_type=jnp.float32
        ) * scale
        masked = jnp.where(allowed, s, NEG)
        peak = jnp.max(masked, axis=1, keepdims=True)
        weights = jnp.exp(masked - peak)
        denom = jnp.sum(weights, axis=1, keepdims=True)
        blended = jnp.dot(weights.astype(jnp.bfloat16), v, preferred_element_type=jnp.float32)
        divisor = jnp.where(query_valid, denom, 1.0)
        att_ref[:, cols] = jnp.where(query_valid, blended / divisor, 0.0).astype(jnp.bfloat16)
    result = jnp.dot(att_ref[...], w_ref[...], preferred_element_type=jnp.float32)
    block_width = o_ref.shape[2]
    for b in range(o_ref.shape[0]):
        o_ref[b] = result[:, b * block_width : (b + 1) * block_width].astype(jnp.bfloat16)


def window_attention(
    query, keyed, valued, low, high, w_out, first_frame, length, row_base, rows, blocks
):
    frame_count, width = query.shape
    out_width = w_out.shape[1]
    block_width = out_width // blocks
    tq = min(512, rows)
    block_base = row_base // tq
    span = tq + 2 * HALF
    scal = jnp.array([0, 0, row_base], jnp.int32).at[0].set(first_frame).at[1].set(length)
    kernel = functools.partial(window_kernel, heads=width // HD, scale=HD ** (-0.5))
    cost = pl.CostEstimate(
        flops=4 * rows * span * width + 2 * rows * width * out_width,
        transcendentals=rows * span * (width // HD),
        bytes_accessed=2 * (2 * query.size + rows * width + 2 * low.size + w_out.size + rows * out_width),
    )
    full = lambda i, s: (0, 0)
    return pl.pallas_call(
        kernel,
        cost_estimate=cost,
        out_shape=jax.ShapeDtypeStruct((blocks, rows, block_width), jnp.bfloat16),
        grid_spec=pltpu.PrefetchScalarGridSpec(
            num_scalar_prefetch=1,
            grid=(rows // tq,),
            in_specs=[
                pl.BlockSpec((tq, width), lambda i, s: (i + block_base, 0)),
                pl.BlockSpec(keyed.shape, full),
                pl.BlockSpec(valued.shape, full),
                pl.BlockSpec(low.shape, full),
                pl.BlockSpec(high.shape, full),
                pl.BlockSpec(w_out.shape, full),
            ],
            out_specs=pl.BlockSpec((blocks, tq, block_width), lambda i, s: (0, i, 0)),
            scratch_shapes=[
                pltpu.VMEM((frame_count + 2 * HALF, width), jnp.bfloat16),
                pltpu.VMEM((frame_count + 2 * HALF, width), jnp.bfloat16),
                pltpu.VMEM((tq, width), jnp.bfloat16),
            ],
        ),
        compiler_params=pltpu.CompilerParams(dimension_semantics=("arbitrary",)),
    )(scal, query, keyed, valued, low, high, w_out)


def latent_kernel(scal_ref, q_ref, k_ref, v_ref, acc_ref, stat_ref, *, heads, scale):
    tl = q_ref.shape[0]
    frame_count = k_ref.shape[0]
    valid = lax.broadcasted_iota(jnp.int32, (tl, frame_count), 1) < scal_ref[0]
    stat_ref[...] = jnp.zeros_like(stat_ref)
    for h in range(heads):
        cols = slice(h * HD, (h + 1) * HD)
        s = lax.dot_general(
            q_ref[:, cols], k_ref[:, cols], (((1,), (1,)), ((), ())),
            preferred_element_type=jnp.float32,
        ) * scale
        masked = jnp.where(valid, s, NEG)
        peak = jnp.max(masked, axis=1, keepdims=True)
        weights = jnp.exp(masked - peak)
        total = jnp.sum(weights, axis=1, keepdims=True)
        acc_ref[:, cols] = jnp.dot(
            weights.astype(jnp.bfloat16), v_ref[:, cols], preferred_element_type=jnp.float32
        )
        stat_ref[:, h : h + 1] = peak
        stat_ref[:, heads + h : heads + h + 1] = total


def latent_attention(latent_query, keyed, valued, valid_count):
    latent_count, width = latent_query.shape
    heads = width // HD
    tl = min(512, latent_count)
    scal = jnp.reshape(valid_count, (1,)).astype(jnp.int32)
    kernel = functools.partial(latent_kernel, heads=heads, scale=HD ** (-0.5))
    frame_count = keyed.shape[0]
    cost = pl.CostEstimate(
        flops=4 * latent_count * frame_count * width,
        transcendentals=latent_count * frame_count * heads,
        bytes_accessed=2 * (latent_query.size + 2 * keyed.size) + 4 * latent_count * (width + 128),
    )
    acc, stat = pl.pallas_call(
        kernel,
        cost_estimate=cost,
        out_shape=(
            jax.ShapeDtypeStruct((latent_count, width), jnp.float32),
            jax.ShapeDtypeStruct((latent_count, 128), jnp.float32),
        ),
        grid_spec=pltpu.PrefetchScalarGridSpec(
            num_scalar_prefetch=1,
            grid=(latent_count // tl,),
            in_specs=[
                pl.BlockSpec((tl, width), lambda i, s: (i, 0)),
                pl.BlockSpec(keyed.shape, lambda i, s: (0, 0)),
                pl.BlockSpec(valued.shape, lambda i, s: (0, 0)),
            ],
            out_specs=[
                pl.BlockSpec((tl, width), lambda i, s: (i, 0)),
                pl.BlockSpec((tl, 128), lambda i, s: (i, 0)),
            ],
        ),
    )(scal, latent_query, keyed, valued)
    return stat[:, :heads], stat[:, heads : 2 * heads], acc


def shifted_blocks(payload, axis, rows):
    count = lax.axis_size(axis)
    place = lax.axis_index(axis)
    own = lax.dynamic_slice_in_dim(payload, place * rows, rows, 0)
    parts = [own]
    for shift in range(1, count):
        target = (place + shift) % count
        block = lax.dynamic_slice_in_dim(payload, target * rows, rows, 0)
        pairs = [(i, (i + shift) % count) for i in range(count)]
        parts.append(lax.ppermute(block, axis, pairs))
    return jnp.stack(parts)


def column_sum(partial, axis):
    count = lax.axis_size(axis)
    place = lax.axis_index(axis)
    width = partial.shape[1] // count
    own = lax.dynamic_slice_in_dim(partial, place * width, width, 1)
    total = own.astype(jnp.float32)
    for shift in range(1, count):
        target = (place + shift) % count
        block = lax.dynamic_slice_in_dim(partial, target * width, width, 1)
        pairs = [(i, (i + shift) % count) for i in range(count)]
        total = total + lax.ppermute(block, axis, pairs).astype(jnp.float32)
    return total.astype(jnp.bfloat16)


def send_order(axis):
    count = lax.axis_size(axis)
    place = lax.axis_index(axis)
    if count % 2 != 0:
        return [(place + j) % count for j in range(count)]
    chips = count // 2
    core = place % 2
    chip = place // 2
    theirs = [2 * ((chip + d) % chips) + 1 - core for d in range(chips)]
    mine = [2 * ((chip + d) % chips) + core for d in range(chips)]
    return theirs + mine


def ordered_columns(weight, axis):
    count = lax.axis_size(axis)
    width = weight.shape[1] // count
    return jnp.concatenate(
        [lax.dynamic_slice_in_dim(weight, b * width, width, 1) for b in send_order(axis)], axis=1
    )


def chip_pair_sums(blocks, axis):
    count = lax.axis_size(axis)
    chips = count // 2
    swap = [(i, i ^ 1) for i in range(count)]
    received = lax.ppermute(blocks[:chips], axis, swap)
    return [
        (blocks[chips + d].astype(jnp.float32) + received[d].astype(jnp.float32)).astype(
            jnp.bfloat16
        )
        for d in range(chips)
    ]


def cross_chip_sum(chip_sums, axis):
    count = lax.axis_size(axis)
    chips = count // 2
    total = chip_sums[0].astype(jnp.float32)
    for d in range(1, chips):
        pairs = [(2 * c + k, 2 * ((c + d) % chips) + k) for c in range(chips) for k in range(2)]
        total = total + lax.ppermute(chip_sums[d], axis, pairs).astype(jnp.float32)
    return total.astype(jnp.bfloat16)


def plain_block_sum(blocks, axis):
    count = lax.axis_size(axis)
    total = blocks[0].astype(jnp.float32)
    for shift in range(1, count):
        pairs = [(i, (i + shift) % count) for i in range(count)]
        total = total + lax.ppermute(blocks[shift], axis, pairs).astype(jnp.float32)
    return total.astype(jnp.bfloat16)


def split_three(values):
    hi = values.astype(jnp.bfloat16)
    rest = values - hi.astype(jnp.float32)
    mid = rest.astype(jnp.bfloat16)
    lo = (rest - mid.astype(jnp.float32)).astype(jnp.bfloat16)
    return [hi, mid, lo]


def exchange_rows(payload, axis, rows):
    count = lax.axis_size(axis)
    place = lax.axis_index(axis)
    parts = [lax.dynamic_slice_in_dim(payload, place * rows, rows, 0)]
    for shift in range(1, count):
        pairs = [(i, (i + shift) % count) for i in range(count)]
        block = lax.dynamic_slice_in_dim(payload, ((place + shift) % count) * rows, rows, 0)
        parts.append(lax.ppermute(block, axis, pairs))
    return parts


def merge_kernel(*refs, heads):
    part_refs, out_ref = refs[:-1], refs[-1]
    width = out_ref.shape[1]
    stat_width = 2 * heads

    stat_blocks = []
    for ref in part_refs:
        raw = ref[:, width : width + 3 * stat_width].astype(jnp.float32)
        stat_blocks.append(
            raw[:, 0:stat_width]
            + raw[:, stat_width : 2 * stat_width]
            + raw[:, 2 * stat_width : 3 * stat_width]
        )

    def column(k, c):
        return stat_blocks[k][:, c : c + 1]

    for h in range(heads):
        peaks = [column(k, h) for k in range(len(part_refs))]
        joint = peaks[0]
        for peak in peaks[1:]:
            joint = jnp.maximum(joint, peak)
        total = jnp.zeros_like(joint)
        accum = jnp.zeros((out_ref.shape[0], HD), jnp.float32)
        for k, (ref, peak) in enumerate(zip(part_refs, peaks)):
            factor = jnp.exp(peak - joint)
            total = total + column(k, heads + h) * factor
            accum = accum + ref[:, h * HD : (h + 1) * HD].astype(jnp.float32) * factor
        out_ref[:, h * HD : (h + 1) * HD] = (accum / total).astype(jnp.bfloat16)


def merge_parts(parts, width, heads):
    rows = parts[0].shape[0]
    return pl.pallas_call(
        functools.partial(merge_kernel, heads=heads),
        out_shape=jax.ShapeDtypeStruct((rows, width), jnp.bfloat16),
        in_specs=[pl.BlockSpec(memory_space=pltpu.VMEM)] * len(parts),
        out_specs=pl.BlockSpec(memory_space=pltpu.VMEM),
    )(*parts)


def per_device(
    frames, latents, lengths, w_query, w_key, w_value, w_out, w_latent_query, w_latent_out
):
    frame_count = frames.shape[0]
    head_width = w_query.shape[1]
    heads_here = head_width // HD
    seq_devices = lax.axis_size("seq")
    seq_place = lax.axis_index("seq")
    first_frame = seq_place * frame_count
    length = lengths[0]
    query = project(frames, w_query)
    keyed = project(frames, w_key)
    valued = project(frames, w_value)
    low, high = halos(keyed, valued, "seq")
    chunks = 2 if frame_count % 512 == 0 else 1
    chunk_rows = frame_count // chunks
    head_devices = lax.axis_size("head")
    paired = head_devices % 2 == 0
    w_ordered = ordered_columns(w_out, "head")
    parts = [
        window_attention(
            query, keyed, valued, low, high, w_ordered, first_frame, length,
            c * chunk_rows, chunk_rows, head_devices,
        )
        for c in range(chunks)
    ]
    latent_count = latents.shape[0]
    latent_query = project(latents, w_latent_query)
    valid_count = jnp.clip(length - first_frame, 0, frame_count)
    frame_parts = []
    if paired:
        first_sums = chip_pair_sums(parts[0], "head")
        first_sums, rest, keyed, valued = lax.optimization_barrier(
            (first_sums, parts[1:], keyed, valued)
        )
        frame_parts.append(cross_chip_sum(first_sums, "head"))
        rest_sums = [chip_pair_sums(blocks, "head") for blocks in rest]
    else:
        frame_parts = [plain_block_sum(blocks, "head") for blocks in parts]
    peaks, totals, local_accum = latent_attention(latent_query, keyed, valued, valid_count)
    payload = jnp.concatenate(
        [local_accum.astype(jnp.bfloat16)] + split_three(jnp.concatenate([peaks, totals], axis=1)),
        axis=1,
    )
    if paired:
        rest_sums, payload = lax.optimization_barrier((rest_sums, payload))
        frame_parts.extend(cross_chip_sum(sums, "head") for sums in rest_sums)
    frames_out = jnp.concatenate(frame_parts, axis=0)
    rows_here = latent_count // seq_devices
    parts = exchange_rows(payload, "seq", rows_here)
    summary = merge_parts(parts, head_width, heads_here)
    if paired:
        latent_terms = jnp.dot(
            summary, ordered_columns(w_latent_out, "head"), preferred_element_type=jnp.float32
        ).astype(jnp.bfloat16)
        block_width = latent_terms.shape[1] // head_devices
        latent_blocks = jnp.stack(
            [latent_terms[:, j * block_width : (j + 1) * block_width] for j in range(head_devices)]
        )
        latents_out = cross_chip_sum(chip_pair_sums(latent_blocks, "head"), "head")
    else:
        latent_terms = jnp.dot(summary, w_latent_out, preferred_element_type=jnp.float32)
        latents_out = column_sum(latent_terms.astype(jnp.bfloat16), "head")
    return (frames_out, latents_out)


def solution(mesh):
    return jax.shard_map(
        per_device,
        mesh=mesh,
        in_specs=(
            P(("groups", "seq"), None),
            P(),
            P("groups"),
            P(None, "head"),
            P(None, "head"),
            P(None, "head"),
            P("head", None),
            P(None, "head"),
            P("head", None),
        ),
        out_specs=(P(("groups", "seq"), "head"), P(("groups", "seq"), "head")),
        check_vma=False,
    )
```

```python
import functools

import jax
import jax.numpy as jnp
from jax import lax
from jax.experimental import pallas as pl
from jax.experimental.pallas import tpu as pltpu
from jax.sharding import PartitionSpec as P

HD = 64
HALF = 256
NEG = -1e30


def halos(keyed, valued, axis):
    count = lax.axis_size(axis)
    forward = [(i, i + 1) for i in range(count - 1)]
    backward = [(target, source) for source, target in forward]
    tail = jnp.concatenate([keyed[-HALF:], valued[-HALF:]], axis=1)
    head = jnp.concatenate([keyed[:HALF], valued[:HALF]], axis=1)
    return lax.ppermute(tail, axis, forward), lax.ppermute(head, axis, backward)


def project(source, weight):
    return jnp.dot(source, weight, preferred_element_type=jnp.float32).astype(jnp.bfloat16)


def window_kernel(
    scal_ref, q_ref, k_ref, v_ref, low_ref, high_ref, w_ref, o_ref, kbuf, vbuf, att_ref, *,
    heads, scale
):
    tq = q_ref.shape[0]
    frame_count, width = k_ref.shape
    span = tq + 2 * HALF

    @pl.when(pl.program_id(0) == 0)
    def _fill():
        kbuf[0:HALF, :] = low_ref[:, 0:width]
        vbuf[0:HALF, :] = low_ref[:, width : 2 * width]
        kbuf[HALF : HALF + frame_count, :] = k_ref[...]
        vbuf[HALF : HALF + frame_count, :] = v_ref[...]
        kbuf[HALF + frame_count :, :] = high_ref[:, 0:width]
        vbuf[HALF + frame_count :, :] = high_ref[:, width : 2 * width]

    start = pl.multiple_of(scal_ref[2] + pl.program_id(0) * tq, tq)
    first = scal_ref[0]
    length = scal_ref[1]
    row = lax.broadcasted_iota(jnp.int32, (tq, span), 0)
    col = lax.broadcasted_iota(jnp.int32, (tq, span), 1)
    offset = col - row
    key_pos = first + start - HALF + col
    allowed = (offset >= 0) & (offset <= 2 * HALF) & (key_pos >= 0) & (key_pos < length)
    query_pos = first + start + lax.broadcasted_iota(jnp.int32, (tq, 1), 0)
    query_valid = query_pos < length
    for h in range(heads):
        cols = slice(h * HD, (h + 1) * HD)
        q = q_ref[:, cols]
        k = kbuf[pl.ds(start, span), cols]
        v = vbuf[pl.ds(start, span), cols]
        s = lax.dot_general(
            q, k, (((1,), (1,)), ((), ())), preferred_element_type=jnp.float32
        ) * scale
        masked = jnp.where(allowed, s, NEG)
        peak = jnp.max(masked, axis=1, keepdims=True)
        weights = jnp.exp(masked - peak)
        denom = jnp.sum(weights, axis=1, keepdims=True)
        blended = jnp.dot(weights.astype(jnp.bfloat16), v, preferred_element_type=jnp.float32)
        divisor = jnp.where(query_valid, denom, 1.0)
        att_ref[:, cols] = jnp.where(query_valid, blended / divisor, 0.0).astype(jnp.bfloat16)
    result = jnp.dot(att_ref[...], w_ref[...], preferred_element_type=jnp.float32)
    block_width = o_ref.shape[2]
    for b in range(o_ref.shape[0]):
        o_ref[b] = result[:, b * block_width : (b + 1) * block_width].astype(jnp.bfloat16)


def window_attention(
    query, keyed, valued, low, high, w_out, first_frame, length, row_base, rows, blocks
):
    frame_count = query.shape[0]
    width = low.shape[1] // 2
    out_width = w_out.shape[1]
    block_width = out_width // blocks
    tq = min(512, rows)
    block_base = row_base // tq
    span = tq + 2 * HALF
    scal = jnp.array([0, 0, row_base], jnp.int32).at[0].set(first_frame).at[1].set(length)
    kernel = functools.partial(window_kernel, heads=width // HD, scale=HD ** (-0.5))
    cost = pl.CostEstimate(
        flops=4 * rows * span * width + 2 * rows * width * out_width,
        transcendentals=rows * span * (width // HD),
        bytes_accessed=2 * (2 * query.size + rows * width + 2 * low.size + w_out.size + rows * out_width),
    )
    full = lambda i, s: (0, 0)
    return pl.pallas_call(
        kernel,
        cost_estimate=cost,
        out_shape=jax.ShapeDtypeStruct((blocks, rows, block_width), jnp.bfloat16),
        grid_spec=pltpu.PrefetchScalarGridSpec(
            num_scalar_prefetch=1,
            grid=(rows // tq,),
            in_specs=[
                pl.BlockSpec((tq, width), lambda i, s: (i + block_base, 0)),
                pl.BlockSpec((frame_count, width), lambda i, s: (0, 1)),
                pl.BlockSpec((frame_count, width), lambda i, s: (0, 2)),
                pl.BlockSpec(low.shape, full),
                pl.BlockSpec(high.shape, full),
                pl.BlockSpec(w_out.shape, full),
            ],
            out_specs=pl.BlockSpec((blocks, tq, block_width), lambda i, s: (0, i, 0)),
            scratch_shapes=[
                pltpu.VMEM((frame_count + 2 * HALF, width), jnp.bfloat16),
                pltpu.VMEM((frame_count + 2 * HALF, width), jnp.bfloat16),
                pltpu.VMEM((tq, width), jnp.bfloat16),
            ],
        ),
        compiler_params=pltpu.CompilerParams(dimension_semantics=("arbitrary",)),
    )(scal, query, keyed, valued, low, high, w_out)


def latent_kernel(scal_ref, q_ref, k_ref, v_ref, acc_ref, stat_ref, *, heads, scale):
    tl = q_ref.shape[0]
    frame_count = k_ref.shape[0]
    valid = lax.broadcasted_iota(jnp.int32, (tl, frame_count), 1) < scal_ref[0]
    stat_ref[...] = jnp.zeros_like(stat_ref)
    for h in range(heads):
        cols = slice(h * HD, (h + 1) * HD)
        s = lax.dot_general(
            q_ref[:, cols], k_ref[:, cols], (((1,), (1,)), ((), ())),
            preferred_element_type=jnp.float32,
        ) * scale
        masked = jnp.where(valid, s, NEG)
        peak = jnp.max(masked, axis=1, keepdims=True)
        weights = jnp.exp(masked - peak)
        total = jnp.sum(weights, axis=1, keepdims=True)
        acc_ref[:, cols] = jnp.dot(
            weights.astype(jnp.bfloat16), v_ref[:, cols], preferred_element_type=jnp.float32
        )
        stat_ref[:, h : h + 1] = peak
        stat_ref[:, heads + h : heads + h + 1] = total


def latent_attention(latent_query, keyed, valued, valid_count):
    latent_count, width = latent_query.shape
    heads = width // HD
    tl = min(256, latent_count)
    scal = jnp.reshape(valid_count, (1,)).astype(jnp.int32)
    kernel = functools.partial(latent_kernel, heads=heads, scale=HD ** (-0.5))
    frame_count = keyed.shape[0]
    cost = pl.CostEstimate(
        flops=4 * latent_count * frame_count * width,
        transcendentals=latent_count * frame_count * heads,
        bytes_accessed=2 * (latent_query.size + 2 * keyed.size) + 4 * latent_count * (width + 128),
    )
    acc, stat = pl.pallas_call(
        kernel,
        cost_estimate=cost,
        out_shape=(
            jax.ShapeDtypeStruct((latent_count, width), jnp.float32),
            jax.ShapeDtypeStruct((latent_count, 128), jnp.float32),
        ),
        grid_spec=pltpu.PrefetchScalarGridSpec(
            num_scalar_prefetch=1,
            grid=(latent_count // tl,),
            in_specs=[
                pl.BlockSpec((tl, width), lambda i, s: (i, 0)),
                pl.BlockSpec((frame_count, width), lambda i, s: (0, 1)),
                pl.BlockSpec((frame_count, width), lambda i, s: (0, 2)),
            ],
            out_specs=[
                pl.BlockSpec((tl, width), lambda i, s: (i, 0)),
                pl.BlockSpec((tl, 128), lambda i, s: (i, 0)),
            ],
        ),
    )(scal, latent_query, keyed, valued)
    return stat[:, :heads], stat[:, heads : 2 * heads], acc


def shifted_blocks(payload, axis, rows):
    count = lax.axis_size(axis)
    place = lax.axis_index(axis)
    own = lax.dynamic_slice_in_dim(payload, place * rows, rows, 0)
    parts = [own]
    for shift in range(1, count):
        target = (place + shift) % count
        block = lax.dynamic_slice_in_dim(payload, target * rows, rows, 0)
        pairs = [(i, (i + shift) % count) for i in range(count)]
        parts.append(lax.ppermute(block, axis, pairs))
    return jnp.stack(parts)


def column_sum(partial, axis):
    count = lax.axis_size(axis)
    place = lax.axis_index(axis)
    width = partial.shape[1] // count
    own = lax.dynamic_slice_in_dim(partial, place * width, width, 1)
    total = own.astype(jnp.float32)
    for shift in range(1, count):
        target = (place + shift) % count
        block = lax.dynamic_slice_in_dim(partial, target * width, width, 1)
        pairs = [(i, (i + shift) % count) for i in range(count)]
        total = total + lax.ppermute(block, axis, pairs).astype(jnp.float32)
    return total.astype(jnp.bfloat16)


def send_order(axis):
    count = lax.axis_size(axis)
    place = lax.axis_index(axis)
    if count % 2 != 0:
        return [(place + j) % count for j in range(count)]
    chips = count // 2
    core = place % 2
    chip = place // 2
    theirs = [2 * ((chip + d) % chips) + 1 - core for d in range(chips)]
    mine = [2 * ((chip + d) % chips) + core for d in range(chips)]
    return theirs + mine


def ordered_columns(weight, axis):
    count = lax.axis_size(axis)
    width = weight.shape[1] // count
    return jnp.concatenate(
        [lax.dynamic_slice_in_dim(weight, b * width, width, 1) for b in send_order(axis)], axis=1
    )


def chip_pair_sums(blocks, axis):
    count = lax.axis_size(axis)
    chips = count // 2
    swap = [(i, i ^ 1) for i in range(count)]
    received = lax.ppermute(blocks[:chips], axis, swap)
    return [
        (blocks[chips + d].astype(jnp.float32) + received[d].astype(jnp.float32)).astype(
            jnp.bfloat16
        )
        for d in range(chips)
    ]


def cross_chip_sum(chip_sums, axis):
    count = lax.axis_size(axis)
    chips = count // 2
    total = chip_sums[0].astype(jnp.float32)
    for d in range(1, chips):
        pairs = [(2 * c + k, 2 * ((c + d) % chips) + k) for c in range(chips) for k in range(2)]
        total = total + lax.ppermute(chip_sums[d], axis, pairs).astype(jnp.float32)
    return total.astype(jnp.bfloat16)


def plain_block_sum(blocks, axis):
    count = lax.axis_size(axis)
    total = blocks[0].astype(jnp.float32)
    for shift in range(1, count):
        pairs = [(i, (i + shift) % count) for i in range(count)]
        total = total + lax.ppermute(blocks[shift], axis, pairs).astype(jnp.float32)
    return total.astype(jnp.bfloat16)


def split_three(values):
    hi = values.astype(jnp.bfloat16)
    rest = values - hi.astype(jnp.float32)
    mid = rest.astype(jnp.bfloat16)
    lo = (rest - mid.astype(jnp.float32)).astype(jnp.bfloat16)
    return [hi, mid, lo]


def exchange_rows(payload, axis, rows):
    count = lax.axis_size(axis)
    place = lax.axis_index(axis)
    parts = [lax.dynamic_slice_in_dim(payload, place * rows, rows, 0)]
    for shift in range(1, count):
        pairs = [(i, (i + shift) % count) for i in range(count)]
        block = lax.dynamic_slice_in_dim(payload, ((place + shift) % count) * rows, rows, 0)
        parts.append(lax.ppermute(block, axis, pairs))
    return parts


def merge_kernel(*refs, heads):
    part_refs, out_ref = refs[:-1], refs[-1]
    width = out_ref.shape[1]
    stat_width = 2 * heads

    stat_blocks = []
    for ref in part_refs:
        raw = ref[:, width : width + 3 * stat_width].astype(jnp.float32)
        stat_blocks.append(
            raw[:, 0:stat_width]
            + raw[:, stat_width : 2 * stat_width]
            + raw[:, 2 * stat_width : 3 * stat_width]
        )

    def column(k, c):
        return stat_blocks[k][:, c : c + 1]

    for h in range(heads):
        peaks = [column(k, h) for k in range(len(part_refs))]
        joint = peaks[0]
        for peak in peaks[1:]:
            joint = jnp.maximum(joint, peak)
        total = jnp.zeros_like(joint)
        accum = jnp.zeros((out_ref.shape[0], HD), jnp.float32)
        for k, (ref, peak) in enumerate(zip(part_refs, peaks)):
            factor = jnp.exp(peak - joint)
            total = total + column(k, heads + h) * factor
            accum = accum + ref[:, h * HD : (h + 1) * HD].astype(jnp.float32) * factor
        out_ref[:, h * HD : (h + 1) * HD] = (accum / total).astype(jnp.bfloat16)


def merge_parts(parts, width, heads):
    rows = parts[0].shape[0]
    return pl.pallas_call(
        functools.partial(merge_kernel, heads=heads),
        out_shape=jax.ShapeDtypeStruct((rows, width), jnp.bfloat16),
        in_specs=[pl.BlockSpec(memory_space=pltpu.VMEM)] * len(parts),
        out_specs=pl.BlockSpec(memory_space=pltpu.VMEM),
    )(*parts)


def per_device(
    frames, latents, lengths, w_query, w_key, w_value, w_out, w_latent_query, w_latent_out
):
    frame_count = frames.shape[0]
    head_width = w_query.shape[1]
    heads_here = head_width // HD
    seq_devices = lax.axis_size("seq")
    seq_place = lax.axis_index("seq")
    first_frame = seq_place * frame_count
    length = lengths[0]
    qkv = project(frames, jnp.concatenate([w_query, w_key, w_value], axis=1))
    keyed = qkv[:, head_width : 2 * head_width]
    valued = qkv[:, 2 * head_width :]
    low, high = halos(keyed, valued, "seq")
    chunks = 2 if frame_count % 512 == 0 else 1
    chunk_rows = frame_count // chunks
    head_devices = lax.axis_size("head")
    paired = head_devices % 2 == 0
    w_ordered = ordered_columns(w_out, "head")
    parts = [
        window_attention(
            qkv, qkv, qkv, low, high, w_ordered, first_frame, length,
            c * chunk_rows, chunk_rows, head_devices,
        )
        for c in range(chunks)
    ]
    latent_count = latents.shape[0]
    latent_query = project(latents, w_latent_query)
    valid_count = jnp.clip(length - first_frame, 0, frame_count)
    frame_parts = []
    if paired:
        first_sums = chip_pair_sums(parts[0], "head")
        first_sums, rest, qkv = lax.optimization_barrier((first_sums, parts[1:], qkv))
        frame_parts.append(cross_chip_sum(first_sums, "head"))
        rest_sums = [chip_pair_sums(blocks, "head") for blocks in rest]
    else:
        frame_parts = [plain_block_sum(blocks, "head") for blocks in parts]
    peaks, totals, local_accum = latent_attention(latent_query, qkv, qkv, valid_count)
    payload = jnp.concatenate(
        [local_accum.astype(jnp.bfloat16)] + split_three(jnp.concatenate([peaks, totals], axis=1)),
        axis=1,
    )
    if paired:
        rest_sums, payload = lax.optimization_barrier((rest_sums, payload))
        frame_parts.extend(cross_chip_sum(sums, "head") for sums in rest_sums)
    frames_out = jnp.concatenate(frame_parts, axis=0)
    rows_here = latent_count // seq_devices
    parts = exchange_rows(payload, "seq", rows_here)
    summary = merge_parts(parts, head_width, heads_here)
    if paired:
        latent_terms = jnp.dot(
            summary, ordered_columns(w_latent_out, "head"), preferred_element_type=jnp.float32
        ).astype(jnp.bfloat16)
        block_width = latent_terms.shape[1] // head_devices
        latent_blocks = jnp.stack(
            [latent_terms[:, j * block_width : (j + 1) * block_width] for j in range(head_devices)]
        )
        latents_out = cross_chip_sum(chip_pair_sums(latent_blocks, "head"), "head")
    else:
        latent_terms = jnp.dot(summary, w_latent_out, preferred_element_type=jnp.float32)
        latents_out = column_sum(latent_terms.astype(jnp.bfloat16), "head")
    return (frames_out, latents_out)


def solution(mesh):
    return jax.shard_map(
        per_device,
        mesh=mesh,
        in_specs=(
            P(("groups", "seq"), None),
            P(),
            P("groups"),
            P(None, "head"),
            P(None, "head"),
            P(None, "head"),
            P("head", None),
            P(None, "head"),
            P("head", None),
        ),
        out_specs=(P(("groups", "seq"), "head"), P(("groups", "seq"), "head")),
        check_vma=False,
    )
```

```python
import functools

import jax
import jax.numpy as jnp
from jax import lax
from jax.experimental import pallas as pl
from jax.experimental.pallas import tpu as pltpu
from jax.sharding import PartitionSpec as P

HD = 64
HALF = 256
NEG = -1e30


def halos(keyed, valued, axis):
    count = lax.axis_size(axis)
    forward = [(i, i + 1) for i in range(count - 1)]
    backward = [(target, source) for source, target in forward]
    tail = jnp.concatenate([keyed[-HALF:], valued[-HALF:]], axis=1)
    head = jnp.concatenate([keyed[:HALF], valued[:HALF]], axis=1)
    return lax.ppermute(tail, axis, forward), lax.ppermute(head, axis, backward)


def project(source, weight):
    return jnp.dot(source, weight, preferred_element_type=jnp.float32).astype(jnp.bfloat16)


def window_kernel(
    scal_ref, q_ref, k_ref, v_ref, low_ref, high_ref, w_ref, o_ref, kbuf, vbuf, att_ref, *,
    heads, scale
):
    tq = q_ref.shape[0]
    frame_count, width = k_ref.shape
    span = tq + 2 * HALF

    @pl.when(pl.program_id(0) == 0)
    def _fill():
        kbuf[0:HALF, :] = low_ref[:, 0:width]
        vbuf[0:HALF, :] = low_ref[:, width : 2 * width]
        kbuf[HALF : HALF + frame_count, :] = k_ref[...]
        vbuf[HALF : HALF + frame_count, :] = v_ref[...]
        kbuf[HALF + frame_count :, :] = high_ref[:, 0:width]
        vbuf[HALF + frame_count :, :] = high_ref[:, width : 2 * width]

    start = pl.multiple_of(scal_ref[2] + pl.program_id(0) * tq, tq)
    first = scal_ref[0]
    length = scal_ref[1]
    row = lax.broadcasted_iota(jnp.int32, (tq, span), 0)
    col = lax.broadcasted_iota(jnp.int32, (tq, span), 1)
    offset = col - row
    key_pos = first + start - HALF + col
    allowed = (offset >= 0) & (offset <= 2 * HALF) & (key_pos >= 0) & (key_pos < length)
    query_pos = first + start + lax.broadcasted_iota(jnp.int32, (tq, 1), 0)
    query_valid = query_pos < length
    for h in range(heads):
        cols = slice(h * HD, (h + 1) * HD)
        q = q_ref[:, cols]
        k = kbuf[pl.ds(start, span), cols]
        v = vbuf[pl.ds(start, span), cols]
        s = lax.dot_general(
            q, k, (((1,), (1,)), ((), ())), preferred_element_type=jnp.float32
        ) * scale
        masked = jnp.where(allowed, s, NEG)
        peak = jnp.max(masked, axis=1, keepdims=True)
        weights = jnp.exp(masked - peak)
        denom = jnp.sum(weights, axis=1, keepdims=True)
        blended = jnp.dot(weights.astype(jnp.bfloat16), v, preferred_element_type=jnp.float32)
        divisor = jnp.where(query_valid, denom, 1.0)
        att_ref[:, cols] = jnp.where(query_valid, blended / divisor, 0.0).astype(jnp.bfloat16)
    result = jnp.dot(att_ref[...], w_ref[...], preferred_element_type=jnp.float32)
    block_width = o_ref.shape[2]
    for b in range(o_ref.shape[0]):
        o_ref[b] = result[:, b * block_width : (b + 1) * block_width].astype(jnp.bfloat16)


def window_attention(
    query, keyed, valued, low, high, w_out, first_frame, length, row_base, rows, blocks
):
    frame_count, width = query.shape
    out_width = w_out.shape[1]
    block_width = out_width // blocks
    tq = min(512, rows)
    block_base = row_base // tq
    span = tq + 2 * HALF
    scal = jnp.array([0, 0, row_base], jnp.int32).at[0].set(first_frame).at[1].set(length)
    kernel = functools.partial(window_kernel, heads=width // HD, scale=HD ** (-0.5))
    cost = pl.CostEstimate(
        flops=4 * rows * span * width + 2 * rows * width * out_width,
        transcendentals=rows * span * (width // HD),
        bytes_accessed=2 * (2 * query.size + rows * width + 2 * low.size + w_out.size + rows * out_width),
    )
    full = lambda i, s: (0, 0)
    return pl.pallas_call(
        kernel,
        cost_estimate=cost,
        out_shape=jax.ShapeDtypeStruct((blocks, rows, block_width), jnp.bfloat16),
        grid_spec=pltpu.PrefetchScalarGridSpec(
            num_scalar_prefetch=1,
            grid=(rows // tq,),
            in_specs=[
                pl.BlockSpec((tq, width), lambda i, s: (i + block_base, 0)),
                pl.BlockSpec(keyed.shape, full),
                pl.BlockSpec(valued.shape, full),
                pl.BlockSpec(low.shape, full),
                pl.BlockSpec(high.shape, full),
                pl.BlockSpec(w_out.shape, full),
            ],
            out_specs=pl.BlockSpec((blocks, tq, block_width), lambda i, s: (0, i, 0)),
            scratch_shapes=[
                pltpu.VMEM((frame_count + 2 * HALF, width), jnp.bfloat16),
                pltpu.VMEM((frame_count + 2 * HALF, width), jnp.bfloat16),
                pltpu.VMEM((tq, width), jnp.bfloat16),
            ],
        ),
        compiler_params=pltpu.CompilerParams(dimension_semantics=("arbitrary",)),
    )(scal, query, keyed, valued, low, high, w_out)


def latent_kernel(scal_ref, q_ref, k_ref, v_ref, acc_ref, stat_ref, *, heads, scale):
    tl = q_ref.shape[0]
    frame_count = k_ref.shape[0]
    valid = lax.broadcasted_iota(jnp.int32, (tl, frame_count), 1) < scal_ref[0]
    stat_ref[...] = jnp.zeros_like(stat_ref)
    for h in range(heads):
        cols = slice(h * HD, (h + 1) * HD)
        s = lax.dot_general(
            q_ref[:, cols], k_ref[:, cols], (((1,), (1,)), ((), ())),
            preferred_element_type=jnp.float32,
        ) * scale
        masked = jnp.where(valid, s, NEG)
        peak = jnp.max(masked, axis=1, keepdims=True)
        weights = jnp.exp(masked - peak)
        total = jnp.sum(weights, axis=1, keepdims=True)
        acc_ref[:, cols] = jnp.dot(
            weights.astype(jnp.bfloat16), v_ref[:, cols], preferred_element_type=jnp.float32
        )
        stat_ref[:, h : h + 1] = peak
        stat_ref[:, heads + h : heads + h + 1] = total


def latent_attention(latent_query, keyed, valued, valid_count):
    latent_count, width = latent_query.shape
    heads = width // HD
    tl = min(256, latent_count)
    scal = jnp.reshape(valid_count, (1,)).astype(jnp.int32)
    kernel = functools.partial(latent_kernel, heads=heads, scale=HD ** (-0.5))
    frame_count = keyed.shape[0]
    cost = pl.CostEstimate(
        flops=4 * latent_count * frame_count * width,
        transcendentals=latent_count * frame_count * heads,
        bytes_accessed=2 * (latent_query.size + 2 * keyed.size) + 4 * latent_count * (width + 128),
    )
    acc, stat = pl.pallas_call(
        kernel,
        cost_estimate=cost,
        out_shape=(
            jax.ShapeDtypeStruct((latent_count, width), jnp.float32),
            jax.ShapeDtypeStruct((latent_count, 128), jnp.float32),
        ),
        grid_spec=pltpu.PrefetchScalarGridSpec(
            num_scalar_prefetch=1,
            grid=(latent_count // tl,),
            in_specs=[
                pl.BlockSpec((tl, width), lambda i, s: (i, 0)),
                pl.BlockSpec(keyed.shape, lambda i, s: (0, 0)),
                pl.BlockSpec(valued.shape, lambda i, s: (0, 0)),
            ],
            out_specs=[
                pl.BlockSpec((tl, width), lambda i, s: (i, 0)),
                pl.BlockSpec((tl, 128), lambda i, s: (i, 0)),
            ],
        ),
    )(scal, latent_query, keyed, valued)
    return stat[:, :heads], stat[:, heads : 2 * heads], acc


def shifted_blocks(payload, axis, rows):
    count = lax.axis_size(axis)
    place = lax.axis_index(axis)
    own = lax.dynamic_slice_in_dim(payload, place * rows, rows, 0)
    parts = [own]
    for shift in range(1, count):
        target = (place + shift) % count
        block = lax.dynamic_slice_in_dim(payload, target * rows, rows, 0)
        pairs = [(i, (i + shift) % count) for i in range(count)]
        parts.append(lax.ppermute(block, axis, pairs))
    return jnp.stack(parts)


def column_sum(partial, axis):
    count = lax.axis_size(axis)
    place = lax.axis_index(axis)
    width = partial.shape[1] // count
    own = lax.dynamic_slice_in_dim(partial, place * width, width, 1)
    total = own.astype(jnp.float32)
    for shift in range(1, count):
        target = (place + shift) % count
        block = lax.dynamic_slice_in_dim(partial, target * width, width, 1)
        pairs = [(i, (i + shift) % count) for i in range(count)]
        total = total + lax.ppermute(block, axis, pairs).astype(jnp.float32)
    return total.astype(jnp.bfloat16)


def send_order(axis):
    count = lax.axis_size(axis)
    place = lax.axis_index(axis)
    if count % 2 != 0:
        return [(place + j) % count for j in range(count)]
    chips = count // 2
    core = place % 2
    chip = place // 2
    theirs = [2 * ((chip + d) % chips) + 1 - core for d in range(chips)]
    mine = [2 * ((chip + d) % chips) + core for d in range(chips)]
    return theirs + mine


def ordered_columns(weight, axis):
    count = lax.axis_size(axis)
    width = weight.shape[1] // count
    return jnp.concatenate(
        [lax.dynamic_slice_in_dim(weight, b * width, width, 1) for b in send_order(axis)], axis=1
    )


def chip_pair_sums(blocks, axis):
    count = lax.axis_size(axis)
    chips = count // 2
    swap = [(i, i ^ 1) for i in range(count)]
    received = lax.ppermute(blocks[:chips], axis, swap)
    return [
        (blocks[chips + d].astype(jnp.float32) + received[d].astype(jnp.float32)).astype(
            jnp.bfloat16
        )
        for d in range(chips)
    ]


def cross_chip_sum(chip_sums, axis):
    count = lax.axis_size(axis)
    chips = count // 2
    total = chip_sums[0].astype(jnp.float32)
    for d in range(1, chips):
        pairs = [(2 * c + k, 2 * ((c + d) % chips) + k) for c in range(chips) for k in range(2)]
        total = total + lax.ppermute(chip_sums[d], axis, pairs).astype(jnp.float32)
    return total.astype(jnp.bfloat16)


def plain_block_sum(blocks, axis):
    count = lax.axis_size(axis)
    total = blocks[0].astype(jnp.float32)
    for shift in range(1, count):
        pairs = [(i, (i + shift) % count) for i in range(count)]
        total = total + lax.ppermute(blocks[shift], axis, pairs).astype(jnp.float32)
    return total.astype(jnp.bfloat16)


def split_three(values):
    hi = values.astype(jnp.bfloat16)
    rest = values - hi.astype(jnp.float32)
    mid = rest.astype(jnp.bfloat16)
    lo = (rest - mid.astype(jnp.float32)).astype(jnp.bfloat16)
    return [hi, mid, lo]


def exchange_rows(payload, axis, rows):
    count = lax.axis_size(axis)
    place = lax.axis_index(axis)
    parts = [lax.dynamic_slice_in_dim(payload, place * rows, rows, 0)]
    for shift in range(1, count):
        pairs = [(i, (i + shift) % count) for i in range(count)]
        block = lax.dynamic_slice_in_dim(payload, ((place + shift) % count) * rows, rows, 0)
        parts.append(lax.ppermute(block, axis, pairs))
    return parts


def merge_kernel(*refs, heads):
    part_refs, out_ref = refs[:-1], refs[-1]
    width = out_ref.shape[1]
    stat_width = 2 * heads

    stat_blocks = []
    for ref in part_refs:
        raw = ref[:, width : width + 3 * stat_width].astype(jnp.float32)
        stat_blocks.append(
            raw[:, 0:stat_width]
            + raw[:, stat_width : 2 * stat_width]
            + raw[:, 2 * stat_width : 3 * stat_width]
        )

    def column(k, c):
        return stat_blocks[k][:, c : c + 1]

    for h in range(heads):
        peaks = [column(k, h) for k in range(len(part_refs))]
        joint = peaks[0]
        for peak in peaks[1:]:
            joint = jnp.maximum(joint, peak)
        total = jnp.zeros_like(joint)
        accum = jnp.zeros((out_ref.shape[0], HD), jnp.float32)
        for k, (ref, peak) in enumerate(zip(part_refs, peaks)):
            factor = jnp.exp(peak - joint)
            total = total + column(k, heads + h) * factor
            accum = accum + ref[:, h * HD : (h + 1) * HD].astype(jnp.float32) * factor
        out_ref[:, h * HD : (h + 1) * HD] = (accum / total).astype(jnp.bfloat16)


def merge_parts(parts, width, heads):
    rows = parts[0].shape[0]
    return pl.pallas_call(
        functools.partial(merge_kernel, heads=heads),
        out_shape=jax.ShapeDtypeStruct((rows, width), jnp.bfloat16),
        in_specs=[pl.BlockSpec(memory_space=pltpu.VMEM)] * len(parts),
        out_specs=pl.BlockSpec(memory_space=pltpu.VMEM),
    )(*parts)


def per_device(
    frames, latents, lengths, w_query, w_key, w_value, w_out, w_latent_query, w_latent_out
):
    frame_count = frames.shape[0]
    head_width = w_query.shape[1]
    heads_here = head_width // HD
    seq_devices = lax.axis_size("seq")
    seq_place = lax.axis_index("seq")
    first_frame = seq_place * frame_count
    length = lengths[0]
    query = project(frames, w_query)
    keyed = project(frames, w_key)
    valued = project(frames, w_value)
    low, high = halos(keyed, valued, "seq")
    chunks = 1
    chunk_rows = frame_count // chunks
    head_devices = lax.axis_size("head")
    paired = head_devices % 2 == 0
    w_ordered = ordered_columns(w_out, "head")
    parts = [
        window_attention(
            query, keyed, valued, low, high, w_ordered, first_frame, length,
            c * chunk_rows, chunk_rows, head_devices,
        )
        for c in range(chunks)
    ]
    latent_count = latents.shape[0]
    latent_query = project(latents, w_latent_query)
    valid_count = jnp.clip(length - first_frame, 0, frame_count)
    frame_parts = []
    if paired:
        first_sums = chip_pair_sums(parts[0], "head")
        first_sums, rest, keyed, valued = lax.optimization_barrier(
            (first_sums, parts[1:], keyed, valued)
        )
        frame_parts.append(cross_chip_sum(first_sums, "head"))
        rest_sums = [chip_pair_sums(blocks, "head") for blocks in rest]
    else:
        frame_parts = [plain_block_sum(blocks, "head") for blocks in parts]
    peaks, totals, local_accum = latent_attention(latent_query, keyed, valued, valid_count)
    payload = jnp.concatenate(
        [local_accum.astype(jnp.bfloat16)] + split_three(jnp.concatenate([peaks, totals], axis=1)),
        axis=1,
    )
    if paired:
        rest_sums, payload = lax.optimization_barrier((rest_sums, payload))
        frame_parts.extend(cross_chip_sum(sums, "head") for sums in rest_sums)
    frames_out = jnp.concatenate(frame_parts, axis=0)
    rows_here = latent_count // seq_devices
    parts = exchange_rows(payload, "seq", rows_here)
    summary = merge_parts(parts, head_width, heads_here)
    if paired:
        latent_terms = jnp.dot(
            summary, ordered_columns(w_latent_out, "head"), preferred_element_type=jnp.float32
        ).astype(jnp.bfloat16)
        block_width = latent_terms.shape[1] // head_devices
        latent_blocks = jnp.stack(
            [latent_terms[:, j * block_width : (j + 1) * block_width] for j in range(head_devices)]
        )
        latents_out = cross_chip_sum(chip_pair_sums(latent_blocks, "head"), "head")
    else:
        latent_terms = jnp.dot(summary, w_latent_out, preferred_element_type=jnp.float32)
        latents_out = column_sum(latent_terms.astype(jnp.bfloat16), "head")
    return (frames_out, latents_out)


def solution(mesh):
    return jax.shard_map(
        per_device,
        mesh=mesh,
        in_specs=(
            P(("groups", "seq"), None),
            P(),
            P("groups"),
            P(None, "head"),
            P(None, "head"),
            P(None, "head"),
            P("head", None),
            P(None, "head"),
            P("head", None),
        ),
        out_specs=(P(("groups", "seq"), "head"), P(("groups", "seq"), "head")),
        check_vma=False,
    )
```

```python
import functools

import jax
import jax.numpy as jnp
from jax import lax
from jax.experimental import pallas as pl
from jax.experimental.pallas import tpu as pltpu
from jax.sharding import PartitionSpec as P

HD = 64
HALF = 256
NEG = -1e30


def halos(keyed, valued, axis):
    count = lax.axis_size(axis)
    forward = [(i, i + 1) for i in range(count - 1)]
    backward = [(target, source) for source, target in forward]
    tail = jnp.concatenate([keyed[-HALF:], valued[-HALF:]], axis=1)
    head = jnp.concatenate([keyed[:HALF], valued[:HALF]], axis=1)
    return lax.ppermute(tail, axis, forward), lax.ppermute(head, axis, backward)


def project(source, weight):
    return jnp.dot(source, weight, preferred_element_type=jnp.float32).astype(jnp.bfloat16)


def window_kernel(
    scal_ref, q_ref, k_ref, v_ref, low_ref, high_ref, w_ref, o_ref, kbuf, vbuf, att_ref, *,
    heads, scale
):
    tq = q_ref.shape[0]
    frame_count, width = k_ref.shape
    span = tq + 2 * HALF

    @pl.when(pl.program_id(0) == 0)
    def _fill():
        kbuf[0:HALF, :] = low_ref[:, 0:width]
        vbuf[0:HALF, :] = low_ref[:, width : 2 * width]
        kbuf[HALF : HALF + frame_count, :] = k_ref[...]
        vbuf[HALF : HALF + frame_count, :] = v_ref[...]
        kbuf[HALF + frame_count :, :] = high_ref[:, 0:width]
        vbuf[HALF + frame_count :, :] = high_ref[:, width : 2 * width]

    start = pl.multiple_of(scal_ref[2] + pl.program_id(0) * tq, tq)
    first = scal_ref[0]
    length = scal_ref[1]
    row = lax.broadcasted_iota(jnp.int32, (tq, span), 0)
    col = lax.broadcasted_iota(jnp.int32, (tq, span), 1)
    offset = col - row
    key_pos = first + start - HALF + col
    allowed = (offset >= 0) & (offset <= 2 * HALF) & (key_pos >= 0) & (key_pos < length)
    query_pos = first + start + lax.broadcasted_iota(jnp.int32, (tq, 1), 0)
    query_valid = query_pos < length
    for h in range(heads):
        cols = slice(h * HD, (h + 1) * HD)
        q = q_ref[:, cols]
        k = kbuf[pl.ds(start, span), cols]
        v = vbuf[pl.ds(start, span), cols]
        s = lax.dot_general(
            q, k, (((1,), (1,)), ((), ())), preferred_element_type=jnp.float32
        ) * scale
        masked = jnp.where(allowed, s, NEG)
        peak = jnp.max(masked, axis=1, keepdims=True)
        weights = jnp.exp(masked - peak)
        denom = jnp.sum(weights, axis=1, keepdims=True)
        blended = jnp.dot(weights.astype(jnp.bfloat16), v, preferred_element_type=jnp.float32)
        divisor = jnp.where(query_valid, denom, 1.0)
        att_ref[:, cols] = jnp.where(query_valid, blended / divisor, 0.0).astype(jnp.bfloat16)
    result = jnp.dot(att_ref[...], w_ref[...], preferred_element_type=jnp.float32)
    block_width = o_ref.shape[2]
    for b in range(o_ref.shape[0]):
        o_ref[b] = result[:, b * block_width : (b + 1) * block_width].astype(jnp.bfloat16)


def window_attention(
    query, keyed, valued, low, high, w_out, first_frame, length, row_base, rows, blocks
):
    frame_count, width = query.shape
    out_width = w_out.shape[1]
    block_width = out_width // blocks
    tq = min(512, rows)
    block_base = row_base // tq
    span = tq + 2 * HALF
    scal = jnp.array([0, 0, row_base], jnp.int32).at[0].set(first_frame).at[1].set(length)
    kernel = functools.partial(window_kernel, heads=width // HD, scale=HD ** (-0.5))
    cost = pl.CostEstimate(
        flops=4 * rows * span * width + 2 * rows * width * out_width,
        transcendentals=rows * span * (width // HD),
        bytes_accessed=2 * (2 * query.size + rows * width + 2 * low.size + w_out.size + rows * out_width),
    )
    full = lambda i, s: (0, 0)
    return pl.pallas_call(
        kernel,
        cost_estimate=cost,
        out_shape=jax.ShapeDtypeStruct((blocks, rows, block_width), jnp.bfloat16),
        grid_spec=pltpu.PrefetchScalarGridSpec(
            num_scalar_prefetch=1,
            grid=(rows // tq,),
            in_specs=[
                pl.BlockSpec((tq, width), lambda i, s: (i + block_base, 0)),
                pl.BlockSpec(keyed.shape, full),
                pl.BlockSpec(valued.shape, full),
                pl.BlockSpec(low.shape, full),
                pl.BlockSpec(high.shape, full),
                pl.BlockSpec(w_out.shape, full),
            ],
            out_specs=pl.BlockSpec((blocks, tq, block_width), lambda i, s: (0, i, 0)),
            scratch_shapes=[
                pltpu.VMEM((frame_count + 2 * HALF, width), jnp.bfloat16),
                pltpu.VMEM((frame_count + 2 * HALF, width), jnp.bfloat16),
                pltpu.VMEM((tq, width), jnp.bfloat16),
            ],
        ),
        compiler_params=pltpu.CompilerParams(dimension_semantics=("arbitrary",)),
    )(scal, query, keyed, valued, low, high, w_out)


def latent_kernel(scal_ref, q_ref, k_ref, v_ref, acc_ref, stat_ref, *, heads, scale):
    tl = q_ref.shape[0]
    frame_count = k_ref.shape[0]
    valid = lax.broadcasted_iota(jnp.int32, (tl, frame_count), 1) < scal_ref[0]
    stat_ref[...] = jnp.zeros_like(stat_ref)
    for h in range(heads):
        cols = slice(h * HD, (h + 1) * HD)
        s = lax.dot_general(
            q_ref[:, cols], k_ref[:, cols], (((1,), (1,)), ((), ())),
            preferred_element_type=jnp.float32,
        ) * scale
        masked = jnp.where(valid, s, NEG)
        peak = jnp.max(masked, axis=1, keepdims=True)
        weights = jnp.exp(masked - peak)
        total = jnp.sum(weights, axis=1, keepdims=True)
        acc_ref[:, cols] = jnp.dot(
            weights.astype(jnp.bfloat16), v_ref[:, cols], preferred_element_type=jnp.float32
        )
        stat_ref[:, h : h + 1] = peak
        stat_ref[:, heads + h : heads + h + 1] = total


def latent_attention(latent_query, keyed, valued, valid_count):
    latent_count, width = latent_query.shape
    heads = width // HD
    tl = min(256, latent_count)
    scal = jnp.reshape(valid_count, (1,)).astype(jnp.int32)
    kernel = functools.partial(latent_kernel, heads=heads, scale=HD ** (-0.5))
    frame_count = keyed.shape[0]
    cost = pl.CostEstimate(
        flops=4 * latent_count * frame_count * width,
        transcendentals=latent_count * frame_count * heads,
        bytes_accessed=2 * (latent_query.size + 2 * keyed.size) + 4 * latent_count * (width + 128),
    )
    acc, stat = pl.pallas_call(
        kernel,
        cost_estimate=cost,
        out_shape=(
            jax.ShapeDtypeStruct((latent_count, width), jnp.float32),
            jax.ShapeDtypeStruct((latent_count, 128), jnp.float32),
        ),
        grid_spec=pltpu.PrefetchScalarGridSpec(
            num_scalar_prefetch=1,
            grid=(latent_count // tl,),
            in_specs=[
                pl.BlockSpec((tl, width), lambda i, s: (i, 0)),
                pl.BlockSpec(keyed.shape, lambda i, s: (0, 0)),
                pl.BlockSpec(valued.shape, lambda i, s: (0, 0)),
            ],
            out_specs=[
                pl.BlockSpec((tl, width), lambda i, s: (i, 0)),
                pl.BlockSpec((tl, 128), lambda i, s: (i, 0)),
            ],
        ),
    )(scal, latent_query, keyed, valued)
    return stat[:, :heads], stat[:, heads : 2 * heads], acc


def shifted_blocks(payload, axis, rows):
    count = lax.axis_size(axis)
    place = lax.axis_index(axis)
    own = lax.dynamic_slice_in_dim(payload, place * rows, rows, 0)
    parts = [own]
    for shift in range(1, count):
        target = (place + shift) % count
        block = lax.dynamic_slice_in_dim(payload, target * rows, rows, 0)
        pairs = [(i, (i + shift) % count) for i in range(count)]
        parts.append(lax.ppermute(block, axis, pairs))
    return jnp.stack(parts)


def column_sum(partial, axis):
    count = lax.axis_size(axis)
    place = lax.axis_index(axis)
    width = partial.shape[1] // count
    own = lax.dynamic_slice_in_dim(partial, place * width, width, 1)
    total = own.astype(jnp.float32)
    for shift in range(1, count):
        target = (place + shift) % count
        block = lax.dynamic_slice_in_dim(partial, target * width, width, 1)
        pairs = [(i, (i + shift) % count) for i in range(count)]
        total = total + lax.ppermute(block, axis, pairs).astype(jnp.float32)
    return total.astype(jnp.bfloat16)


def send_order(axis):
    count = lax.axis_size(axis)
    place = lax.axis_index(axis)
    if count % 2 != 0:
        return [(place + j) % count for j in range(count)]
    chips = count // 2
    core = place % 2
    chip = place // 2
    theirs = [2 * ((chip + d) % chips) + 1 - core for d in range(chips)]
    mine = [2 * ((chip + d) % chips) + core for d in range(chips)]
    return theirs + mine


def ordered_columns(weight, axis):
    count = lax.axis_size(axis)
    width = weight.shape[1] // count
    return jnp.concatenate(
        [lax.dynamic_slice_in_dim(weight, b * width, width, 1) for b in send_order(axis)], axis=1
    )


def chip_pair_sums(blocks, axis):
    count = lax.axis_size(axis)
    chips = count // 2
    swap = [(i, i ^ 1) for i in range(count)]
    received = lax.ppermute(blocks[:chips], axis, swap)
    return [
        (blocks[chips + d].astype(jnp.float32) + received[d].astype(jnp.float32)).astype(
            jnp.bfloat16
        )
        for d in range(chips)
    ]


def cross_chip_sum(chip_sums, axis):
    count = lax.axis_size(axis)
    chips = count // 2
    total = chip_sums[0].astype(jnp.float32)
    for d in range(1, chips):
        pairs = [(2 * c + k, 2 * ((c + d) % chips) + k) for c in range(chips) for k in range(2)]
        total = total + lax.ppermute(chip_sums[d], axis, pairs).astype(jnp.float32)
    return total.astype(jnp.bfloat16)


def plain_block_sum(blocks, axis):
    count = lax.axis_size(axis)
    total = blocks[0].astype(jnp.float32)
    for shift in range(1, count):
        pairs = [(i, (i + shift) % count) for i in range(count)]
        total = total + lax.ppermute(blocks[shift], axis, pairs).astype(jnp.float32)
    return total.astype(jnp.bfloat16)


def split_three(values):
    hi = values.astype(jnp.bfloat16)
    rest = values - hi.astype(jnp.float32)
    mid = rest.astype(jnp.bfloat16)
    lo = (rest - mid.astype(jnp.float32)).astype(jnp.bfloat16)
    return [hi, mid, lo]


def exchange_rows(payload, axis, rows):
    count = lax.axis_size(axis)
    place = lax.axis_index(axis)
    parts = [lax.dynamic_slice_in_dim(payload, place * rows, rows, 0)]
    for shift in range(1, count):
        pairs = [(i, (i + shift) % count) for i in range(count)]
        block = lax.dynamic_slice_in_dim(payload, ((place + shift) % count) * rows, rows, 0)
        parts.append(lax.ppermute(block, axis, pairs))
    return parts


def merge_kernel(*refs, heads):
    part_refs, out_ref = refs[:-1], refs[-1]
    width = out_ref.shape[1]
    stat_width = 2 * heads

    stat_blocks = []
    for ref in part_refs:
        raw = ref[:, width : width + 3 * stat_width].astype(jnp.float32)
        stat_blocks.append(
            raw[:, 0:stat_width]
            + raw[:, stat_width : 2 * stat_width]
            + raw[:, 2 * stat_width : 3 * stat_width]
        )

    def column(k, c):
        return stat_blocks[k][:, c : c + 1]

    for h in range(heads):
        peaks = [column(k, h) for k in range(len(part_refs))]
        joint = peaks[0]
        for peak in peaks[1:]:
            joint = jnp.maximum(joint, peak)
        total = jnp.zeros_like(joint)
        accum = jnp.zeros((out_ref.shape[0], HD), jnp.float32)
        for k, (ref, peak) in enumerate(zip(part_refs, peaks)):
            factor = jnp.exp(peak - joint)
            total = total + column(k, heads + h) * factor
            accum = accum + ref[:, h * HD : (h + 1) * HD].astype(jnp.float32) * factor
        out_ref[:, h * HD : (h + 1) * HD] = (accum / total).astype(jnp.bfloat16)


def merge_parts(parts, width, heads):
    rows = parts[0].shape[0]
    return pl.pallas_call(
        functools.partial(merge_kernel, heads=heads),
        out_shape=jax.ShapeDtypeStruct((rows, width), jnp.bfloat16),
        in_specs=[pl.BlockSpec(memory_space=pltpu.VMEM)] * len(parts),
        out_specs=pl.BlockSpec(memory_space=pltpu.VMEM),
    )(*parts)


def per_device(
    frames, latents, lengths, w_query, w_key, w_value, w_out, w_latent_query, w_latent_out
):
    frame_count = frames.shape[0]
    head_width = w_query.shape[1]
    heads_here = head_width // HD
    seq_devices = lax.axis_size("seq")
    seq_place = lax.axis_index("seq")
    first_frame = seq_place * frame_count
    length = lengths[0]
    query = project(frames, w_query)
    keyed = project(frames, w_key)
    valued = project(frames, w_value)
    low, high = halos(keyed, valued, "seq")
    chunks = 1
    chunk_rows = frame_count // chunks
    head_devices = lax.axis_size("head")
    paired = head_devices % 2 == 0
    w_ordered = ordered_columns(w_out, "head")
    latent_count = latents.shape[0]
    latent_query = project(latents, w_latent_query)
    valid_count = jnp.clip(length - first_frame, 0, frame_count)
    peaks, totals, local_accum = latent_attention(latent_query, keyed, valued, valid_count)
    payload = jnp.concatenate(
        [local_accum.astype(jnp.bfloat16)] + split_three(jnp.concatenate([peaks, totals], axis=1)),
        axis=1,
    )
    payload, query, keyed, valued, low, high = lax.optimization_barrier(
        (payload, query, keyed, valued, low, high)
    )
    rows_here = latent_count // seq_devices
    parts = exchange_rows(payload, "seq", rows_here)
    windows = [
        window_attention(
            query, keyed, valued, low, high, w_ordered, first_frame, length,
            c * chunk_rows, chunk_rows, head_devices,
        )
        for c in range(chunks)
    ]
    if paired:
        frame_parts = [cross_chip_sum(chip_pair_sums(blocks, "head"), "head") for blocks in windows]
    else:
        frame_parts = [plain_block_sum(blocks, "head") for blocks in windows]
    frames_out = jnp.concatenate(frame_parts, axis=0)
    summary = merge_parts(parts, head_width, heads_here)
    if paired:
        latent_terms = jnp.dot(
            summary, ordered_columns(w_latent_out, "head"), preferred_element_type=jnp.float32
        ).astype(jnp.bfloat16)
        block_width = latent_terms.shape[1] // head_devices
        latent_blocks = jnp.stack(
            [latent_terms[:, j * block_width : (j + 1) * block_width] for j in range(head_devices)]
        )
        latents_out = cross_chip_sum(chip_pair_sums(latent_blocks, "head"), "head")
    else:
        latent_terms = jnp.dot(summary, w_latent_out, preferred_element_type=jnp.float32)
        latents_out = column_sum(latent_terms.astype(jnp.bfloat16), "head")
    return (frames_out, latents_out)


def solution(mesh):
    return jax.shard_map(
        per_device,
        mesh=mesh,
        in_specs=(
            P(("groups", "seq"), None),
            P(),
            P("groups"),
            P(None, "head"),
            P(None, "head"),
            P(None, "head"),
            P("head", None),
            P(None, "head"),
            P("head", None),
        ),
        out_specs=(P(("groups", "seq"), "head"), P(("groups", "seq"), "head")),
        check_vma=False,
    )
```

```python
import functools

import jax
import jax.numpy as jnp
from jax import lax
from jax.experimental import pallas as pl
from jax.experimental.pallas import tpu as pltpu
from jax.sharding import PartitionSpec as P

HD = 64
HALF = 256
NEG = -1e30


def halos(keyed, valued, axis):
    count = lax.axis_size(axis)
    forward = [(i, i + 1) for i in range(count - 1)]
    backward = [(target, source) for source, target in forward]
    tail = jnp.concatenate([keyed[-HALF:], valued[-HALF:]], axis=1)
    head = jnp.concatenate([keyed[:HALF], valued[:HALF]], axis=1)
    return lax.ppermute(tail, axis, forward), lax.ppermute(head, axis, backward)


def project(source, weight):
    return jnp.dot(source, weight, preferred_element_type=jnp.float32).astype(jnp.bfloat16)


def window_kernel(
    scal_ref, q_ref, k_ref, v_ref, low_ref, high_ref, w_ref, o_ref, kbuf, vbuf, att_ref, *,
    heads, scale
):
    tq = q_ref.shape[0]
    frame_count, width = k_ref.shape
    span = tq + 2 * HALF

    @pl.when(pl.program_id(0) == 0)
    def _fill():
        kbuf[0:HALF, :] = low_ref[:, 0:width]
        vbuf[0:HALF, :] = low_ref[:, width : 2 * width]
        kbuf[HALF : HALF + frame_count, :] = k_ref[...]
        vbuf[HALF : HALF + frame_count, :] = v_ref[...]
        kbuf[HALF + frame_count :, :] = high_ref[:, 0:width]
        vbuf[HALF + frame_count :, :] = high_ref[:, width : 2 * width]

    start = pl.multiple_of(scal_ref[2] + pl.program_id(0) * tq, tq)
    first = scal_ref[0]
    length = scal_ref[1]
    row = lax.broadcasted_iota(jnp.int32, (tq, span), 0)
    col = lax.broadcasted_iota(jnp.int32, (tq, span), 1)
    offset = col - row
    key_pos = first + start - HALF + col
    allowed = (offset >= 0) & (offset <= 2 * HALF) & (key_pos >= 0) & (key_pos < length)
    query_pos = first + start + lax.broadcasted_iota(jnp.int32, (tq, 1), 0)
    query_valid = query_pos < length
    for h in range(heads):
        cols = slice(h * HD, (h + 1) * HD)
        q = q_ref[:, cols]
        k = kbuf[pl.ds(start, span), cols]
        v = vbuf[pl.ds(start, span), cols]
        s = lax.dot_general(
            q, k, (((1,), (1,)), ((), ())), preferred_element_type=jnp.float32
        ) * scale
        masked = jnp.where(allowed, s, NEG)
        peak = jnp.max(masked, axis=1, keepdims=True)
        weights = jnp.exp(masked - peak)
        denom = jnp.sum(weights, axis=1, keepdims=True)
        blended = jnp.dot(weights.astype(jnp.bfloat16), v, preferred_element_type=jnp.float32)
        divisor = jnp.where(query_valid, denom, 1.0)
        att_ref[:, cols] = jnp.where(query_valid, blended / divisor, 0.0).astype(jnp.bfloat16)
    result = jnp.dot(att_ref[...], w_ref[...], preferred_element_type=jnp.float32)
    block_width = o_ref.shape[2]
    for b in range(o_ref.shape[0]):
        o_ref[b] = result[:, b * block_width : (b + 1) * block_width].astype(jnp.bfloat16)


def window_attention(
    query, keyed, valued, low, high, w_out, first_frame, length, row_base, rows, blocks
):
    frame_count, width = query.shape
    out_width = w_out.shape[1]
    block_width = out_width // blocks
    tq = min(512, rows)
    block_base = row_base // tq
    span = tq + 2 * HALF
    scal = jnp.array([0, 0, row_base], jnp.int32).at[0].set(first_frame).at[1].set(length)
    kernel = functools.partial(window_kernel, heads=width // HD, scale=HD ** (-0.5))
    cost = pl.CostEstimate(
        flops=4 * rows * span * width + 2 * rows * width * out_width,
        transcendentals=rows * span * (width // HD),
        bytes_accessed=2 * (2 * query.size + rows * width + 2 * low.size + w_out.size + rows * out_width),
    )
    full = lambda i, s: (0, 0)
    return pl.pallas_call(
        kernel,
        cost_estimate=cost,
        out_shape=jax.ShapeDtypeStruct((blocks, rows, block_width), jnp.bfloat16),
        grid_spec=pltpu.PrefetchScalarGridSpec(
            num_scalar_prefetch=1,
            grid=(rows // tq,),
            in_specs=[
                pl.BlockSpec((tq, width), lambda i, s: (i + block_base, 0)),
                pl.BlockSpec(keyed.shape, full),
                pl.BlockSpec(valued.shape, full),
                pl.BlockSpec(low.shape, full),
                pl.BlockSpec(high.shape, full),
                pl.BlockSpec(w_out.shape, full),
            ],
            out_specs=pl.BlockSpec((blocks, tq, block_width), lambda i, s: (0, i, 0)),
            scratch_shapes=[
                pltpu.VMEM((frame_count + 2 * HALF, width), jnp.bfloat16),
                pltpu.VMEM((frame_count + 2 * HALF, width), jnp.bfloat16),
                pltpu.VMEM((tq, width), jnp.bfloat16),
            ],
        ),
        compiler_params=pltpu.CompilerParams(dimension_semantics=("arbitrary",)),
    )(scal, query, keyed, valued, low, high, w_out)


def latent_kernel(scal_ref, q_ref, k_ref, v_ref, acc_ref, stat_ref, *, heads, scale):
    tl = q_ref.shape[0]
    frame_count = k_ref.shape[0]
    valid = lax.broadcasted_iota(jnp.int32, (tl, frame_count), 1) < scal_ref[0]
    stat_ref[...] = jnp.zeros_like(stat_ref)
    for h in range(heads):
        cols = slice(h * HD, (h + 1) * HD)
        s = lax.dot_general(
            q_ref[:, cols], k_ref[:, cols], (((1,), (1,)), ((), ())),
            preferred_element_type=jnp.float32,
        ) * scale
        masked = jnp.where(valid, s, NEG)
        peak = jnp.max(masked, axis=1, keepdims=True)
        weights = jnp.exp(masked - peak)
        total = jnp.sum(weights, axis=1, keepdims=True)
        acc_ref[:, cols] = jnp.dot(
            weights.astype(jnp.bfloat16), v_ref[:, cols], preferred_element_type=jnp.float32
        )
        stat_ref[:, h : h + 1] = peak
        stat_ref[:, heads + h : heads + h + 1] = total


def latent_attention(latent_query, keyed, valued, valid_count):
    latent_count, width = latent_query.shape
    heads = width // HD
    tl = min(256, latent_count)
    scal = jnp.reshape(valid_count, (1,)).astype(jnp.int32)
    kernel = functools.partial(latent_kernel, heads=heads, scale=HD ** (-0.5))
    frame_count = keyed.shape[0]
    cost = pl.CostEstimate(
        flops=4 * latent_count * frame_count * width,
        transcendentals=latent_count * frame_count * heads,
        bytes_accessed=2 * (latent_query.size + 2 * keyed.size) + 4 * latent_count * (width + 128),
    )
    acc, stat = pl.pallas_call(
        kernel,
        cost_estimate=cost,
        out_shape=(
            jax.ShapeDtypeStruct((latent_count, width), jnp.float32),
            jax.ShapeDtypeStruct((latent_count, 128), jnp.float32),
        ),
        grid_spec=pltpu.PrefetchScalarGridSpec(
            num_scalar_prefetch=1,
            grid=(latent_count // tl,),
            in_specs=[
                pl.BlockSpec((tl, width), lambda i, s: (i, 0)),
                pl.BlockSpec(keyed.shape, lambda i, s: (0, 0)),
                pl.BlockSpec(valued.shape, lambda i, s: (0, 0)),
            ],
            out_specs=[
                pl.BlockSpec((tl, width), lambda i, s: (i, 0)),
                pl.BlockSpec((tl, 128), lambda i, s: (i, 0)),
            ],
        ),
    )(scal, latent_query, keyed, valued)
    return stat[:, :heads], stat[:, heads : 2 * heads], acc


def shifted_blocks(payload, axis, rows):
    count = lax.axis_size(axis)
    place = lax.axis_index(axis)
    own = lax.dynamic_slice_in_dim(payload, place * rows, rows, 0)
    parts = [own]
    for shift in range(1, count):
        target = (place + shift) % count
        block = lax.dynamic_slice_in_dim(payload, target * rows, rows, 0)
        pairs = [(i, (i + shift) % count) for i in range(count)]
        parts.append(lax.ppermute(block, axis, pairs))
    return jnp.stack(parts)


def column_sum(partial, axis):
    count = lax.axis_size(axis)
    place = lax.axis_index(axis)
    width = partial.shape[1] // count
    own = lax.dynamic_slice_in_dim(partial, place * width, width, 1)
    total = own.astype(jnp.float32)
    for shift in range(1, count):
        target = (place + shift) % count
        block = lax.dynamic_slice_in_dim(partial, target * width, width, 1)
        pairs = [(i, (i + shift) % count) for i in range(count)]
        total = total + lax.ppermute(block, axis, pairs).astype(jnp.float32)
    return total.astype(jnp.bfloat16)


def send_order(axis):
    count = lax.axis_size(axis)
    place = lax.axis_index(axis)
    if count % 2 != 0:
        return [(place + j) % count for j in range(count)]
    chips = count // 2
    core = place % 2
    chip = place // 2
    theirs = [2 * ((chip + d) % chips) + 1 - core for d in range(chips)]
    mine = [2 * ((chip + d) % chips) + core for d in range(chips)]
    return theirs + mine


def ordered_columns(weight, axis):
    count = lax.axis_size(axis)
    width = weight.shape[1] // count
    return jnp.concatenate(
        [lax.dynamic_slice_in_dim(weight, b * width, width, 1) for b in send_order(axis)], axis=1
    )


def chip_pair_sums(blocks, axis):
    count = lax.axis_size(axis)
    chips = count // 2
    swap = [(i, i ^ 1) for i in range(count)]
    received = lax.ppermute(blocks[:chips], axis, swap)
    return [
        (blocks[chips + d].astype(jnp.float32) + received[d].astype(jnp.float32)).astype(
            jnp.bfloat16
        )
        for d in range(chips)
    ]


def cross_chip_sum(chip_sums, axis):
    count = lax.axis_size(axis)
    chips = count // 2
    total = chip_sums[0].astype(jnp.float32)
    for d in range(1, chips):
        pairs = [(2 * c + k, 2 * ((c + d) % chips) + k) for c in range(chips) for k in range(2)]
        total = total + lax.ppermute(chip_sums[d], axis, pairs).astype(jnp.float32)
    return total.astype(jnp.bfloat16)


def plain_block_sum(blocks, axis):
    count = lax.axis_size(axis)
    total = blocks[0].astype(jnp.float32)
    for shift in range(1, count):
        pairs = [(i, (i + shift) % count) for i in range(count)]
        total = total + lax.ppermute(blocks[shift], axis, pairs).astype(jnp.float32)
    return total.astype(jnp.bfloat16)


def split_three(values):
    hi = values.astype(jnp.bfloat16)
    rest = values - hi.astype(jnp.float32)
    mid = rest.astype(jnp.bfloat16)
    lo = (rest - mid.astype(jnp.float32)).astype(jnp.bfloat16)
    return [hi, mid, lo]


def exchange_rows(payload, axis, rows):
    count = lax.axis_size(axis)
    place = lax.axis_index(axis)
    parts = [lax.dynamic_slice_in_dim(payload, place * rows, rows, 0)]
    for shift in range(1, count):
        pairs = [(i, (i + shift) % count) for i in range(count)]
        block = lax.dynamic_slice_in_dim(payload, ((place + shift) % count) * rows, rows, 0)
        parts.append(lax.ppermute(block, axis, pairs))
    return parts


def merge_kernel(*refs, heads):
    part_refs, out_ref = refs[:-1], refs[-1]
    width = out_ref.shape[1]
    stat_width = 2 * heads

    stat_blocks = []
    for ref in part_refs:
        raw = ref[:, width : width + 3 * stat_width].astype(jnp.float32)
        stat_blocks.append(
            raw[:, 0:stat_width]
            + raw[:, stat_width : 2 * stat_width]
            + raw[:, 2 * stat_width : 3 * stat_width]
        )

    def column(k, c):
        return stat_blocks[k][:, c : c + 1]

    for h in range(heads):
        peaks = [column(k, h) for k in range(len(part_refs))]
        joint = peaks[0]
        for peak in peaks[1:]:
            joint = jnp.maximum(joint, peak)
        total = jnp.zeros_like(joint)
        accum = jnp.zeros((out_ref.shape[0], HD), jnp.float32)
        for k, (ref, peak) in enumerate(zip(part_refs, peaks)):
            factor = jnp.exp(peak - joint)
            total = total + column(k, heads + h) * factor
            accum = accum + ref[:, h * HD : (h + 1) * HD].astype(jnp.float32) * factor
        out_ref[:, h * HD : (h + 1) * HD] = (accum / total).astype(jnp.bfloat16)


def merge_parts(parts, width, heads):
    rows = parts[0].shape[0]
    return pl.pallas_call(
        functools.partial(merge_kernel, heads=heads),
        out_shape=jax.ShapeDtypeStruct((rows, width), jnp.bfloat16),
        in_specs=[pl.BlockSpec(memory_space=pltpu.VMEM)] * len(parts),
        out_specs=pl.BlockSpec(memory_space=pltpu.VMEM),
    )(*parts)


def per_device(
    frames, latents, lengths, w_query, w_key, w_value, w_out, w_latent_query, w_latent_out
):
    frame_count = frames.shape[0]
    head_width = w_query.shape[1]
    heads_here = head_width // HD
    seq_devices = lax.axis_size("seq")
    seq_place = lax.axis_index("seq")
    first_frame = seq_place * frame_count
    length = lengths[0]
    query = project(frames, w_query)
    keyed = project(frames, w_key)
    valued = project(frames, w_value)
    low, high = halos(keyed, valued, "seq")
    chunks = 1
    chunk_rows = frame_count // chunks
    head_devices = lax.axis_size("head")
    paired = head_devices % 2 == 0
    w_ordered = ordered_columns(w_out, "head")
    parts = [
        window_attention(
            query, keyed, valued, low, high, w_ordered, first_frame, length,
            c * chunk_rows, chunk_rows, head_devices,
        )
        for c in range(chunks)
    ]
    latent_count = latents.shape[0]
    latent_query = project(latents, w_latent_query)
    valid_count = jnp.clip(length - first_frame, 0, frame_count)
    frame_parts = []
    if paired:
        first_sums = chip_pair_sums(parts[0], "head")
        rest = parts[1:]
        if rest:
            first_sums, rest, keyed, valued = lax.optimization_barrier(
                (first_sums, rest, keyed, valued)
            )
        frame_parts.append(cross_chip_sum(first_sums, "head"))
        rest_sums = [chip_pair_sums(blocks, "head") for blocks in rest]
    else:
        frame_parts = [plain_block_sum(blocks, "head") for blocks in parts]
    peaks, totals, local_accum = latent_attention(latent_query, keyed, valued, valid_count)
    payload = jnp.concatenate(
        [local_accum.astype(jnp.bfloat16)] + split_three(jnp.concatenate([peaks, totals], axis=1)),
        axis=1,
    )
    if paired:
        rest_sums, payload = lax.optimization_barrier((rest_sums, payload))
        frame_parts.extend(cross_chip_sum(sums, "head") for sums in rest_sums)
    frames_out = jnp.concatenate(frame_parts, axis=0)
    rows_here = latent_count // seq_devices
    parts = exchange_rows(payload, "seq", rows_here)
    summary = merge_parts(parts, head_width, heads_here)
    if paired:
        latent_terms = jnp.dot(
            summary, ordered_columns(w_latent_out, "head"), preferred_element_type=jnp.float32
        ).astype(jnp.bfloat16)
        block_width = latent_terms.shape[1] // head_devices
        latent_blocks = jnp.stack(
            [latent_terms[:, j * block_width : (j + 1) * block_width] for j in range(head_devices)]
        )
        latents_out = cross_chip_sum(chip_pair_sums(latent_blocks, "head"), "head")
    else:
        latent_terms = jnp.dot(summary, w_latent_out, preferred_element_type=jnp.float32)
        latents_out = column_sum(latent_terms.astype(jnp.bfloat16), "head")
    return (frames_out, latents_out)


def solution(mesh):
    return jax.shard_map(
        per_device,
        mesh=mesh,
        in_specs=(
            P(("groups", "seq"), None),
            P(),
            P("groups"),
            P(None, "head"),
            P(None, "head"),
            P(None, "head"),
            P("head", None),
            P(None, "head"),
            P("head", None),
        ),
        out_specs=(P(("groups", "seq"), "head"), P(("groups", "seq"), "head")),
        check_vma=False,
    )
```

```python
import functools

import jax
import jax.numpy as jnp
from jax import lax
from jax.experimental import pallas as pl
from jax.experimental.pallas import tpu as pltpu
from jax.sharding import PartitionSpec as P

HD = 64
HALF = 256
NEG = -1e30


def halos(keyed, valued, axis):
    count = lax.axis_size(axis)
    forward = [(i, i + 1) for i in range(count - 1)]
    backward = [(target, source) for source, target in forward]
    tail = jnp.concatenate([keyed[-HALF:], valued[-HALF:]], axis=1)
    head = jnp.concatenate([keyed[:HALF], valued[:HALF]], axis=1)
    return lax.ppermute(tail, axis, forward), lax.ppermute(head, axis, backward)


def project(source, weight):
    return jnp.dot(source, weight, preferred_element_type=jnp.float32).astype(jnp.bfloat16)


def window_kernel(
    scal_ref, q_ref, k_ref, v_ref, low_ref, high_ref, w_ref, *rest, heads, scale, groups
):
    out_refs = rest[:groups]
    kbuf, vbuf, att_ref = rest[groups:]
    tq = q_ref.shape[0]
    frame_count, width = k_ref.shape
    span = tq + 2 * HALF

    @pl.when(pl.program_id(0) == 0)
    def _fill():
        kbuf[0:HALF, :] = low_ref[:, 0:width]
        vbuf[0:HALF, :] = low_ref[:, width : 2 * width]
        kbuf[HALF : HALF + frame_count, :] = k_ref[...]
        vbuf[HALF : HALF + frame_count, :] = v_ref[...]
        kbuf[HALF + frame_count :, :] = high_ref[:, 0:width]
        vbuf[HALF + frame_count :, :] = high_ref[:, width : 2 * width]

    start = pl.multiple_of(scal_ref[2] + pl.program_id(0) * tq, tq)
    first = scal_ref[0]
    length = scal_ref[1]
    row = lax.broadcasted_iota(jnp.int32, (tq, span), 0)
    col = lax.broadcasted_iota(jnp.int32, (tq, span), 1)
    offset = col - row
    key_pos = first + start - HALF + col
    allowed = (offset >= 0) & (offset <= 2 * HALF) & (key_pos >= 0) & (key_pos < length)
    query_pos = first + start + lax.broadcasted_iota(jnp.int32, (tq, 1), 0)
    query_valid = query_pos < length
    for h in range(heads):
        cols = slice(h * HD, (h + 1) * HD)
        q = q_ref[:, cols]
        k = kbuf[pl.ds(start, span), cols]
        v = vbuf[pl.ds(start, span), cols]
        s = lax.dot_general(
            q, k, (((1,), (1,)), ((), ())), preferred_element_type=jnp.float32
        ) * scale
        masked = jnp.where(allowed, s, NEG)
        peak = jnp.max(masked, axis=1, keepdims=True)
        weights = jnp.exp(masked - peak)
        denom = jnp.sum(weights, axis=1, keepdims=True)
        blended = jnp.dot(weights.astype(jnp.bfloat16), v, preferred_element_type=jnp.float32)
        divisor = jnp.where(query_valid, denom, 1.0)
        att_ref[:, cols] = jnp.where(query_valid, blended / divisor, 0.0).astype(jnp.bfloat16)
    result = jnp.dot(att_ref[...], w_ref[...], preferred_element_type=jnp.float32)
    per_group = out_refs[0].shape[0]
    block_width = out_refs[0].shape[2]
    for b in range(groups * per_group):
        out_refs[b // per_group][b % per_group] = result[
            :, b * block_width : (b + 1) * block_width
        ].astype(jnp.bfloat16)


def window_attention(
    query, keyed, valued, low, high, w_out, first_frame, length, row_base, rows, blocks
):
    frame_count, width = query.shape
    out_width = w_out.shape[1]
    block_width = out_width // blocks
    tq = min(512, rows)
    block_base = row_base // tq
    span = tq + 2 * HALF
    scal = jnp.array([0, 0, row_base], jnp.int32).at[0].set(first_frame).at[1].set(length)
    groups = 2 if blocks % 2 == 0 else 1
    kernel = functools.partial(
        window_kernel, heads=width // HD, scale=HD ** (-0.5), groups=groups
    )
    cost = pl.CostEstimate(
        flops=4 * rows * span * width + 2 * rows * width * out_width,
        transcendentals=rows * span * (width // HD),
        bytes_accessed=2 * (2 * query.size + rows * width + 2 * low.size + w_out.size + rows * out_width),
    )
    full = lambda i, s: (0, 0)
    return pl.pallas_call(
        kernel,
        cost_estimate=cost,
        out_shape=[
            jax.ShapeDtypeStruct((blocks // groups, rows, block_width), jnp.bfloat16)
        ] * groups,
        grid_spec=pltpu.PrefetchScalarGridSpec(
            num_scalar_prefetch=1,
            grid=(rows // tq,),
            in_specs=[
                pl.BlockSpec((tq, width), lambda i, s: (i + block_base, 0)),
                pl.BlockSpec(keyed.shape, full),
                pl.BlockSpec(valued.shape, full),
                pl.BlockSpec(low.shape, full),
                pl.BlockSpec(high.shape, full),
                pl.BlockSpec(w_out.shape, full),
            ],
            out_specs=[
                pl.BlockSpec((blocks // groups, tq, block_width), lambda i, s: (0, i, 0))
            ] * groups,
            scratch_shapes=[
                pltpu.VMEM((frame_count + 2 * HALF, width), jnp.bfloat16),
                pltpu.VMEM((frame_count + 2 * HALF, width), jnp.bfloat16),
                pltpu.VMEM((tq, width), jnp.bfloat16),
            ],
        ),
        compiler_params=pltpu.CompilerParams(dimension_semantics=("arbitrary",)),
    )(scal, query, keyed, valued, low, high, w_out)


def latent_kernel(scal_ref, q_ref, k_ref, v_ref, acc_ref, stat_ref, *, heads, scale):
    tl = q_ref.shape[0]
    frame_count = k_ref.shape[0]
    valid = lax.broadcasted_iota(jnp.int32, (tl, frame_count), 1) < scal_ref[0]
    stat_ref[...] = jnp.zeros_like(stat_ref)
    for h in range(heads):
        cols = slice(h * HD, (h + 1) * HD)
        s = lax.dot_general(
            q_ref[:, cols], k_ref[:, cols], (((1,), (1,)), ((), ())),
            preferred_element_type=jnp.float32,
        ) * scale
        masked = jnp.where(valid, s, NEG)
        peak = jnp.max(masked, axis=1, keepdims=True)
        weights = jnp.exp(masked - peak)
        total = jnp.sum(weights, axis=1, keepdims=True)
        acc_ref[:, cols] = jnp.dot(
            weights.astype(jnp.bfloat16), v_ref[:, cols], preferred_element_type=jnp.float32
        )
        stat_ref[:, h : h + 1] = peak
        stat_ref[:, heads + h : heads + h + 1] = total


def latent_attention(latent_query, keyed, valued, valid_count):
    latent_count, width = latent_query.shape
    heads = width // HD
    tl = min(256, latent_count)
    scal = jnp.reshape(valid_count, (1,)).astype(jnp.int32)
    kernel = functools.partial(latent_kernel, heads=heads, scale=HD ** (-0.5))
    frame_count = keyed.shape[0]
    cost = pl.CostEstimate(
        flops=4 * latent_count * frame_count * width,
        transcendentals=latent_count * frame_count * heads,
        bytes_accessed=2 * (latent_query.size + 2 * keyed.size) + 4 * latent_count * (width + 128),
    )
    acc, stat = pl.pallas_call(
        kernel,
        cost_estimate=cost,
        out_shape=(
            jax.ShapeDtypeStruct((latent_count, width), jnp.float32),
            jax.ShapeDtypeStruct((latent_count, 128), jnp.float32),
        ),
        grid_spec=pltpu.PrefetchScalarGridSpec(
            num_scalar_prefetch=1,
            grid=(latent_count // tl,),
            in_specs=[
                pl.BlockSpec((tl, width), lambda i, s: (i, 0)),
                pl.BlockSpec(keyed.shape, lambda i, s: (0, 0)),
                pl.BlockSpec(valued.shape, lambda i, s: (0, 0)),
            ],
            out_specs=[
                pl.BlockSpec((tl, width), lambda i, s: (i, 0)),
                pl.BlockSpec((tl, 128), lambda i, s: (i, 0)),
            ],
        ),
    )(scal, latent_query, keyed, valued)
    return stat[:, :heads], stat[:, heads : 2 * heads], acc


def shifted_blocks(payload, axis, rows):
    count = lax.axis_size(axis)
    place = lax.axis_index(axis)
    own = lax.dynamic_slice_in_dim(payload, place * rows, rows, 0)
    parts = [own]
    for shift in range(1, count):
        target = (place + shift) % count
        block = lax.dynamic_slice_in_dim(payload, target * rows, rows, 0)
        pairs = [(i, (i + shift) % count) for i in range(count)]
        parts.append(lax.ppermute(block, axis, pairs))
    return jnp.stack(parts)


def column_sum(partial, axis):
    count = lax.axis_size(axis)
    place = lax.axis_index(axis)
    width = partial.shape[1] // count
    own = lax.dynamic_slice_in_dim(partial, place * width, width, 1)
    total = own.astype(jnp.float32)
    for shift in range(1, count):
        target = (place + shift) % count
        block = lax.dynamic_slice_in_dim(partial, target * width, width, 1)
        pairs = [(i, (i + shift) % count) for i in range(count)]
        total = total + lax.ppermute(block, axis, pairs).astype(jnp.float32)
    return total.astype(jnp.bfloat16)


def send_order(axis):
    count = lax.axis_size(axis)
    place = lax.axis_index(axis)
    if count % 2 != 0:
        return [(place + j) % count for j in range(count)]
    chips = count // 2
    core = place % 2
    chip = place // 2
    theirs = [2 * ((chip + d) % chips) + 1 - core for d in range(chips)]
    mine = [2 * ((chip + d) % chips) + core for d in range(chips)]
    return theirs + mine


def ordered_columns(weight, axis):
    count = lax.axis_size(axis)
    width = weight.shape[1] // count
    return jnp.concatenate(
        [lax.dynamic_slice_in_dim(weight, b * width, width, 1) for b in send_order(axis)], axis=1
    )


def chip_pair_sums(blocks, axis):
    count = lax.axis_size(axis)
    chips = count // 2
    swap = [(i, i ^ 1) for i in range(count)]
    theirs, mine = blocks
    received = lax.ppermute(theirs, axis, swap)
    return [
        (mine[d].astype(jnp.float32) + received[d].astype(jnp.float32)).astype(
            jnp.bfloat16
        )
        for d in range(chips)
    ]


def cross_chip_sum(chip_sums, axis):
    count = lax.axis_size(axis)
    chips = count // 2
    total = chip_sums[0].astype(jnp.float32)
    for d in range(1, chips):
        pairs = [(2 * c + k, 2 * ((c + d) % chips) + k) for c in range(chips) for k in range(2)]
        total = total + lax.ppermute(chip_sums[d], axis, pairs).astype(jnp.float32)
    return total.astype(jnp.bfloat16)


def plain_block_sum(blocks, axis):
    count = lax.axis_size(axis)
    total = blocks[0].astype(jnp.float32)
    for shift in range(1, count):
        pairs = [(i, (i + shift) % count) for i in range(count)]
        total = total + lax.ppermute(blocks[shift], axis, pairs).astype(jnp.float32)
    return total.astype(jnp.bfloat16)


def split_three(values):
    hi = values.astype(jnp.bfloat16)
    rest = values - hi.astype(jnp.float32)
    mid = rest.astype(jnp.bfloat16)
    lo = (rest - mid.astype(jnp.float32)).astype(jnp.bfloat16)
    return [hi, mid, lo]


def exchange_rows(payload, axis, rows):
    count = lax.axis_size(axis)
    place = lax.axis_index(axis)
    parts = [lax.dynamic_slice_in_dim(payload, place * rows, rows, 0)]
    for shift in range(1, count):
        pairs = [(i, (i + shift) % count) for i in range(count)]
        block = lax.dynamic_slice_in_dim(payload, ((place + shift) % count) * rows, rows, 0)
        parts.append(lax.ppermute(block, axis, pairs))
    return parts


def merge_kernel(*refs, heads):
    part_refs, out_ref = refs[:-1], refs[-1]
    width = out_ref.shape[1]
    stat_width = 2 * heads

    stat_blocks = []
    for ref in part_refs:
        raw = ref[:, width : width + 3 * stat_width].astype(jnp.float32)
        stat_blocks.append(
            raw[:, 0:stat_width]
            + raw[:, stat_width : 2 * stat_width]
            + raw[:, 2 * stat_width : 3 * stat_width]
        )

    def column(k, c):
        return stat_blocks[k][:, c : c + 1]

    for h in range(heads):
        peaks = [column(k, h) for k in range(len(part_refs))]
        joint = peaks[0]
        for peak in peaks[1:]:
            joint = jnp.maximum(joint, peak)
        total = jnp.zeros_like(joint)
        accum = jnp.zeros((out_ref.shape[0], HD), jnp.float32)
        for k, (ref, peak) in enumerate(zip(part_refs, peaks)):
            factor = jnp.exp(peak - joint)
            total = total + column(k, heads + h) * factor
            accum = accum + ref[:, h * HD : (h + 1) * HD].astype(jnp.float32) * factor
        out_ref[:, h * HD : (h + 1) * HD] = (accum / total).astype(jnp.bfloat16)


def merge_parts(parts, width, heads):
    rows = parts[0].shape[0]
    return pl.pallas_call(
        functools.partial(merge_kernel, heads=heads),
        out_shape=jax.ShapeDtypeStruct((rows, width), jnp.bfloat16),
        in_specs=[pl.BlockSpec(memory_space=pltpu.VMEM)] * len(parts),
        out_specs=pl.BlockSpec(memory_space=pltpu.VMEM),
    )(*parts)


def per_device(
    frames, latents, lengths, w_query, w_key, w_value, w_out, w_latent_query, w_latent_out
):
    frame_count = frames.shape[0]
    head_width = w_query.shape[1]
    heads_here = head_width // HD
    seq_devices = lax.axis_size("seq")
    seq_place = lax.axis_index("seq")
    first_frame = seq_place * frame_count
    length = lengths[0]
    query = project(frames, w_query)
    keyed = project(frames, w_key)
    valued = project(frames, w_value)
    low, high = halos(keyed, valued, "seq")
    chunks = 1
    chunk_rows = frame_count // chunks
    head_devices = lax.axis_size("head")
    paired = head_devices % 2 == 0
    w_ordered = ordered_columns(w_out, "head")
    parts = [
        window_attention(
            query, keyed, valued, low, high, w_ordered, first_frame, length,
            c * chunk_rows, chunk_rows, head_devices,
        )
        for c in range(chunks)
    ]
    latent_count = latents.shape[0]
    latent_query = project(latents, w_latent_query)
    valid_count = jnp.clip(length - first_frame, 0, frame_count)
    frame_parts = []
    if paired:
        first_sums = chip_pair_sums(parts[0], "head")
        first_sums, rest, keyed, valued = lax.optimization_barrier(
            (first_sums, parts[1:], keyed, valued)
        )
        frame_parts.append(cross_chip_sum(first_sums, "head"))
        rest_sums = [chip_pair_sums(blocks, "head") for blocks in rest]
    else:
        frame_parts = [plain_block_sum(blocks[0], "head") for blocks in parts]
    peaks, totals, local_accum = latent_attention(latent_query, keyed, valued, valid_count)
    payload = jnp.concatenate(
        [local_accum.astype(jnp.bfloat16)] + split_three(jnp.concatenate([peaks, totals], axis=1)),
        axis=1,
    )
    if paired:
        rest_sums, payload = lax.optimization_barrier((rest_sums, payload))
        frame_parts.extend(cross_chip_sum(sums, "head") for sums in rest_sums)
    frames_out = jnp.concatenate(frame_parts, axis=0)
    rows_here = latent_count // seq_devices
    parts = exchange_rows(payload, "seq", rows_here)
    summary = merge_parts(parts, head_width, heads_here)
    if paired:
        latent_terms = jnp.dot(
            summary, ordered_columns(w_latent_out, "head"), preferred_element_type=jnp.float32
        ).astype(jnp.bfloat16)
        block_width = latent_terms.shape[1] // head_devices
        latent_blocks = jnp.stack(
            [latent_terms[:, j * block_width : (j + 1) * block_width] for j in range(head_devices)]
        )
        halves = (latent_blocks[: head_devices // 2], latent_blocks[head_devices // 2 :])
        latents_out = cross_chip_sum(chip_pair_sums(halves, "head"), "head")
    else:
        latent_terms = jnp.dot(summary, w_latent_out, preferred_element_type=jnp.float32)
        latents_out = column_sum(latent_terms.astype(jnp.bfloat16), "head")
    return (frames_out, latents_out)


def solution(mesh):
    return jax.shard_map(
        per_device,
        mesh=mesh,
        in_specs=(
            P(("groups", "seq"), None),
            P(),
            P("groups"),
            P(None, "head"),
            P(None, "head"),
            P(None, "head"),
            P("head", None),
            P(None, "head"),
            P("head", None),
        ),
        out_specs=(P(("groups", "seq"), "head"), P(("groups", "seq"), "head")),
        check_vma=False,
    )
```
